32 devices in a mesh: doc: 8 (over y, x, core), term: 4 (over z).
Axes of the slice: x: 2, y: 2, z: 4, core: 2. Of those that a mesh axis runs over, the one named last changes fastest.
Arguments:
- tiles: bfloat16 [8, 4, 512, 128, 128], P('doc', 'term'), as said below
- tile_rows: int32 [8, 4, 512], P('doc', 'term'), may hold values from 0 to 63, as said below
- tile_cols: int32 [8, 4, 512], P('doc', 'term'), may hold values from 0 to 63
- tile_count: int32 [8, 4], P('doc', 'term'), may hold values from 64 to 512, as said below
- start_block: bfloat16 [4, 8192, 64], P('term', 'doc'), may hold values from -6 to 6
- doc_cluster: int32 [8, 8192], P('doc', 'term'), may hold values from 0 to 63, as said below
- term_cluster: int32 [4, 8192], P('term', 'doc'), may hold values from 0 to 63, as said below
Outputs:
- doc_distance: float32 [8, 8192, 64], P('doc', 'term')
- term_distance: float32 [4, 8192, 64], P('term', 'doc')
The draws below stay inside these ranges and needn't reach their ends.
Inputs may be any that keep to these rules, and one draw needn't show every extreme that they name: `tile_rows`: the first 64 slots of every device name every row tile of its block at least once; other slots may repeat a position, and repeated tiles add. `tile_cols`: the first 64 slots of every device name each column tile of its block exactly once. `tile_count`: in every draw some device uses all 512 slots; slots at or beyond a device's count are unused. `doc_cluster`: every co-cluster holds at least one document. `term_cluster`: every co-cluster holds at least one term. `tiles`: entries are positive.
All inputs are finite; a program needn't handle non-finite values.
Results may differ from the reference program's by a relative error of at most 0.0009.
Values may be sent and summed in bfloat16 or wider, within the bound.
No kernel may reach another device: no remote copies, remote signals or barrier semaphores. Data moves between devices by JAX's collectives and lax.ppermute only.
A program may use at most 128 MiB of HBM per device.

```python
import math
import jax
import jax.numpy as jnp
from jax import lax

TILE = 128
K = 64
CLUSTERS = 64
ITERS = 2
DOC_TILES = 64
TERM_TILES = 64
TMAX = 512
DOC_GROUPS = 8
TERM_GROUPS = 4
BLOCK_DOCS = 8192
BLOCK_TERMS = 8192
DOCS = 65536
TERMS = 32768


boost_level = 16.0


def tile_layout(key):
    devices = DOC_GROUPS * TERM_GROUPS
    slots = jnp.arange(TMAX, dtype=jnp.int32)
    row_keys = jax.random.split(jax.random.fold_in(key, 701), devices)
    col_keys = jax.random.split(jax.random.fold_in(key, 702), devices)
    row_cover = jax.vmap(lambda single: jax.random.permutation(single, DOC_TILES))(row_keys).astype(jnp.int32)
    col_cover = jax.vmap(lambda single: jax.random.permutation(single, TERM_TILES))(col_keys).astype(jnp.int32)
    extra_rows = jax.random.randint(jax.random.fold_in(key, 703), (devices, TMAX), 0, DOC_TILES, dtype=jnp.int32)
    extra_cols = jax.random.randint(jax.random.fold_in(key, 704), (devices, TMAX), 0, TERM_TILES, dtype=jnp.int32)
    covered = slots < TERM_TILES
    row_pick = jnp.take(row_cover, slots % DOC_TILES, axis=1)
    col_pick = jnp.take(col_cover, jnp.minimum(slots, TERM_TILES - 1), axis=1)
    row_table = jnp.where(covered[None, :], row_pick, extra_rows).astype(jnp.int32)
    col_table = jnp.where(covered[None, :], col_pick, extra_cols).astype(jnp.int32)
    spread = TMAX - TERM_TILES + 1
    first = jax.random.randint(jax.random.fold_in(key, 705), (devices,), 0, spread, dtype=jnp.int32)
    second = jax.random.randint(jax.random.fold_in(key, 706), (devices,), 0, spread, dtype=jnp.int32)
    counts = TERM_TILES + jnp.minimum(first, second)
    busiest = jax.random.randint(jax.random.fold_in(key, 707), (), 0, devices, dtype=jnp.int32)
    counts = jnp.where(jnp.arange(devices, dtype=jnp.int32) == busiest, TMAX, counts).astype(jnp.int32)
    return (row_table.reshape(DOC_GROUPS, TERM_GROUPS, TMAX), col_table.reshape(DOC_GROUPS, TERM_GROUPS, TMAX), counts.reshape(DOC_GROUPS, TERM_GROUPS))


def cluster_labels(key, salt, total):
    labels = jax.random.randint(jax.random.fold_in(key, salt), (total,), 0, CLUSTERS, dtype=jnp.int32)
    spots = jax.random.permutation(jax.random.fold_in(key, salt + 1), total)[:CLUSTERS]
    return labels.at[spots].set(jnp.arange(CLUSTERS, dtype=jnp.int32))


def draw_tile_rows(key, part):
    return tile_layout(key)[0]


def draw_tile_cols(key, part):
    return tile_layout(key)[1]


def draw_tile_count(key, part):
    return tile_layout(key)[2]


def draw_doc_cluster(key, part):
    return cluster_labels(key, 711, DOCS).reshape(DOC_GROUPS, BLOCK_DOCS)


def draw_term_cluster(key, part):
    return cluster_labels(key, 721, TERMS).reshape(TERM_GROUPS, BLOCK_TERMS)


def draw_tiles(key, part):
    row_table, col_table, counts = tile_layout(key)
    flat_rows = row_table.reshape(DOC_GROUPS * TERM_GROUPS, TMAX)
    flat_cols = col_table.reshape(DOC_GROUPS * TERM_GROUPS, TMAX)
    doc_labels = cluster_labels(key, 711, DOCS).reshape(DOC_GROUPS, BLOCK_DOCS)
    term_labels = cluster_labels(key, 721, TERMS).reshape(TERM_GROUPS, BLOCK_TERMS)
    bottom = math.log(0.1)
    doc_scale = jnp.exp(jax.random.uniform(jax.random.fold_in(key, 731), (DOC_GROUPS, BLOCK_DOCS), jnp.float32, bottom, 0.0))
    term_scale = jnp.exp(jax.random.uniform(jax.random.fold_in(key, 732), (TERM_GROUPS, BLOCK_TERMS), jnp.float32, bottom, 0.0))
    offsets = jnp.arange(TILE, dtype=jnp.int32)

    def one_device(index):
        group_doc = index // TERM_GROUPS
        group_term = index % TERM_GROUPS
        doc_pos = flat_rows[index][:, None] * TILE + offsets[None, :]
        term_pos = flat_cols[index][:, None] * TILE + offsets[None, :]
        doc_lab = doc_labels[group_doc][doc_pos]
        term_lab = term_labels[group_term][term_pos]
        doc_fac = doc_scale[group_doc][doc_pos]
        term_fac = term_scale[group_term][term_pos]
        noise = jax.random.uniform(jax.random.fold_in(key, index + 1000), (TMAX, TILE, TILE), jnp.float32, 0.05, 1.0)
        same = (doc_lab[:, :, None] == term_lab[:, None, :]).astype(jnp.float32)
        values = noise * (1.0 + boost_level * same) * doc_fac[:, :, None] * term_fac[:, None, :]
        return values.astype(jnp.bfloat16)
    flat = lax.map(one_device, jnp.arange(DOC_GROUPS * TERM_GROUPS, dtype=jnp.int32))
    return flat.reshape(DOC_GROUPS, TERM_GROUPS, TMAX, TILE, TILE)


def block_levels(key, dims, cuts, least, largest):
    gain = 1.0
    for position, parts in cuts:
        heights = jax.random.uniform(jax.random.fold_in(jax.random.fold_in(key, 6), position), (parts,), jnp.float32, least / len(cuts), largest / len(cuts))
        gain = gain * jnp.repeat(jnp.exp(heights), dims[position] // parts).reshape((-1,) + (1,) * (len(dims) - 1 - position))
    return gain


def gaussian(stream_key, extent, scale, limit, cuts=(), kind=jnp.bfloat16):
    gain = block_levels(stream_key, extent, cuts, -0.22, 0.18) if cuts else 1.0
    result = jax.random.normal(stream_key, extent, jnp.float32) * scale * gain
    return jnp.minimum(jnp.maximum(result, -limit), limit).astype(kind)


def setup_inputs(seed: int = 0) -> dict:
    key_of = jax.random.split(jax.random.key(seed), 8)
    tiles = draw_tiles(jax.random.fold_in(key_of[7], 71), 0)
    tile_rows = draw_tile_rows(jax.random.fold_in(key_of[7], 71), 0)
    tile_cols = draw_tile_cols(jax.random.fold_in(key_of[7], 71), 0)
    tile_count = draw_tile_count(jax.random.fold_in(key_of[7], 71), 0)
    start_block = gaussian(key_of[4], (TERM_GROUPS, BLOCK_TERMS, K), 1.0, 6.0, ((0, 4), (1, 8)))
    doc_cluster = draw_doc_cluster(jax.random.fold_in(key_of[7], 71), 0)
    term_cluster = draw_term_cluster(jax.random.fold_in(key_of[7], 71), 0)
    return dict(tiles=tiles, tile_rows=tile_rows, tile_cols=tile_cols, tile_count=tile_count, start_block=start_block, doc_cluster=doc_cluster, term_cluster=term_cluster)


def live_tiles(tile_set, count):
    live = (jnp.arange(TMAX, dtype=jnp.int32) < count).astype(jnp.float32)
    return tile_set.astype(jnp.float32) * live[:, None, None]

def reference(tiles, tile_rows, tile_cols, tile_count, start_block, doc_cluster, term_cluster):
    devices = DOC_GROUPS * TERM_GROUPS
    flat_tiles = tiles.reshape(devices, TMAX, TILE, TILE)
    flat_rows = tile_rows.reshape(devices, TMAX)
    flat_cols = tile_cols.reshape(devices, TMAX)
    flat_count = tile_count.reshape(devices)
    indices = jnp.arange(devices, dtype=jnp.int32)

    def degrees(index):
        tile_set = live_tiles(flat_tiles[index], flat_count[index])
        row_sum = jax.ops.segment_sum(lax.optimization_barrier(jnp.sum(tile_set, axis=2)), flat_rows[index], num_segments=DOC_TILES)
        col_sum = jax.ops.segment_sum(lax.optimization_barrier(jnp.sum(tile_set, axis=1)), flat_cols[index], num_segments=TERM_TILES)
        return (row_sum, col_sum)
    row_parts, col_parts = lax.map(degrees, indices)
    doc_degree = row_parts.reshape(DOC_GROUPS, TERM_GROUPS, BLOCK_DOCS).sum(axis=1)
    term_degree = col_parts.reshape(DOC_GROUPS, TERM_GROUPS, BLOCK_TERMS).sum(axis=0)
    volume = jnp.sum(term_degree)
    root = jnp.sqrt(term_degree)
    flat_root = root.reshape(TERMS)
    weights = start_block
    basis = (root[:, :, None] * start_block.astype(jnp.float32)).reshape(TERMS, K)

    def left_block(index, weights):
        table = weights[index % TERM_GROUPS].reshape(TERM_TILES, TILE, K).astype(jnp.float32)
        tile_set = live_tiles(flat_tiles[index], flat_count[index])
        pieces = table[flat_cols[index]]
        product = jnp.einsum('tij,tjk->tik', tile_set, pieces, precision=lax.Precision.HIGHEST)
        return jax.ops.segment_sum(product, flat_rows[index], num_segments=DOC_TILES)

    def right_block(index, quotient):
        table = quotient[index // TERM_GROUPS].reshape(DOC_TILES, TILE, K).astype(jnp.float32)
        tile_set = live_tiles(flat_tiles[index], flat_count[index])
        pieces = table[flat_rows[index]]
        product = jnp.einsum('tij,tik->tjk', tile_set, pieces, precision=lax.Precision.HIGHEST)
        return jax.ops.segment_sum(product, flat_cols[index], num_segments=TERM_TILES)
    summed = None
    energy = None
    for step in range(ITERS):
        left_parts = lax.map(lambda index: left_block(index, weights), indices)
        summed = left_parts.reshape(DOC_GROUPS, TERM_GROUPS, BLOCK_DOCS, K).sum(axis=1)
        quotient = (summed / doc_degree[:, :, None]).astype(jnp.bfloat16)
        right_parts = lax.map(lambda index: right_block(index, quotient), indices)
        right_sum = right_parts.reshape(DOC_GROUPS, TERM_GROUPS, BLOCK_TERMS, K).sum(axis=0)
        raw = (right_sum / root[:, :, None]).reshape(TERMS, K)
        gram_matrix = jnp.dot(raw.T, raw, precision=lax.Precision.HIGHEST)
        along = jnp.dot(flat_root, raw, precision=lax.Precision.HIGHEST)
        energy = lax.optimization_barrier(jnp.sum(basis * raw, axis=0))
        lower = jnp.linalg.cholesky(gram_matrix - jnp.outer(along, along) / volume)
        projected = raw - jnp.outer(flat_root, along) / volume
        basis = jax.scipy.linalg.solve_triangular(lower, projected.T, lower=True).T
        weights = (basis / flat_root[:, None]).astype(jnp.bfloat16).reshape(TERM_GROUPS, BLOCK_TERMS, K)
    scale = jnp.sqrt(volume)
    doc_embed = (scale * (summed / doc_degree[:, :, None]) * lax.rsqrt(energy)[None, None, :]).reshape(DOCS, K)
    term_embed = scale * basis / flat_root[:, None]
    doc_labels = doc_cluster.reshape(DOCS)
    term_labels = term_cluster.reshape(TERMS)
    center_sums = jax.ops.segment_sum(doc_embed, doc_labels, num_segments=CLUSTERS) + jax.ops.segment_sum(term_embed, term_labels, num_segments=CLUSTERS)
    counts = jax.ops.segment_sum(jnp.ones((DOCS,), jnp.float32), doc_labels, num_segments=CLUSTERS) + jax.ops.segment_sum(jnp.ones((TERMS,), jnp.float32), term_labels, num_segments=CLUSTERS)
    centers = center_sums / counts[:, None]

    def distances(embed):
        near = jnp.dot(embed, centers.T, precision=lax.Precision.HIGHEST)
        return (lax.optimization_barrier(jnp.sum(embed * embed, axis=1))[:, None] - 2.0 * near + lax.optimization_barrier(jnp.sum(centers * centers, axis=1))[None, :]) / K
    doc_distance = distances(doc_embed).reshape(DOC_GROUPS, BLOCK_DOCS, CLUSTERS)
    term_distance = distances(term_embed).reshape(TERM_GROUPS, BLOCK_TERMS, CLUSTERS)
    return (doc_distance, term_distance)
```

```python
import functools

import jax
import jax.numpy as jnp
from jax import lax
from jax.experimental import pallas as pl
from jax.experimental.pallas import tpu as pltpu
from jax.sharding import PartitionSpec as P

CLUSTERS = 64
ITERS = 2
CHUNK = 32
DEG_ROWS = 8

HIGH = lax.Precision.HIGHEST
NT_DIMS = (((1,), (1,)), ((), ()))


def tile_kernel(transpose_tile, with_degree, shard_tiles_in, shard_tiles_out, rows_ref, cols_ref, cnt_ref, tiles_ref, side_ref, out_ref):
    step = pl.program_id(0)
    chunk = tiles_ref.shape[0]
    width = side_ref.shape[1]

    @pl.when(step == 0)
    def _():
        out_ref[...] = jnp.zeros_like(out_ref)

    base = step * chunk
    live = jnp.clip(cnt_ref[0] - base, 0, chunk)
    ones = jnp.ones((DEG_ROWS, tiles_ref.shape[2]), jnp.bfloat16)

    def body(j, carry):
        slot = base + j
        if transpose_tile:
            src, dst = cols_ref[slot], rows_ref[slot]
        else:
            src, dst = rows_ref[slot], cols_ref[slot]
        tile = tiles_ref[j]
        piece = side_ref[src]
        if transpose_tile:
            prod = lax.dot_general(piece, tile, NT_DIMS, preferred_element_type=jnp.float32)
        else:
            prod = jnp.dot(piece, tile, preferred_element_type=jnp.float32)
        out_ref[dst, pl.ds(0, width), :] += prod
        if with_degree:
            if transpose_tile:
                deg = lax.dot_general(ones, tile, NT_DIMS, preferred_element_type=jnp.float32)
            else:
                deg = jnp.dot(ones, tile, preferred_element_type=jnp.float32)
            out_ref[dst, pl.ds(width, DEG_ROWS), :] += deg
        return carry

    lax.fori_loop(0, live, body, 0)


def tile_pass(tiles, rows, cols, count, side, transpose_tile, with_degree):
    slots, edge, _ = tiles.shape
    n_tiles, width, _ = side.shape
    chunk = min(CHUNK, slots)
    steps = slots // chunk
    out_rows = width + (DEG_ROWS if with_degree else 0)
    kernel = functools.partial(tile_kernel, transpose_tile, with_degree, None, None)

    def tile_map(i, rows_ref, cols_ref, cnt_ref):
        return (jnp.minimum(i, jnp.maximum(cnt_ref[0] - 1, 0) // chunk), 0, 0)

    def whole_map(i, rows_ref, cols_ref, cnt_ref):
        return (0, 0, 0)

    flops = 2 * slots * edge * edge * out_rows
    cost = pl.CostEstimate(
        flops=flops,
        transcendentals=0,
        bytes_accessed=tiles.size * 2 + side.size * 2 + n_tiles * out_rows * edge * 4,
    )
    return pl.pallas_call(
        kernel,
        out_shape=jax.ShapeDtypeStruct((n_tiles, out_rows, edge), jnp.float32),
        grid_spec=pltpu.PrefetchScalarGridSpec(
            num_scalar_prefetch=3,
            grid=(steps,),
            in_specs=[
                pl.BlockSpec((chunk, edge, edge), tile_map),
                pl.BlockSpec((n_tiles, width, edge), whole_map),
            ],
            out_specs=pl.BlockSpec((n_tiles, out_rows, edge), whole_map),
        ),
        compiler_params=pltpu.CompilerParams(dimension_semantics=("arbitrary",)),
        cost_estimate=cost,
    )(rows, cols, count, tiles, side)


def per_device(tiles, tile_rows, tile_cols, tile_count, start_block, doc_cluster, term_cluster):
    local_tiles = tiles[0, 0]
    rows = tile_rows[0, 0]
    cols = tile_cols[0, 0]
    count = tile_count[0, 0].reshape(1)
    edge = local_tiles.shape[1]
    start_rows = start_block[0]
    width_k = start_rows.shape[1]
    term_tiles_own = start_rows.shape[0] // edge
    start_t = start_rows.reshape(term_tiles_own, edge, width_k).transpose(0, 2, 1)
    doc_labels = doc_cluster[0].reshape(-1, edge)
    term_labels = term_cluster[0].reshape(-1, edge)
    clusters = jnp.arange(CLUSTERS, dtype=jnp.int32)

    weights = start_t
    basis = None
    doc_degree = None
    term_degree = None
    root = None
    summed_own = None
    energy = None
    volume = None
    for step in range(ITERS):
        first = step == 0
        w_all = lax.all_gather(weights, "doc", axis=0, tiled=True)
        left = tile_pass(local_tiles, rows, cols, count, w_all, True, first)
        left_own = lax.psum_scatter(left, "term", scatter_dimension=0, tiled=True)
        summed_own = left_own[:, :width_k, :]
        if first:
            doc_degree = left_own[:, width_k, :]
        quotient = (summed_own / doc_degree[:, None, :]).astype(jnp.bfloat16)
        q_all = lax.all_gather(quotient, "term", axis=0, tiled=True)
        right = tile_pass(local_tiles, rows, cols, count, q_all, False, first)
        right_own = lax.psum_scatter(right, "doc", scatter_dimension=0, tiled=True)
        if first:
            term_degree = right_own[:, width_k, :]
            root = jnp.sqrt(term_degree)
        raw = right_own[:, :width_k, :] / root[:, None, :]
        previous = root[:, None, :] * start_t.astype(jnp.float32) if first else basis
        gram_part = jnp.einsum("tki,tli->kl", raw, raw, precision=HIGH)
        along_part = jnp.einsum("tki,ti->k", raw, root, precision=HIGH)
        energy_part = jnp.sum(previous * raw, axis=(0, 2))
        volume_part = jnp.sum(term_degree)
        gram_matrix, along, energy, volume = lax.psum(
            (gram_part, along_part, energy_part, volume_part), ("doc", "term")
        )
        lower = jnp.linalg.cholesky(gram_matrix - jnp.outer(along, along) / volume)
        projected = raw - root[:, None, :] * (along / volume)[None, :, None]
        flat = projected.transpose(1, 0, 2).reshape(width_k, -1)
        solved = jax.scipy.linalg.solve_triangular(lower, flat, lower=True)
        basis = solved.reshape(width_k, term_tiles_own, edge).transpose(1, 0, 2)
        weights = (basis / root[:, None, :]).astype(jnp.bfloat16)

    scale = jnp.sqrt(volume)
    column_scale = scale * lax.rsqrt(energy)
    doc_embed = summed_own / doc_degree[:, None, :] * column_scale[None, :, None]
    term_embed = scale * basis / root[:, None, :]
    doc_onehot = (doc_labels[:, :, None] == clusters).astype(jnp.float32)
    term_onehot = (term_labels[:, :, None] == clusters).astype(jnp.float32)
    center_part = jnp.einsum("tki,tij->kj", doc_embed, doc_onehot, precision=HIGH) + jnp.einsum(
        "tki,tij->kj", term_embed, term_onehot, precision=HIGH
    )
    count_part = jnp.sum(doc_onehot, axis=(0, 1)) + jnp.sum(term_onehot, axis=(0, 1))
    center_sums, counts = lax.psum((center_part, count_part), ("doc", "term"))
    centers = center_sums / counts[None, :]
    center_norm = jnp.sum(centers * centers, axis=0)

    def distances(embed):
        near = jnp.einsum("tki,kj->tij", embed, centers, precision=HIGH)
        norm = jnp.sum(embed * embed, axis=1)
        dist = (norm[:, :, None] - 2.0 * near + center_norm[None, None, :]) / width_k
        return dist.reshape(-1, CLUSTERS)

    return (distances(doc_embed)[None], distances(term_embed)[None])


def solution(mesh):
    placed = (
        P("doc", "term", None, None, None),
        P("doc", "term", None),
        P("doc", "term", None),
        P("doc", "term"),
        P("term", "doc", None),
        P("doc", "term"),
        P("term", "doc"),
    )
    return jax.shard_map(
        per_device,
        mesh=mesh,
        in_specs=placed,
        out_specs=(P("doc", "term", None), P("term", "doc", None)),
        check_vma=False,
    )
```

```python
import functools

import jax
import jax.numpy as jnp
from jax import lax
from jax.experimental import pallas as pl
from jax.experimental.pallas import tpu as pltpu
from jax.sharding import PartitionSpec as P

CLUSTERS = 64
ITERS = 2
CHUNK = 64
GROUP = 4
DEG_ROWS = 8

HIGH = lax.Precision.HIGHEST
NT_DIMS = (((1,), (1,)), ((), ()))


def tile_kernel(transpose_tile, with_degree, group, rows_ref, cols_ref, cnt_ref, tiles_ref, side_ref, out_ref):
    step = pl.program_id(0)
    chunk = tiles_ref.shape[0]
    width = side_ref.shape[1]

    @pl.when(step == 0)
    def _():
        out_ref[...] = jnp.zeros_like(out_ref)

    count = cnt_ref[0]
    base = step * chunk
    live = jnp.clip(count - base, 0, chunk)
    ones = jnp.ones((DEG_ROWS, tiles_ref.shape[2]), jnp.bfloat16)

    def product(lhs, tile):
        if transpose_tile:
            return lax.dot_general(lhs, tile, NT_DIMS, preferred_element_type=jnp.float32)
        return jnp.dot(lhs, tile, preferred_element_type=jnp.float32)

    def body(g, carry):
        results = []
        for u in range(group):
            j = g * group + u
            slot = base + j
            if transpose_tile:
                src, dst = cols_ref[slot], rows_ref[slot]
            else:
                src, dst = rows_ref[slot], cols_ref[slot]
            tile = tiles_ref[j]
            keep = slot < count
            prod = jnp.where(keep, product(side_ref[src], tile), 0.0)
            deg = jnp.where(keep, product(ones, tile), 0.0) if with_degree else None
            results.append((dst, prod, deg))
        for dst, prod, deg in results:
            out_ref[dst, pl.ds(0, width), :] += prod
            if with_degree:
                out_ref[dst, pl.ds(width, DEG_ROWS), :] += deg
        return carry

    lax.fori_loop(0, (live + group - 1) // group, body, 0)


def tile_pass(tiles, rows, cols, count, side, transpose_tile, with_degree):
    slots, edge, _ = tiles.shape
    n_tiles, width, _ = side.shape
    chunk = min(CHUNK, slots)
    steps = slots // chunk
    out_rows = width + (DEG_ROWS if with_degree else 0)
    kernel = functools.partial(tile_kernel, transpose_tile, with_degree, GROUP)

    def tile_map(i, rows_ref, cols_ref, cnt_ref):
        return (jnp.minimum(i, jnp.maximum(cnt_ref[0] - 1, 0) // chunk), 0, 0)

    def whole_map(i, rows_ref, cols_ref, cnt_ref):
        return (0, 0, 0)

    flops = 2 * slots * edge * edge * out_rows
    cost = pl.CostEstimate(
        flops=flops,
        transcendentals=0,
        bytes_accessed=tiles.size * 2 + side.size * 2 + n_tiles * out_rows * edge * 4,
    )
    return pl.pallas_call(
        kernel,
        out_shape=jax.ShapeDtypeStruct((n_tiles, out_rows, edge), jnp.float32),
        grid_spec=pltpu.PrefetchScalarGridSpec(
            num_scalar_prefetch=3,
            grid=(steps,),
            in_specs=[
                pl.BlockSpec((chunk, edge, edge), tile_map),
                pl.BlockSpec((n_tiles, width, edge), whole_map),
            ],
            out_specs=pl.BlockSpec((n_tiles, out_rows, edge), whole_map),
        ),
        compiler_params=pltpu.CompilerParams(dimension_semantics=("arbitrary",)),
        cost_estimate=cost,
    )(rows, cols, count, tiles, side)


def per_device(tiles, tile_rows, tile_cols, tile_count, start_block, doc_cluster, term_cluster):
    local_tiles = tiles[0, 0]
    rows = tile_rows[0, 0]
    cols = tile_cols[0, 0]
    count = tile_count[0, 0].reshape(1)
    edge = local_tiles.shape[1]
    start_rows = start_block[0]
    width_k = start_rows.shape[1]
    term_tiles_own = start_rows.shape[0] // edge
    start_t = start_rows.reshape(term_tiles_own, edge, width_k).transpose(0, 2, 1)
    doc_labels = doc_cluster[0].reshape(-1, edge)
    term_labels = term_cluster[0].reshape(-1, edge)
    clusters = jnp.arange(CLUSTERS, dtype=jnp.int32)

    weights = start_t
    basis = None
    doc_degree = None
    term_degree = None
    root = None
    summed_own = None
    energy = None
    volume = None
    for step in range(ITERS):
        first = step == 0
        w_all = lax.all_gather(weights, "doc", axis=0, tiled=True)
        left = tile_pass(local_tiles, rows, cols, count, w_all, True, first)
        left_own = lax.psum_scatter(left, "term", scatter_dimension=0, tiled=True)
        summed_own = left_own[:, :width_k, :]
        if first:
            doc_degree = left_own[:, width_k, :]
        quotient = (summed_own / doc_degree[:, None, :]).astype(jnp.bfloat16)
        q_all = lax.all_gather(quotient, "term", axis=0, tiled=True)
        right = tile_pass(local_tiles, rows, cols, count, q_all, False, first)
        right_own = lax.psum_scatter(right, "doc", scatter_dimension=0, tiled=True)
        if first:
            term_degree = right_own[:, width_k, :]
            root = jnp.sqrt(term_degree)
        raw = right_own[:, :width_k, :] / root[:, None, :]
        previous = root[:, None, :] * start_t.astype(jnp.float32) if first else basis
        gram_part = jnp.einsum("tki,tli->kl", raw, raw, precision=HIGH)
        along_part = jnp.einsum("tki,ti->k", raw, root, precision=HIGH)
        energy_part = jnp.sum(previous * raw, axis=(0, 2))
        volume_part = jnp.sum(term_degree)
        gram_matrix, along, energy, volume = lax.psum(
            lax.psum((gram_part, along_part, energy_part, volume_part), "term"), "doc"
        )
        lower = jnp.linalg.cholesky(gram_matrix - jnp.outer(along, along) / volume)
        projected = raw - root[:, None, :] * (along / volume)[None, :, None]
        flat = projected.transpose(1, 0, 2).reshape(width_k, -1)
        solved = jax.scipy.linalg.solve_triangular(lower, flat, lower=True)
        basis = solved.reshape(width_k, term_tiles_own, edge).transpose(1, 0, 2)
        weights = (basis / root[:, None, :]).astype(jnp.bfloat16)

    scale = jnp.sqrt(volume)
    column_scale = scale * lax.rsqrt(energy)
    doc_embed = summed_own / doc_degree[:, None, :] * column_scale[None, :, None]
    term_embed = scale * basis / root[:, None, :]
    doc_onehot = (doc_labels[:, :, None] == clusters).astype(jnp.float32)
    term_onehot = (term_labels[:, :, None] == clusters).astype(jnp.float32)
    center_part = jnp.einsum("tki,tij->kj", doc_embed, doc_onehot, precision=HIGH) + jnp.einsum(
        "tki,tij->kj", term_embed, term_onehot, precision=HIGH
    )
    count_part = jnp.sum(doc_onehot, axis=(0, 1)) + jnp.sum(term_onehot, axis=(0, 1))
    packed = jnp.concatenate([center_part.reshape(-1), count_part])
    gathered = lax.all_gather(packed, ("doc", "term"), axis=0, tiled=False)
    totals = jnp.sum(gathered, axis=0)
    center_sums = totals[: center_part.size].reshape(center_part.shape)
    counts = totals[center_part.size :]
    centers = center_sums / counts[None, :]
    center_norm = jnp.sum(centers * centers, axis=0)

    def distances(embed):
        near = jnp.einsum("tki,kj->tij", embed, centers, precision=HIGH)
        norm = jnp.sum(embed * embed, axis=1)
        dist = (norm[:, :, None] - 2.0 * near + center_norm[None, None, :]) / width_k
        return dist.reshape(-1, CLUSTERS)

    return (distances(doc_embed)[None], distances(term_embed)[None])


def solution(mesh):
    placed = (
        P("doc", "term", None, None, None),
        P("doc", "term", None),
        P("doc", "term", None),
        P("doc", "term"),
        P("term", "doc", None),
        P("doc", "term"),
        P("term", "doc"),
    )
    return jax.shard_map(
        per_device,
        mesh=mesh,
        in_specs=placed,
        out_specs=(P("doc", "term", None), P("term", "doc", None)),
        check_vma=False,
    )
```

```python
import functools

import jax
import jax.numpy as jnp
from jax import lax
from jax.experimental import pallas as pl
from jax.experimental.pallas import tpu as pltpu
from jax.sharding import PartitionSpec as P

CLUSTERS = 64
ITERS = 2
CHUNK = 64
GROUP = 4
DEG_ROWS = 8

HIGH = lax.Precision.HIGHEST
NT_DIMS = (((1,), (1,)), ((), ()))


def tile_kernel(transpose_tile, with_degree, group, rows_ref, cols_ref, cnt_ref, tiles_ref, side_ref, out_ref):
    step = pl.program_id(0)
    chunk = tiles_ref.shape[0]
    width = side_ref.shape[1]

    @pl.when(step == 0)
    def _():
        out_ref[...] = jnp.zeros_like(out_ref)

    count = cnt_ref[0]
    base = step * chunk
    live = jnp.clip(count - base, 0, chunk)
    ones = jnp.ones((DEG_ROWS, tiles_ref.shape[2]), jnp.bfloat16)

    def product(lhs, tile):
        if transpose_tile:
            return lax.dot_general(lhs, tile, NT_DIMS, preferred_element_type=jnp.float32)
        return jnp.dot(lhs, tile, preferred_element_type=jnp.float32)

    def body(g, carry):
        results = []
        for u in range(group):
            j = g * group + u
            slot = base + j
            if transpose_tile:
                src, dst = cols_ref[slot], rows_ref[slot]
            else:
                src, dst = rows_ref[slot], cols_ref[slot]
            tile = tiles_ref[j]
            keep = slot < count
            prod = jnp.where(keep, product(side_ref[src], tile), 0.0)
            deg = jnp.where(keep, product(ones, tile), 0.0) if with_degree else None
            results.append((dst, prod, deg))
        for dst, prod, deg in results:
            out_ref[dst, pl.ds(0, width), :] += prod
            if with_degree:
                out_ref[dst, pl.ds(width, DEG_ROWS), :] += deg
        return carry

    lax.fori_loop(0, (live + group - 1) // group, body, 0)


def tile_pass(tiles, rows, cols, count, side, transpose_tile, with_degree):
    slots, edge, _ = tiles.shape
    n_tiles, width, _ = side.shape
    chunk = min(CHUNK, slots)
    steps = slots // chunk
    out_rows = width + (DEG_ROWS if with_degree else 0)
    kernel = functools.partial(tile_kernel, transpose_tile, with_degree, GROUP)

    def tile_map(i, rows_ref, cols_ref, cnt_ref):
        return (jnp.minimum(i, jnp.maximum(cnt_ref[0] - 1, 0) // chunk), 0, 0)

    def whole_map(i, rows_ref, cols_ref, cnt_ref):
        return (0, 0, 0)

    flops = 2 * slots * edge * edge * out_rows
    cost = pl.CostEstimate(
        flops=flops,
        transcendentals=0,
        bytes_accessed=tiles.size * 2 + side.size * 2 + n_tiles * out_rows * edge * 4,
    )
    return pl.pallas_call(
        kernel,
        out_shape=jax.ShapeDtypeStruct((n_tiles, out_rows, edge), jnp.float32),
        grid_spec=pltpu.PrefetchScalarGridSpec(
            num_scalar_prefetch=3,
            grid=(steps,),
            in_specs=[
                pl.BlockSpec((chunk, edge, edge), tile_map),
                pl.BlockSpec((n_tiles, width, edge), whole_map),
            ],
            out_specs=pl.BlockSpec((n_tiles, out_rows, edge), whole_map),
        ),
        compiler_params=pltpu.CompilerParams(dimension_semantics=("arbitrary",)),
        cost_estimate=cost,
    )(rows, cols, count, tiles, side)


def scatter_sum(x, axis_name, parts):
    pieces = x.reshape((parts, x.shape[0] // parts) + x.shape[1:])
    return jnp.sum(lax.all_to_all(pieces, axis_name, 0, 0, tiled=False), axis=0)


def small_sum(values):
    flat = jnp.concatenate([jnp.reshape(v, (-1,)) for v in values])
    flat = jnp.sum(lax.all_gather(flat, "term", axis=0, tiled=False), axis=0)
    flat = jnp.sum(lax.all_gather(flat, "doc", axis=0, tiled=False), axis=0)
    out, start = [], 0
    for v in values:
        size = int(jnp.size(v))
        out.append(flat[start : start + size].reshape(jnp.shape(v)))
        start += size
    return out


def per_device(n_doc, n_term, tiles, tile_rows, tile_cols, tile_count, start_block, doc_cluster, term_cluster):
    local_tiles = tiles[0, 0]
    rows = tile_rows[0, 0]
    cols = tile_cols[0, 0]
    count = tile_count[0, 0].reshape(1)
    edge = local_tiles.shape[1]
    start_rows = start_block[0]
    width_k = start_rows.shape[1]
    term_tiles_own = start_rows.shape[0] // edge
    start_t = start_rows.reshape(term_tiles_own, edge, width_k).transpose(0, 2, 1)
    doc_labels = doc_cluster[0].reshape(-1, edge)
    term_labels = term_cluster[0].reshape(-1, edge)
    clusters = jnp.arange(CLUSTERS, dtype=jnp.int32)

    weights = start_t
    basis = None
    doc_degree = None
    term_degree = None
    root = None
    summed_own = None
    energy = None
    volume = None
    for step in range(ITERS):
        first = step == 0
        w_all = lax.all_gather(weights, "doc", axis=0, tiled=True)
        left = tile_pass(local_tiles, rows, cols, count, w_all, True, first)
        left_own = scatter_sum(left, "term", n_term)
        summed_own = left_own[:, :width_k, :]
        if first:
            doc_degree = left_own[:, width_k, :]
        quotient = (summed_own / doc_degree[:, None, :]).astype(jnp.bfloat16)
        q_all = lax.all_gather(quotient, "term", axis=0, tiled=True)
        right = tile_pass(local_tiles, rows, cols, count, q_all, False, first)
        right_own = scatter_sum(right, "doc", n_doc)
        if first:
            term_degree = right_own[:, width_k, :]
            root = jnp.sqrt(term_degree)
        raw = right_own[:, :width_k, :] / root[:, None, :]
        previous = root[:, None, :] * start_t.astype(jnp.float32) if first else basis
        gram_part = jnp.einsum("tki,tli->kl", raw, raw, precision=HIGH)
        along_part = jnp.einsum("tki,ti->k", raw, root, precision=HIGH)
        energy_part = jnp.sum(previous * raw, axis=(0, 2))
        volume_part = jnp.sum(term_degree)
        gram_matrix, along, energy, volume = small_sum((gram_part, along_part, energy_part, volume_part))
        lower = jnp.linalg.cholesky(gram_matrix - jnp.outer(along, along) / volume)
        projected = raw - root[:, None, :] * (along / volume)[None, :, None]
        flat = projected.transpose(1, 0, 2).reshape(width_k, -1)
        solved = jax.scipy.linalg.solve_triangular(lower, flat, lower=True)
        basis = solved.reshape(width_k, term_tiles_own, edge).transpose(1, 0, 2)
        weights = (basis / root[:, None, :]).astype(jnp.bfloat16)

    scale = jnp.sqrt(volume)
    column_scale = scale * lax.rsqrt(energy)
    doc_embed = summed_own / doc_degree[:, None, :] * column_scale[None, :, None]
    term_embed = scale * basis / root[:, None, :]
    doc_onehot = (doc_labels[:, :, None] == clusters).astype(jnp.float32)
    term_onehot = (term_labels[:, :, None] == clusters).astype(jnp.float32)
    center_part = jnp.einsum("tki,tij->kj", doc_embed, doc_onehot, precision=HIGH) + jnp.einsum(
        "tki,tij->kj", term_embed, term_onehot, precision=HIGH
    )
    count_part = jnp.sum(doc_onehot, axis=(0, 1)) + jnp.sum(term_onehot, axis=(0, 1))
    center_sums, counts = small_sum((center_part, count_part))
    centers = center_sums / counts[None, :]
    center_norm = jnp.sum(centers * centers, axis=0)

    def distances(embed):
        near = jnp.einsum("tki,kj->tij", embed, centers, precision=HIGH)
        norm = jnp.sum(embed * embed, axis=1)
        dist = (norm[:, :, None] - 2.0 * near + center_norm[None, None, :]) / width_k
        return dist.reshape(-1, CLUSTERS)

    return (distances(doc_embed)[None], distances(term_embed)[None])


def solution(mesh):
    placed = (
        P("doc", "term", None, None, None),
        P("doc", "term", None),
        P("doc", "term", None),
        P("doc", "term"),
        P("term", "doc", None),
        P("doc", "term"),
        P("term", "doc"),
    )
    return jax.shard_map(
        functools.partial(per_device, mesh.shape["doc"], mesh.shape["term"]),
        mesh=mesh,
        in_specs=placed,
        out_specs=(P("doc", "term", None), P("term", "doc", None)),
        check_vma=False,
    )
```

```python
import functools

import jax
import jax.numpy as jnp
from jax import lax
from jax.experimental import pallas as pl
from jax.experimental.pallas import tpu as pltpu
from jax.sharding import PartitionSpec as P

CLUSTERS = 64
ITERS = 2
CHUNK = 64
GROUP = 4
DEG_ROWS = 8

HIGH = lax.Precision.HIGHEST
NT_DIMS = (((1,), (1,)), ((), ()))


def tile_kernel(transpose_tile, with_degree, group, rows_ref, cols_ref, cnt_ref, tiles_ref, side_ref, out_ref):
    step = pl.program_id(0)
    chunk = tiles_ref.shape[0]
    width = side_ref.shape[1]

    @pl.when(step == 0)
    def _():
        out_ref[...] = jnp.zeros_like(out_ref)

    count = cnt_ref[0]
    base = step * chunk
    live = jnp.clip(count - base, 0, chunk)
    ones = jnp.ones((DEG_ROWS, tiles_ref.shape[2]), jnp.bfloat16)

    def product(lhs, tile):
        if transpose_tile:
            return lax.dot_general(lhs, tile, NT_DIMS, preferred_element_type=jnp.float32)
        return jnp.dot(lhs, tile, preferred_element_type=jnp.float32)

    def body(g, carry):
        results = []
        for u in range(group):
            j = g * group + u
            slot = base + j
            if transpose_tile:
                src, dst = cols_ref[slot], rows_ref[slot]
            else:
                src, dst = rows_ref[slot], cols_ref[slot]
            tile = tiles_ref[j]
            keep = slot < count
            prod = jnp.where(keep, product(side_ref[src], tile), 0.0)
            deg = jnp.where(keep, product(ones, tile), 0.0) if with_degree else None
            results.append((dst, prod, deg))
        for dst, prod, deg in results:
            out_ref[dst, pl.ds(0, width), :] += prod
            if with_degree:
                out_ref[dst, pl.ds(width, DEG_ROWS), :] += deg
        return carry

    lax.fori_loop(0, (live + group - 1) // group, body, 0)


def tile_pass(tiles, rows, cols, count, side, transpose_tile, with_degree):
    slots, edge, _ = tiles.shape
    n_tiles, width, _ = side.shape
    chunk = min(CHUNK, slots)
    steps = slots // chunk
    out_rows = width + (DEG_ROWS if with_degree else 0)
    kernel = functools.partial(tile_kernel, transpose_tile, with_degree, GROUP)

    def tile_map(i, rows_ref, cols_ref, cnt_ref):
        return (jnp.minimum(i, jnp.maximum(cnt_ref[0] - 1, 0) // chunk), 0, 0)

    def whole_map(i, rows_ref, cols_ref, cnt_ref):
        return (0, 0, 0)

    flops = 2 * slots * edge * edge * out_rows
    cost = pl.CostEstimate(
        flops=flops,
        transcendentals=0,
        bytes_accessed=tiles.size * 2 + side.size * 2 + n_tiles * out_rows * edge * 4,
    )
    return pl.pallas_call(
        kernel,
        out_shape=jax.ShapeDtypeStruct((n_tiles, out_rows, edge), jnp.float32),
        grid_spec=pltpu.PrefetchScalarGridSpec(
            num_scalar_prefetch=3,
            grid=(steps,),
            in_specs=[
                pl.BlockSpec((chunk, edge, edge), tile_map),
                pl.BlockSpec((n_tiles, width, edge), whole_map),
            ],
            out_specs=pl.BlockSpec((n_tiles, out_rows, edge), whole_map),
        ),
        compiler_params=pltpu.CompilerParams(dimension_semantics=("arbitrary",)),
        cost_estimate=cost,
    )(rows, cols, count, tiles, side)


def scatter_sum(x, axis_name, parts):
    pieces = x.reshape((parts, x.shape[0] // parts) + x.shape[1:])
    return jnp.sum(lax.all_to_all(pieces, axis_name, 0, 0, tiled=False), axis=0)


def packed_psum(values):
    flat = jnp.concatenate([jnp.reshape(v, (-1,)) for v in values])
    flat = lax.psum(flat, ("doc", "term"))
    out, start = [], 0
    for v in values:
        size = int(jnp.size(v))
        out.append(flat[start : start + size].reshape(jnp.shape(v)))
        start += size
    return out


def per_device(n_doc, n_term, tiles, tile_rows, tile_cols, tile_count, start_block, doc_cluster, term_cluster):
    local_tiles = tiles[0, 0]
    rows = tile_rows[0, 0]
    cols = tile_cols[0, 0]
    count = tile_count[0, 0].reshape(1)
    edge = local_tiles.shape[1]
    start_rows = start_block[0]
    width_k = start_rows.shape[1]
    term_tiles_own = start_rows.shape[0] // edge
    start_t = start_rows.reshape(term_tiles_own, edge, width_k).transpose(0, 2, 1)
    doc_labels = doc_cluster[0].reshape(-1, edge)
    term_labels = term_cluster[0].reshape(-1, edge)
    clusters = jnp.arange(CLUSTERS, dtype=jnp.int32)
    doc_onehot = (doc_labels[:, :, None] == clusters).astype(jnp.float32)
    term_onehot = (term_labels[:, :, None] == clusters).astype(jnp.float32)

    weights = start_t
    basis = None
    doc_degree = None
    term_degree = None
    root = None
    summed_own = None
    energy = None
    volume = None
    for step in range(ITERS):
        first = step == 0
        w_all = lax.all_gather(weights, "doc", axis=0, tiled=True)
        left = tile_pass(local_tiles, rows, cols, count, w_all, True, first)
        left_own = lax.psum_scatter(left, "term", scatter_dimension=0, tiled=True)
        summed_own = left_own[:, :width_k, :]
        if first:
            doc_degree = left_own[:, width_k, :]
        quotient = (summed_own / doc_degree[:, None, :]).astype(jnp.bfloat16)
        q_all = lax.all_gather(quotient, "term", axis=0, tiled=True)
        right = tile_pass(local_tiles, rows, cols, count, q_all, False, first)
        right_own = scatter_sum(right, "doc", n_doc)
        if first:
            term_degree = right_own[:, width_k, :]
            root = jnp.sqrt(term_degree)
        raw = right_own[:, :width_k, :] / root[:, None, :]
        previous = root[:, None, :] * start_t.astype(jnp.float32) if first else basis
        gram_part = jnp.einsum("tki,tli->kl", raw, raw, precision=HIGH)
        along_part = jnp.einsum("tki,ti->k", raw, root, precision=HIGH)
        energy_part = jnp.sum(previous * raw, axis=(0, 2))
        volume_part = jnp.sum(term_degree)
        sums = [gram_part, along_part, energy_part, volume_part]
        if step == ITERS - 1:
            doc_ratio = summed_own / doc_degree[:, None, :]
            doc_part = jnp.einsum("tki,tij->kj", doc_ratio, doc_onehot, precision=HIGH)
            term_part = jnp.einsum("tki,tij->kj", raw / root[:, None, :], term_onehot, precision=HIGH)
            sums += [doc_part, term_part, jnp.sum(doc_onehot, axis=(0, 1)), jnp.sum(term_onehot, axis=(0, 1))]
        sums = packed_psum(sums)
        gram_matrix, along, energy, volume = sums[:4]
        lower = jnp.linalg.cholesky(gram_matrix - jnp.outer(along, along) / volume)
        projected = raw - root[:, None, :] * (along / volume)[None, :, None]
        flat = projected.transpose(1, 0, 2).reshape(width_k, -1)
        solved = jax.scipy.linalg.solve_triangular(lower, flat, lower=True)
        basis = solved.reshape(width_k, term_tiles_own, edge).transpose(1, 0, 2)
        weights = (basis / root[:, None, :]).astype(jnp.bfloat16)

    doc_part, term_part, doc_count, term_count = sums[4:]
    scale = jnp.sqrt(volume)
    column_scale = scale * lax.rsqrt(energy)
    doc_embed = summed_own / doc_degree[:, None, :] * column_scale[None, :, None]
    term_embed = scale * basis / root[:, None, :]
    term_centered = term_part - jnp.outer(along / volume, term_count)
    term_sums = scale * jax.scipy.linalg.solve_triangular(lower, term_centered, lower=True)
    centers = (column_scale[:, None] * doc_part + term_sums) / (doc_count + term_count)[None, :]
    center_norm = jnp.sum(centers * centers, axis=0)

    def distances(embed):
        near = jnp.einsum("tki,kj->tij", embed, centers, precision=HIGH)
        norm = jnp.sum(embed * embed, axis=1)
        dist = (norm[:, :, None] - 2.0 * near + center_norm[None, None, :]) / width_k
        return dist.reshape(-1, CLUSTERS)

    return (distances(doc_embed)[None], distances(term_embed)[None])


def solution(mesh):
    placed = (
        P("doc", "term", None, None, None),
        P("doc", "term", None),
        P("doc", "term", None),
        P("doc", "term"),
        P("term", "doc", None),
        P("doc", "term"),
        P("term", "doc"),
    )
    return jax.shard_map(
        functools.partial(per_device, mesh.shape["doc"], mesh.shape["term"]),
        mesh=mesh,
        in_specs=placed,
        out_specs=(P("doc", "term", None), P("term", "doc", None)),
        check_vma=False,
    )
```

```python
import functools

import jax
import jax.numpy as jnp
from jax import lax
from jax.experimental import pallas as pl
from jax.experimental.pallas import tpu as pltpu
from jax.sharding import PartitionSpec as P

CLUSTERS = 64
ITERS = 2
CHUNK = 128
GROUP = 8
DEG_ROWS = 8

HIGH = lax.Precision.HIGHEST
NT_DIMS = (((1,), (1,)), ((), ()))


def tile_kernel(transpose_tile, with_degree, group, rows_ref, cols_ref, cnt_ref, tiles_ref, side_ref, out_ref):
    step = pl.program_id(0)
    chunk = tiles_ref.shape[0]
    width = side_ref.shape[1]

    @pl.when(step == 0)
    def _():
        out_ref[...] = jnp.zeros_like(out_ref)

    count = cnt_ref[0]
    base = step * chunk
    live = jnp.clip(count - base, 0, chunk)
    ones = jnp.ones((DEG_ROWS, tiles_ref.shape[2]), jnp.bfloat16)

    def product(lhs, tile):
        if transpose_tile:
            return lax.dot_general(lhs, tile, NT_DIMS, preferred_element_type=jnp.float32)
        return jnp.dot(lhs, tile, preferred_element_type=jnp.float32)

    def body(g, carry):
        results = []
        for u in range(group):
            j = g * group + u
            slot = base + j
            if transpose_tile:
                src, dst = cols_ref[slot], rows_ref[slot]
            else:
                src, dst = rows_ref[slot], cols_ref[slot]
            tile = tiles_ref[j]
            keep = slot < count
            prod = jnp.where(keep, product(side_ref[src], tile), 0.0)
            deg = jnp.where(keep, product(ones, tile), 0.0) if with_degree else None
            results.append((dst, prod, deg))
        for dst, prod, deg in results:
            out_ref[dst, pl.ds(0, width), :] += prod
            if with_degree:
                out_ref[dst, pl.ds(width, DEG_ROWS), :] += deg
        return carry

    lax.fori_loop(0, (live + group - 1) // group, body, 0)


def tile_pass(tiles, rows, cols, count, side, transpose_tile, with_degree):
    slots, edge, _ = tiles.shape
    n_tiles, width, _ = side.shape
    chunk = min(CHUNK, slots)
    steps = slots // chunk
    out_rows = width + (DEG_ROWS if with_degree else 0)
    kernel = functools.partial(tile_kernel, transpose_tile, with_degree, GROUP)

    def tile_map(i, rows_ref, cols_ref, cnt_ref):
        return (jnp.minimum(i, jnp.maximum(cnt_ref[0] - 1, 0) // chunk), 0, 0)

    def whole_map(i, rows_ref, cols_ref, cnt_ref):
        return (0, 0, 0)

    flops = 2 * slots * edge * edge * out_rows
    cost = pl.CostEstimate(
        flops=flops,
        transcendentals=0,
        bytes_accessed=tiles.size * 2 + side.size * 2 + n_tiles * out_rows * edge * 4,
    )
    return pl.pallas_call(
        kernel,
        out_shape=jax.ShapeDtypeStruct((n_tiles, out_rows, edge), jnp.float32),
        grid_spec=pltpu.PrefetchScalarGridSpec(
            num_scalar_prefetch=3,
            grid=(steps,),
            in_specs=[
                pl.BlockSpec((chunk, edge, edge), tile_map),
                pl.BlockSpec((n_tiles, width, edge), whole_map),
            ],
            out_specs=pl.BlockSpec((n_tiles, out_rows, edge), whole_map),
        ),
        compiler_params=pltpu.CompilerParams(dimension_semantics=("arbitrary",)),
        cost_estimate=cost,
    )(rows, cols, count, tiles, side)


def scatter_sum(x, axis_name, parts):
    pieces = x.reshape((parts, x.shape[0] // parts) + x.shape[1:])
    return jnp.sum(lax.all_to_all(pieces, axis_name, 0, 0, tiled=False), axis=0)


def packed_psum(values):
    flat = jnp.concatenate([jnp.reshape(v, (-1,)) for v in values])
    flat = lax.psum(lax.psum(flat, "term"), "doc")
    out, start = [], 0
    for v in values:
        size = int(jnp.size(v))
        out.append(flat[start : start + size].reshape(jnp.shape(v)))
        start += size
    return out


def per_device(n_doc, n_term, tiles, tile_rows, tile_cols, tile_count, start_block, doc_cluster, term_cluster):
    local_tiles = tiles[0, 0]
    rows = tile_rows[0, 0]
    cols = tile_cols[0, 0]
    count = tile_count[0, 0].reshape(1)
    edge = local_tiles.shape[1]
    start_rows = start_block[0]
    width_k = start_rows.shape[1]
    term_tiles_own = start_rows.shape[0] // edge
    start_t = start_rows.reshape(term_tiles_own, edge, width_k).transpose(0, 2, 1)
    doc_labels = doc_cluster[0].reshape(-1, edge)
    term_labels = term_cluster[0].reshape(-1, edge)
    clusters = jnp.arange(CLUSTERS, dtype=jnp.int32)
    doc_onehot = (doc_labels[:, :, None] == clusters).astype(jnp.float32)
    term_onehot = (term_labels[:, :, None] == clusters).astype(jnp.float32)

    weights = start_t
    basis = None
    doc_degree = None
    term_degree = None
    root = None
    summed_own = None
    energy = None
    volume = None
    for step in range(ITERS):
        first = step == 0
        w_all = lax.all_gather(weights, "doc", axis=0, tiled=True)
        left = tile_pass(local_tiles, rows, cols, count, w_all, True, first)
        left_own = lax.psum_scatter(left, "term", scatter_dimension=0, tiled=True)
        summed_own = left_own[:, :width_k, :]
        if first:
            doc_degree = left_own[:, width_k, :]
        quotient = (summed_own / doc_degree[:, None, :]).astype(jnp.bfloat16)
        q_all = lax.all_gather(quotient, "term", axis=0, tiled=True)
        right = tile_pass(local_tiles, rows, cols, count, q_all, False, first)
        right_own = scatter_sum(right, "doc", n_doc)
        if first:
            term_degree = right_own[:, width_k, :]
            root = jnp.sqrt(term_degree)
        raw = right_own[:, :width_k, :] / root[:, None, :]
        previous = root[:, None, :] * start_t.astype(jnp.float32) if first else basis
        gram_part = jnp.einsum("tki,tli->kl", raw, raw, precision=HIGH)
        along_part = jnp.einsum("tki,ti->k", raw, root, precision=HIGH)
        energy_part = jnp.sum(previous * raw, axis=(0, 2))
        volume_part = jnp.sum(term_degree)
        sums = [gram_part, along_part, energy_part, volume_part]
        if step == ITERS - 1:
            doc_ratio = summed_own / doc_degree[:, None, :]
            doc_part = jnp.einsum("tki,tij->kj", doc_ratio, doc_onehot, precision=HIGH)
            term_part = jnp.einsum("tki,tij->kj", raw / root[:, None, :], term_onehot, precision=HIGH)
            sums += [doc_part, term_part, jnp.sum(doc_onehot, axis=(0, 1)), jnp.sum(term_onehot, axis=(0, 1))]
        sums = packed_psum(sums)
        gram_matrix, along, energy, volume = sums[:4]
        lower = jnp.linalg.cholesky(gram_matrix - jnp.outer(along, along) / volume)
        projected = raw - root[:, None, :] * (along / volume)[None, :, None]
        flat = projected.transpose(1, 0, 2).reshape(width_k, -1)
        solved = jax.scipy.linalg.solve_triangular(lower, flat, lower=True)
        basis = solved.reshape(width_k, term_tiles_own, edge).transpose(1, 0, 2)
        weights = (basis / root[:, None, :]).astype(jnp.bfloat16)

    doc_part, term_part, doc_count, term_count = sums[4:]
    scale = jnp.sqrt(volume)
    column_scale = scale * lax.rsqrt(energy)
    doc_embed = summed_own / doc_degree[:, None, :] * column_scale[None, :, None]
    term_embed = scale * basis / root[:, None, :]
    term_centered = term_part - jnp.outer(along / volume, term_count)
    term_sums = scale * jax.scipy.linalg.solve_triangular(lower, term_centered, lower=True)
    centers = (column_scale[:, None] * doc_part + term_sums) / (doc_count + term_count)[None, :]
    center_norm = jnp.sum(centers * centers, axis=0)

    def distances(embed):
        near = jnp.einsum("tki,kj->tij", embed, centers, precision=HIGH)
        norm = jnp.sum(embed * embed, axis=1)
        dist = (norm[:, :, None] - 2.0 * near + center_norm[None, None, :]) / width_k
        return dist.reshape(-1, CLUSTERS)

    return (distances(doc_embed)[None], distances(term_embed)[None])


def solution(mesh):
    placed = (
        P("doc", "term", None, None, None),
        P("doc", "term", None),
        P("doc", "term", None),
        P("doc", "term"),
        P("term", "doc", None),
        P("doc", "term"),
        P("term", "doc"),
    )
    return jax.shard_map(
        functools.partial(per_device, mesh.shape["doc"], mesh.shape["term"]),
        mesh=mesh,
        in_specs=placed,
        out_specs=(P("doc", "term", None), P("term", "doc", None)),
        check_vma=False,
    )
```

```python
import functools

import jax
import jax.numpy as jnp
from jax import lax
from jax.experimental import pallas as pl
from jax.experimental.pallas import tpu as pltpu
from jax.sharding import PartitionSpec as P

CLUSTERS = 64
ITERS = 2
CHUNK = 128
GROUP = 8
DEG_ROWS = 8

HIGH = lax.Precision.HIGHEST
NT_DIMS = (((1,), (1,)), ((), ()))


def tile_kernel(transpose_tile, with_degree, group, rows_ref, cols_ref, cnt_ref, tiles_ref, side_ref, out_ref):
    step = pl.program_id(0)
    chunk = tiles_ref.shape[0]
    width = side_ref.shape[1]

    @pl.when(step == 0)
    def _():
        out_ref[...] = jnp.zeros_like(out_ref)

    count = cnt_ref[0]
    base = step * chunk
    live = jnp.clip(count - base, 0, chunk)
    ones = jnp.ones((DEG_ROWS, tiles_ref.shape[2]), jnp.bfloat16)

    def product(lhs, tile):
        if transpose_tile:
            return lax.dot_general(lhs, tile, NT_DIMS, preferred_element_type=jnp.float32)
        return jnp.dot(lhs, tile, preferred_element_type=jnp.float32)

    def body(g, carry):
        results = []
        for u in range(group):
            j = g * group + u
            slot = base + j
            if transpose_tile:
                src, dst = cols_ref[slot], rows_ref[slot]
            else:
                src, dst = rows_ref[slot], cols_ref[slot]
            tile = tiles_ref[j]
            keep = slot < count
            prod = jnp.where(keep, product(side_ref[src], tile), 0.0)
            deg = jnp.where(keep, product(ones, tile), 0.0) if with_degree else None
            results.append((dst, prod, deg))
        for dst, prod, deg in results:
            out_ref[dst, pl.ds(0, width), :] += prod
            if with_degree:
                out_ref[dst, pl.ds(width, DEG_ROWS), :] += deg
        return carry

    lax.fori_loop(0, (live + group - 1) // group, body, 0)


def tile_pass(tiles, rows, cols, count, side, transpose_tile, with_degree):
    slots, edge, _ = tiles.shape
    n_tiles, width, _ = side.shape
    chunk = min(CHUNK, slots)
    steps = slots // chunk
    out_rows = width + (DEG_ROWS if with_degree else 0)
    kernel = functools.partial(tile_kernel, transpose_tile, with_degree, GROUP)

    def tile_map(i, rows_ref, cols_ref, cnt_ref):
        return (jnp.minimum(i, jnp.maximum(cnt_ref[0] - 1, 0) // chunk), 0, 0)

    def whole_map(i, rows_ref, cols_ref, cnt_ref):
        return (0, 0, 0)

    flops = 2 * slots * edge * edge * out_rows
    cost = pl.CostEstimate(
        flops=flops,
        transcendentals=0,
        bytes_accessed=tiles.size * 2 + side.size * 2 + n_tiles * out_rows * edge * 4,
    )
    return pl.pallas_call(
        kernel,
        out_shape=jax.ShapeDtypeStruct((n_tiles, out_rows, edge), jnp.float32),
        grid_spec=pltpu.PrefetchScalarGridSpec(
            num_scalar_prefetch=3,
            grid=(steps,),
            in_specs=[
                pl.BlockSpec((chunk, edge, edge), tile_map),
                pl.BlockSpec((n_tiles, width, edge), whole_map),
            ],
            out_specs=pl.BlockSpec((n_tiles, out_rows, edge), whole_map),
        ),
        compiler_params=pltpu.CompilerParams(dimension_semantics=("arbitrary",)),
        cost_estimate=cost,
    )(rows, cols, count, tiles, side)


def scatter_sum(x, axis_name, parts):
    pieces = x.reshape((parts, x.shape[0] // parts) + x.shape[1:])
    return jnp.sum(lax.all_to_all(pieces, axis_name, 0, 0, tiled=False), axis=0)


def exchange_sum(flat, axis_name, parts):
    copies = jnp.broadcast_to(flat, (parts,) + flat.shape)
    return jnp.sum(lax.all_to_all(copies, axis_name, 0, 0, tiled=False), axis=0)


def exchange_gather(x, axis_name, parts):
    copies = jnp.broadcast_to(x, (parts,) + x.shape)
    got = lax.all_to_all(copies, axis_name, 0, 0, tiled=False)
    return got.reshape((parts * x.shape[0],) + x.shape[1:])


def packed_psum(n_doc, n_term, values):
    flat = jnp.concatenate([jnp.reshape(v, (-1,)) for v in values])
    flat = exchange_sum(exchange_sum(flat, "term", n_term), "doc", n_doc)
    out, start = [], 0
    for v in values:
        size = int(jnp.size(v))
        out.append(flat[start : start + size].reshape(jnp.shape(v)))
        start += size
    return out


def per_device(n_doc, n_term, tiles, tile_rows, tile_cols, tile_count, start_block, doc_cluster, term_cluster):
    local_tiles = tiles[0, 0]
    rows = tile_rows[0, 0]
    cols = tile_cols[0, 0]
    count = tile_count[0, 0].reshape(1)
    edge = local_tiles.shape[1]
    start_rows = start_block[0]
    width_k = start_rows.shape[1]
    term_tiles_own = start_rows.shape[0] // edge
    start_t = start_rows.reshape(term_tiles_own, edge, width_k).transpose(0, 2, 1)
    doc_labels = doc_cluster[0].reshape(-1, edge)
    term_labels = term_cluster[0].reshape(-1, edge)
    clusters = jnp.arange(CLUSTERS, dtype=jnp.int32)
    doc_onehot = (doc_labels[:, :, None] == clusters).astype(jnp.float32)
    term_onehot = (term_labels[:, :, None] == clusters).astype(jnp.float32)

    weights = start_t
    basis = None
    doc_degree = None
    term_degree = None
    root = None
    summed_own = None
    energy = None
    volume = None
    for step in range(ITERS):
        first = step == 0
        w_all = exchange_gather(weights, "doc", n_doc)
        left = tile_pass(local_tiles, rows, cols, count, w_all, True, first)
        left_own = lax.psum_scatter(left, "term", scatter_dimension=0, tiled=True)
        summed_own = left_own[:, :width_k, :]
        if first:
            doc_degree = left_own[:, width_k, :]
        quotient = (summed_own / doc_degree[:, None, :]).astype(jnp.bfloat16)
        q_all = lax.all_gather(quotient, "term", axis=0, tiled=True)
        right = tile_pass(local_tiles, rows, cols, count, q_all, False, first)
        right_own = scatter_sum(right, "doc", n_doc)
        if first:
            term_degree = right_own[:, width_k, :]
            root = jnp.sqrt(term_degree)
        raw = right_own[:, :width_k, :] / root[:, None, :]
        previous = root[:, None, :] * start_t.astype(jnp.float32) if first else basis
        gram_part = jnp.einsum("tki,tli->kl", raw, raw, precision=HIGH)
        along_part = jnp.einsum("tki,ti->k", raw, root, precision=HIGH)
        energy_part = jnp.sum(previous * raw, axis=(0, 2))
        volume_part = jnp.sum(term_degree)
        sums = [gram_part, along_part, energy_part, volume_part]
        if step == ITERS - 1:
            doc_ratio = summed_own / doc_degree[:, None, :]
            doc_part = jnp.einsum("tki,tij->kj", doc_ratio, doc_onehot, precision=HIGH)
            term_part = jnp.einsum("tki,tij->kj", raw / root[:, None, :], term_onehot, precision=HIGH)
            sums += [doc_part, term_part, jnp.sum(doc_onehot, axis=(0, 1)), jnp.sum(term_onehot, axis=(0, 1))]
        sums = packed_psum(n_doc, n_term, sums)
        gram_matrix, along, energy, volume = sums[:4]
        lower = jnp.linalg.cholesky(gram_matrix - jnp.outer(along, along) / volume)
        projected = raw - root[:, None, :] * (along / volume)[None, :, None]
        flat = projected.transpose(1, 0, 2).reshape(width_k, -1)
        solved = jax.scipy.linalg.solve_triangular(lower, flat, lower=True)
        basis = solved.reshape(width_k, term_tiles_own, edge).transpose(1, 0, 2)
        weights = (basis / root[:, None, :]).astype(jnp.bfloat16)

    doc_part, term_part, doc_count, term_count = sums[4:]
    scale = jnp.sqrt(volume)
    column_scale = scale * lax.rsqrt(energy)
    doc_embed = summed_own / doc_degree[:, None, :] * column_scale[None, :, None]
    term_embed = scale * basis / root[:, None, :]
    term_centered = term_part - jnp.outer(along / volume, term_count)
    term_sums = scale * jax.scipy.linalg.solve_triangular(lower, term_centered, lower=True)
    centers = (column_scale[:, None] * doc_part + term_sums) / (doc_count + term_count)[None, :]
    center_norm = jnp.sum(centers * centers, axis=0)

    def distances(embed):
        near = jnp.einsum("tki,kj->tij", embed, centers, precision=HIGH)
        norm = jnp.sum(embed * embed, axis=1)
        dist = (norm[:, :, None] - 2.0 * near + center_norm[None, None, :]) / width_k
        return dist.reshape(-1, CLUSTERS)

    return (distances(doc_embed)[None], distances(term_embed)[None])


def solution(mesh):
    placed = (
        P("doc", "term", None, None, None),
        P("doc", "term", None),
        P("doc", "term", None),
        P("doc", "term"),
        P("term", "doc", None),
        P("doc", "term"),
        P("term", "doc"),
    )
    return jax.shard_map(
        functools.partial(per_device, mesh.shape["doc"], mesh.shape["term"]),
        mesh=mesh,
        in_specs=placed,
        out_specs=(P("doc", "term", None), P("term", "doc", None)),
        check_vma=False,
    )
```

```python
import functools

import jax
import jax.numpy as jnp
from jax import lax
from jax.experimental import pallas as pl
from jax.experimental.pallas import tpu as pltpu
from jax.sharding import PartitionSpec as P

CLUSTERS = 64
ITERS = 2
CHUNK = 128
GROUP = 8
DEG_ROWS = 8

HIGH = lax.Precision.HIGHEST
NT_DIMS = (((1,), (1,)), ((), ()))


def tile_kernel(transpose_tile, with_degree, group, rows_ref, cols_ref, cnt_ref, tiles_ref, side_ref, out_ref):
    step = pl.program_id(0)
    chunk = tiles_ref.shape[0]
    width = side_ref.shape[1]

    @pl.when(step == 0)
    def _():
        out_ref[...] = jnp.zeros_like(out_ref)

    count = cnt_ref[0]
    base = step * chunk
    live = jnp.clip(count - base, 0, chunk)
    ones = jnp.ones((DEG_ROWS, tiles_ref.shape[2]), jnp.bfloat16)

    def product(lhs, tile):
        if transpose_tile:
            return lax.dot_general(lhs, tile, NT_DIMS, preferred_element_type=jnp.float32)
        return jnp.dot(lhs, tile, preferred_element_type=jnp.float32)

    def body(g, carry):
        results = []
        for u in range(group):
            j = g * group + u
            slot = base + j
            if transpose_tile:
                src, dst = cols_ref[slot], rows_ref[slot]
            else:
                src, dst = rows_ref[slot], cols_ref[slot]
            tile = tiles_ref[j]
            keep = slot < count
            prod = jnp.where(keep, product(side_ref[src], tile), 0.0)
            deg = jnp.where(keep, product(ones, tile), 0.0) if with_degree else None
            results.append((dst, prod, deg))
        for dst, prod, deg in results:
            out_ref[dst, pl.ds(0, width), :] += prod
            if with_degree:
                out_ref[dst, pl.ds(width, DEG_ROWS), :] += deg
        return carry

    lax.fori_loop(0, (live + group - 1) // group, body, 0)


def tile_pass(tiles, rows, cols, count, side, transpose_tile, with_degree):
    slots, edge, _ = tiles.shape
    n_tiles, width, _ = side.shape
    chunk = min(CHUNK, slots)
    steps = slots // chunk
    out_rows = width + (DEG_ROWS if with_degree else 0)
    kernel = functools.partial(tile_kernel, transpose_tile, with_degree, GROUP)

    def tile_map(i, rows_ref, cols_ref, cnt_ref):
        return (jnp.minimum(i, jnp.maximum(cnt_ref[0] - 1, 0) // chunk), 0, 0)

    def whole_map(i, rows_ref, cols_ref, cnt_ref):
        return (0, 0, 0)

    flops = 2 * slots * edge * edge * out_rows
    cost = pl.CostEstimate(
        flops=flops,
        transcendentals=0,
        bytes_accessed=tiles.size * 2 + side.size * 2 + n_tiles * out_rows * edge * 4,
    )
    return pl.pallas_call(
        kernel,
        out_shape=jax.ShapeDtypeStruct((n_tiles, out_rows, edge), jnp.float32),
        grid_spec=pltpu.PrefetchScalarGridSpec(
            num_scalar_prefetch=3,
            grid=(steps,),
            in_specs=[
                pl.BlockSpec((chunk, edge, edge), tile_map),
                pl.BlockSpec((n_tiles, width, edge), whole_map),
            ],
            out_specs=pl.BlockSpec((n_tiles, out_rows, edge), whole_map),
        ),
        compiler_params=pltpu.CompilerParams(dimension_semantics=("arbitrary",)),
        cost_estimate=cost,
    )(rows, cols, count, tiles, side)


def scatter_sum(x, axis_name, parts):
    pieces = x.reshape((parts, x.shape[0] // parts) + x.shape[1:])
    return jnp.sum(lax.all_to_all(pieces, axis_name, 0, 0, tiled=False), axis=0)


def exchange_sum(flat, axis_name, parts):
    copies = jnp.broadcast_to(flat, (parts,) + flat.shape)
    return jnp.sum(lax.all_to_all(copies, axis_name, 0, 0, tiled=False), axis=0)


def exchange_gather(x, axis_name, parts):
    copies = jnp.broadcast_to(x, (parts,) + x.shape)
    got = lax.all_to_all(copies, axis_name, 0, 0, tiled=False)
    return got.reshape((parts * x.shape[0],) + x.shape[1:])


def line_scatter_sum(x, axis_name, parts):
    me = lax.axis_index(axis_name)
    chunks = x.reshape((parts, x.shape[0] // parts) + x.shape[1:])

    def chunk(index):
        return lax.dynamic_index_in_dim(chunks, jnp.clip(index, 0, parts - 1), 0, keepdims=False)

    rightward = leftward = None
    for s in range(1, parts):
        send_r = chunk(parts - s + me)
        send_l = chunk(s - parts + me)
        if rightward is not None:
            send_r = send_r + rightward
            send_l = send_l + leftward
        rightward = lax.ppermute(send_r, axis_name, [(i, i + 1) for i in range(s)])
        leftward = lax.ppermute(send_l, axis_name, [(parts - 1 - i, parts - 2 - i) for i in range(s)])
    return chunk(me) + rightward + leftward


def packed_psum(n_doc, n_term, values):
    flat = jnp.concatenate([jnp.reshape(v, (-1,)) for v in values])
    flat = exchange_sum(exchange_sum(flat, "term", n_term), "doc", n_doc)
    out, start = [], 0
    for v in values:
        size = int(jnp.size(v))
        out.append(flat[start : start + size].reshape(jnp.shape(v)))
        start += size
    return out


def per_device(n_doc, n_term, tiles, tile_rows, tile_cols, tile_count, start_block, doc_cluster, term_cluster):
    local_tiles = tiles[0, 0]
    rows = tile_rows[0, 0]
    cols = tile_cols[0, 0]
    count = tile_count[0, 0].reshape(1)
    edge = local_tiles.shape[1]
    start_rows = start_block[0]
    width_k = start_rows.shape[1]
    term_tiles_own = start_rows.shape[0] // edge
    start_t = start_rows.reshape(term_tiles_own, edge, width_k).transpose(0, 2, 1)
    doc_labels = doc_cluster[0].reshape(-1, edge)
    term_labels = term_cluster[0].reshape(-1, edge)
    clusters = jnp.arange(CLUSTERS, dtype=jnp.int32)
    doc_onehot = (doc_labels[:, :, None] == clusters).astype(jnp.float32)
    term_onehot = (term_labels[:, :, None] == clusters).astype(jnp.float32)

    weights = start_t
    basis = None
    doc_degree = None
    term_degree = None
    root = None
    summed_own = None
    energy = None
    volume = None
    for step in range(ITERS):
        first = step == 0
        w_all = exchange_gather(weights, "doc", n_doc)
        left = tile_pass(local_tiles, rows, cols, count, w_all, True, first)
        left_own = line_scatter_sum(left, "term", n_term)
        summed_own = left_own[:, :width_k, :]
        if first:
            doc_degree = left_own[:, width_k, :]
        quotient = (summed_own / doc_degree[:, None, :]).astype(jnp.bfloat16)
        q_all = lax.all_gather(quotient, "term", axis=0, tiled=True)
        right = tile_pass(local_tiles, rows, cols, count, q_all, False, first)
        right_own = scatter_sum(right, "doc", n_doc)
        if first:
            term_degree = right_own[:, width_k, :]
            root = jnp.sqrt(term_degree)
        raw = right_own[:, :width_k, :] / root[:, None, :]
        previous = root[:, None, :] * start_t.astype(jnp.float32) if first else basis
        gram_part = jnp.einsum("tki,tli->kl", raw, raw, precision=HIGH)
        along_part = jnp.einsum("tki,ti->k", raw, root, precision=HIGH)
        energy_part = jnp.sum(previous * raw, axis=(0, 2))
        volume_part = jnp.sum(term_degree)
        sums = [gram_part, along_part, energy_part, volume_part]
        if step == ITERS - 1:
            doc_ratio = summed_own / doc_degree[:, None, :]
            doc_part = jnp.einsum("tki,tij->kj", doc_ratio, doc_onehot, precision=HIGH)
            term_part = jnp.einsum("tki,tij->kj", raw / root[:, None, :], term_onehot, precision=HIGH)
            sums += [doc_part, term_part, jnp.sum(doc_onehot, axis=(0, 1)), jnp.sum(term_onehot, axis=(0, 1))]
        sums = packed_psum(n_doc, n_term, sums)
        gram_matrix, along, energy, volume = sums[:4]
        lower = jnp.linalg.cholesky(gram_matrix - jnp.outer(along, along) / volume)
        projected = raw - root[:, None, :] * (along / volume)[None, :, None]
        flat = projected.transpose(1, 0, 2).reshape(width_k, -1)
        solved = jax.scipy.linalg.solve_triangular(lower, flat, lower=True)
        basis = solved.reshape(width_k, term_tiles_own, edge).transpose(1, 0, 2)
        weights = (basis / root[:, None, :]).astype(jnp.bfloat16)

    doc_part, term_part, doc_count, term_count = sums[4:]
    scale = jnp.sqrt(volume)
    column_scale = scale * lax.rsqrt(energy)
    doc_embed = summed_own / doc_degree[:, None, :] * column_scale[None, :, None]
    term_embed = scale * basis / root[:, None, :]
    term_centered = term_part - jnp.outer(along / volume, term_count)
    term_sums = scale * jax.scipy.linalg.solve_triangular(lower, term_centered, lower=True)
    centers = (column_scale[:, None] * doc_part + term_sums) / (doc_count + term_count)[None, :]
    center_norm = jnp.sum(centers * centers, axis=0)

    def distances(embed):
        near = jnp.einsum("tki,kj->tij", embed, centers, precision=HIGH)
        norm = jnp.sum(embed * embed, axis=1)
        dist = (norm[:, :, None] - 2.0 * near + center_norm[None, None, :]) / width_k
        return dist.reshape(-1, CLUSTERS)

    return (distances(doc_embed)[None], distances(term_embed)[None])


def solution(mesh):
    placed = (
        P("doc", "term", None, None, None),
        P("doc", "term", None),
        P("doc", "term", None),
        P("doc", "term"),
        P("term", "doc", None),
        P("doc", "term"),
        P("term", "doc"),
    )
    return jax.shard_map(
        functools.partial(per_device, mesh.shape["doc"], mesh.shape["term"]),
        mesh=mesh,
        in_specs=placed,
        out_specs=(P("doc", "term", None), P("term", "doc", None)),
        check_vma=False,
    )
```

```python
import functools

import jax
import jax.numpy as jnp
from jax import lax
from jax.experimental import pallas as pl
from jax.experimental.pallas import tpu as pltpu
from jax.sharding import PartitionSpec as P

CLUSTERS = 64
ITERS = 2
CHUNK = 128
GROUP = 16
DEG_ROWS = 8

HIGH = lax.Precision.HIGHEST
NT_DIMS = (((1,), (1,)), ((), ()))


def tile_kernel(transpose_tile, with_degree, group, rows_ref, cols_ref, cnt_ref, tiles_ref, side_ref, out_ref):
    step = pl.program_id(0)
    chunk = tiles_ref.shape[0]
    width = side_ref.shape[1]

    @pl.when(step == 0)
    def _():
        out_ref[...] = jnp.zeros_like(out_ref)

    count = cnt_ref[0]
    base = step * chunk
    live = jnp.clip(count - base, 0, chunk)
    ones = jnp.ones((DEG_ROWS, tiles_ref.shape[2]), jnp.bfloat16)

    def product(lhs, tile):
        if transpose_tile:
            return lax.dot_general(lhs, tile, NT_DIMS, preferred_element_type=jnp.float32)
        return jnp.dot(lhs, tile, preferred_element_type=jnp.float32)

    def run(g, masked):
        results = []
        for u in range(group):
            j = g * group + u
            slot = base + j
            if transpose_tile:
                src, dst = cols_ref[slot], rows_ref[slot]
            else:
                src, dst = rows_ref[slot], cols_ref[slot]
            tile = tiles_ref[j]
            prod = product(side_ref[src], tile)
            deg = product(ones, tile) if with_degree else None
            if masked:
                keep = slot < count
                prod = jnp.where(keep, prod, 0.0)
                deg = jnp.where(keep, deg, 0.0) if with_degree else None
            results.append((dst, prod, deg))
        for dst, prod, deg in results:
            out_ref[dst, pl.ds(0, width), :] += prod
            if with_degree:
                out_ref[dst, pl.ds(width, DEG_ROWS), :] += deg

    def body(g, carry):
        run(g, False)
        return carry

    full = live // group
    lax.fori_loop(0, full, body, 0)

    @pl.when(full * group < live)
    def _():
        run(full, True)


def tile_pass(tiles, rows, cols, count, side, transpose_tile, with_degree):
    slots, edge, _ = tiles.shape
    n_tiles, width, _ = side.shape
    chunk = min(CHUNK, slots)
    steps = slots // chunk
    out_rows = width + (DEG_ROWS if with_degree else 0)
    kernel = functools.partial(tile_kernel, transpose_tile, with_degree, GROUP)

    def tile_map(i, rows_ref, cols_ref, cnt_ref):
        return (jnp.minimum(i, jnp.maximum(cnt_ref[0] - 1, 0) // chunk), 0, 0)

    def whole_map(i, rows_ref, cols_ref, cnt_ref):
        return (0, 0, 0)

    flops = 2 * slots * edge * edge * out_rows
    cost = pl.CostEstimate(
        flops=flops,
        transcendentals=0,
        bytes_accessed=tiles.size * 2 + side.size * 2 + n_tiles * out_rows * edge * 4,
    )
    return pl.pallas_call(
        kernel,
        out_shape=jax.ShapeDtypeStruct((n_tiles, out_rows, edge), jnp.float32),
        grid_spec=pltpu.PrefetchScalarGridSpec(
            num_scalar_prefetch=3,
            grid=(steps,),
            in_specs=[
                pl.BlockSpec((chunk, edge, edge), tile_map),
                pl.BlockSpec((n_tiles, width, edge), whole_map),
            ],
            out_specs=pl.BlockSpec((n_tiles, out_rows, edge), whole_map),
        ),
        compiler_params=pltpu.CompilerParams(dimension_semantics=("arbitrary",)),
        cost_estimate=cost,
    )(rows, cols, count, tiles, side)


def scatter_sum(x, axis_name, parts):
    pieces = x.reshape((parts, x.shape[0] // parts) + x.shape[1:])
    return jnp.sum(lax.all_to_all(pieces, axis_name, 0, 0, tiled=False), axis=0)


def exchange_sum(flat, axis_name, parts):
    copies = jnp.broadcast_to(flat, (parts,) + flat.shape)
    return jnp.sum(lax.all_to_all(copies, axis_name, 0, 0, tiled=False), axis=0)


def exchange_gather(x, axis_name, parts):
    copies = jnp.broadcast_to(x, (parts,) + x.shape)
    got = lax.all_to_all(copies, axis_name, 0, 0, tiled=False)
    return got.reshape((parts * x.shape[0],) + x.shape[1:])


def packed_psum(n_doc, n_term, values):
    flat = jnp.concatenate([jnp.reshape(v, (-1,)) for v in values])
    flat = exchange_sum(exchange_sum(flat, "term", n_term), "doc", n_doc)
    out, start = [], 0
    for v in values:
        size = int(jnp.size(v))
        out.append(flat[start : start + size].reshape(jnp.shape(v)))
        start += size
    return out


def per_device(n_doc, n_term, tiles, tile_rows, tile_cols, tile_count, start_block, doc_cluster, term_cluster):
    local_tiles = tiles[0, 0]
    rows = tile_rows[0, 0]
    cols = tile_cols[0, 0]
    count = tile_count[0, 0].reshape(1)
    edge = local_tiles.shape[1]
    start_rows = start_block[0]
    width_k = start_rows.shape[1]
    term_tiles_own = start_rows.shape[0] // edge
    start_t = start_rows.reshape(term_tiles_own, edge, width_k).transpose(0, 2, 1)
    doc_labels = doc_cluster[0].reshape(-1, edge)
    term_labels = term_cluster[0].reshape(-1, edge)
    clusters = jnp.arange(CLUSTERS, dtype=jnp.int32)
    doc_onehot = (doc_labels[:, :, None] == clusters).astype(jnp.float32)
    term_onehot = (term_labels[:, :, None] == clusters).astype(jnp.float32)

    weights = start_t
    basis = None
    doc_degree = None
    term_degree = None
    root = None
    summed_own = None
    energy = None
    volume = None
    for step in range(ITERS):
        first = step == 0
        w_all = exchange_gather(weights, "doc", n_doc)
        left = tile_pass(local_tiles, rows, cols, count, w_all, True, first)
        left_own = lax.psum_scatter(left, "term", scatter_dimension=0, tiled=True)
        summed_own = left_own[:, :width_k, :]
        if first:
            doc_degree = left_own[:, width_k, :]
        quotient = (summed_own / doc_degree[:, None, :]).astype(jnp.bfloat16)
        q_all = lax.all_gather(quotient, "term", axis=0, tiled=True)
        right = tile_pass(local_tiles, rows, cols, count, q_all, False, first)
        right_own = scatter_sum(right, "doc", n_doc)
        if first:
            term_degree = right_own[:, width_k, :]
            root = jnp.sqrt(term_degree)
        raw = right_own[:, :width_k, :] / root[:, None, :]
        previous = root[:, None, :] * start_t.astype(jnp.float32) if first else basis
        gram_part = jnp.einsum("tki,tli->kl", raw, raw, precision=HIGH)
        along_part = jnp.einsum("tki,ti->k", raw, root, precision=HIGH)
        energy_part = jnp.sum(previous * raw, axis=(0, 2))
        volume_part = jnp.sum(term_degree)
        sums = [gram_part, along_part, energy_part, volume_part]
        if step == ITERS - 1:
            doc_ratio = summed_own / doc_degree[:, None, :]
            doc_part = jnp.einsum("tki,tij->kj", doc_ratio, doc_onehot, precision=HIGH)
            term_part = jnp.einsum("tki,tij->kj", raw / root[:, None, :], term_onehot, precision=HIGH)
            sums += [doc_part, term_part, jnp.sum(doc_onehot, axis=(0, 1)), jnp.sum(term_onehot, axis=(0, 1))]
        sums = packed_psum(n_doc, n_term, sums)
        gram_matrix, along, energy, volume = sums[:4]
        lower = jnp.linalg.cholesky(gram_matrix - jnp.outer(along, along) / volume)
        projected = raw - root[:, None, :] * (along / volume)[None, :, None]
        flat = projected.transpose(1, 0, 2).reshape(width_k, -1)
        solved = jax.scipy.linalg.solve_triangular(lower, flat, lower=True)
        basis = solved.reshape(width_k, term_tiles_own, edge).transpose(1, 0, 2)
        weights = (basis / root[:, None, :]).astype(jnp.bfloat16)

    doc_part, term_part, doc_count, term_count = sums[4:]
    scale = jnp.sqrt(volume)
    column_scale = scale * lax.rsqrt(energy)
    doc_embed = summed_own / doc_degree[:, None, :] * column_scale[None, :, None]
    term_embed = scale * basis / root[:, None, :]
    term_centered = term_part - jnp.outer(along / volume, term_count)
    term_sums = scale * jax.scipy.linalg.solve_triangular(lower, term_centered, lower=True)
    centers = (column_scale[:, None] * doc_part + term_sums) / (doc_count + term_count)[None, :]
    center_norm = jnp.sum(centers * centers, axis=0)

    def distances(embed):
        near = jnp.einsum("tki,kj->tij", embed, centers, precision=HIGH)
        norm = jnp.sum(embed * embed, axis=1)
        dist = (norm[:, :, None] - 2.0 * near + center_norm[None, None, :]) / width_k
        return dist.reshape(-1, CLUSTERS)

    return (distances(doc_embed)[None], distances(term_embed)[None])


def solution(mesh):
    placed = (
        P("doc", "term", None, None, None),
        P("doc", "term", None),
        P("doc", "term", None),
        P("doc", "term"),
        P("term", "doc", None),
        P("doc", "term"),
        P("term", "doc"),
    )
    return jax.shard_map(
        functools.partial(per_device, mesh.shape["doc"], mesh.shape["term"]),
        mesh=mesh,
        in_specs=placed,
        out_specs=(P("doc", "term", None), P("term", "doc", None)),
        check_vma=False,
    )
```

```python
import functools

import jax
import jax.numpy as jnp
from jax import lax
from jax.experimental import pallas as pl
from jax.experimental.pallas import tpu as pltpu
from jax.sharding import PartitionSpec as P

CLUSTERS = 64
ITERS = 2
CHUNK = 128
GROUP = 16
DEG_ROWS = 8

HIGH = lax.Precision.HIGHEST
NT_DIMS = (((1,), (1,)), ((), ()))


def tile_kernel(transpose_tile, with_degree, group, rows_ref, cols_ref, cnt_ref, tiles_ref, side_ref, out_ref):
    step = pl.program_id(0)
    chunk = tiles_ref.shape[0]
    width = side_ref.shape[1]

    @pl.when(step == 0)
    def _():
        out_ref[...] = jnp.zeros_like(out_ref)

    count = cnt_ref[0]
    base = step * chunk
    live = jnp.clip(count - base, 0, chunk)
    ones = jnp.ones((DEG_ROWS, tiles_ref.shape[2]), jnp.bfloat16)

    def product(lhs, tile):
        if transpose_tile:
            return lax.dot_general(lhs, tile, NT_DIMS, preferred_element_type=jnp.float32)
        return jnp.dot(lhs, tile, preferred_element_type=jnp.float32)

    def run(g, masked):
        results = []
        for u in range(group):
            j = g * group + u
            slot = base + j
            if transpose_tile:
                src, dst = cols_ref[slot], rows_ref[slot]
            else:
                src, dst = rows_ref[slot], cols_ref[slot]
            tile = tiles_ref[j]
            prod = product(side_ref[src], tile)
            deg = product(ones, tile) if with_degree else None
            if masked:
                keep = slot < count
                prod = jnp.where(keep, prod, 0.0)
                deg = jnp.where(keep, deg, 0.0) if with_degree else None
            results.append((dst, prod, deg))
        for dst, prod, deg in results:
            out_ref[dst, pl.ds(0, width), :] += prod
            if with_degree:
                out_ref[dst, pl.ds(width, DEG_ROWS), :] += deg

    def body(g, carry):
        run(g, False)
        return carry

    full = live // group
    lax.fori_loop(0, full, body, 0)

    @pl.when(full * group < live)
    def _():
        run(full, True)


def tile_pass(tiles, rows, cols, count, side, transpose_tile, with_degree):
    slots, edge, _ = tiles.shape
    n_tiles, width, _ = side.shape
    chunk = min(CHUNK, slots)
    steps = slots // chunk
    out_rows = width + (DEG_ROWS if with_degree else 0)
    kernel = functools.partial(tile_kernel, transpose_tile, with_degree, GROUP)

    def tile_map(i, rows_ref, cols_ref, cnt_ref):
        return (jnp.minimum(i, jnp.maximum(cnt_ref[0] - 1, 0) // chunk), 0, 0)

    def whole_map(i, rows_ref, cols_ref, cnt_ref):
        return (0, 0, 0)

    flops = 2 * slots * edge * edge * out_rows
    cost = pl.CostEstimate(
        flops=flops,
        transcendentals=0,
        bytes_accessed=tiles.size * 2 + side.size * 2 + n_tiles * out_rows * edge * 4,
    )
    return pl.pallas_call(
        kernel,
        out_shape=jax.ShapeDtypeStruct((n_tiles, out_rows, edge), jnp.float32),
        grid_spec=pltpu.PrefetchScalarGridSpec(
            num_scalar_prefetch=3,
            grid=(steps,),
            in_specs=[
                pl.BlockSpec((chunk, edge, edge), tile_map),
                pl.BlockSpec((n_tiles, width, edge), whole_map),
            ],
            out_specs=pl.BlockSpec((n_tiles, out_rows, edge), whole_map),
        ),
        compiler_params=pltpu.CompilerParams(dimension_semantics=("arbitrary",)),
        cost_estimate=cost,
    )(rows, cols, count, tiles, side)


def scatter_sum(x, axis_name, parts):
    pieces = x.reshape((parts, x.shape[0] // parts) + x.shape[1:])
    return jnp.sum(lax.all_to_all(pieces, axis_name, 0, 0, tiled=False), axis=0)


def exchange_sum(flat, axis_name, parts):
    copies = jnp.broadcast_to(flat, (parts,) + flat.shape)
    return jnp.sum(lax.all_to_all(copies, axis_name, 0, 0, tiled=False), axis=0)


def exchange_gather(x, axis_name, parts):
    copies = jnp.broadcast_to(x, (parts,) + x.shape)
    got = lax.all_to_all(copies, axis_name, 0, 0, tiled=False)
    return got.reshape((parts * x.shape[0],) + x.shape[1:])


def packed_psum(n_doc, n_term, values):
    flat = jnp.concatenate([jnp.reshape(v, (-1,)) for v in values])
    flat = exchange_sum(exchange_sum(flat, "term", n_term), "doc", n_doc)
    out, start = [], 0
    for v in values:
        size = int(jnp.size(v))
        out.append(flat[start : start + size].reshape(jnp.shape(v)))
        start += size
    return out


def per_device(n_doc, n_term, tiles, tile_rows, tile_cols, tile_count, start_block, doc_cluster, term_cluster):
    local_tiles = tiles[0, 0]
    rows = tile_rows[0, 0]
    cols = tile_cols[0, 0]
    count = tile_count[0, 0].reshape(1)
    edge = local_tiles.shape[1]
    start_rows = start_block[0]
    width_k = start_rows.shape[1]
    term_tiles_own = start_rows.shape[0] // edge
    start_t = start_rows.reshape(term_tiles_own, edge, width_k).transpose(0, 2, 1)
    doc_labels = doc_cluster[0].reshape(-1, edge)
    term_labels = term_cluster[0].reshape(-1, edge)
    clusters = jnp.arange(CLUSTERS, dtype=jnp.int32)
    doc_onehot = (doc_labels[:, :, None] == clusters).astype(jnp.float32)
    term_onehot = (term_labels[:, :, None] == clusters).astype(jnp.float32)

    weights = start_t
    basis = None
    doc_degree = None
    term_degree = None
    root = None
    summed_own = None
    energy = None
    volume = None
    for step in range(ITERS):
        first = step == 0
        w_all = exchange_gather(weights, "doc", n_doc)
        left = tile_pass(local_tiles, rows, cols, count, w_all, True, first)
        left_own = lax.psum_scatter(left, "term", scatter_dimension=0, tiled=True)
        summed_own = left_own[:, :width_k, :]
        if first:
            doc_degree = left_own[:, width_k, :]
        quotient = (summed_own / doc_degree[:, None, :]).astype(jnp.bfloat16)
        q_all = exchange_gather(quotient, "term", n_term)
        right = tile_pass(local_tiles, rows, cols, count, q_all, False, first)
        right_own = scatter_sum(right, "doc", n_doc)
        if first:
            term_degree = right_own[:, width_k, :]
            root = jnp.sqrt(term_degree)
        raw = right_own[:, :width_k, :] / root[:, None, :]
        previous = root[:, None, :] * start_t.astype(jnp.float32) if first else basis
        gram_part = jnp.einsum("tki,tli->kl", raw, raw, precision=HIGH)
        along_part = jnp.einsum("tki,ti->k", raw, root, precision=HIGH)
        energy_part = jnp.sum(previous * raw, axis=(0, 2))
        volume_part = jnp.sum(term_degree)
        sums = [gram_part, along_part, energy_part, volume_part]
        if step == ITERS - 1:
            doc_ratio = summed_own / doc_degree[:, None, :]
            doc_part = jnp.einsum("tki,tij->kj", doc_ratio, doc_onehot, precision=HIGH)
            term_part = jnp.einsum("tki,tij->kj", raw / root[:, None, :], term_onehot, precision=HIGH)
            sums += [doc_part, term_part, jnp.sum(doc_onehot, axis=(0, 1)), jnp.sum(term_onehot, axis=(0, 1))]
        sums = packed_psum(n_doc, n_term, sums)
        gram_matrix, along, energy, volume = sums[:4]
        lower = jnp.linalg.cholesky(gram_matrix - jnp.outer(along, along) / volume)
        projected = raw - root[:, None, :] * (along / volume)[None, :, None]
        flat = projected.transpose(1, 0, 2).reshape(width_k, -1)
        solved = jax.scipy.linalg.solve_triangular(lower, flat, lower=True)
        basis = solved.reshape(width_k, term_tiles_own, edge).transpose(1, 0, 2)
        weights = (basis / root[:, None, :]).astype(jnp.bfloat16)

    doc_part, term_part, doc_count, term_count = sums[4:]
    scale = jnp.sqrt(volume)
    column_scale = scale * lax.rsqrt(energy)
    doc_embed = summed_own / doc_degree[:, None, :] * column_scale[None, :, None]
    term_embed = scale * basis / root[:, None, :]
    term_centered = term_part - jnp.outer(along / volume, term_count)
    term_sums = scale * jax.scipy.linalg.solve_triangular(lower, term_centered, lower=True)
    centers = (column_scale[:, None] * doc_part + term_sums) / (doc_count + term_count)[None, :]
    center_norm = jnp.sum(centers * centers, axis=0)

    def distances(embed):
        near = jnp.einsum("tki,kj->tij", embed, centers, precision=HIGH)
        norm = jnp.sum(embed * embed, axis=1)
        dist = (norm[:, :, None] - 2.0 * near + center_norm[None, None, :]) / width_k
        return dist.reshape(-1, CLUSTERS)

    return (distances(doc_embed)[None], distances(term_embed)[None])


def solution(mesh):
    placed = (
        P("doc", "term", None, None, None),
        P("doc", "term", None),
        P("doc", "term", None),
        P("doc", "term"),
        P("term", "doc", None),
        P("doc", "term"),
        P("term", "doc"),
    )
    return jax.shard_map(
        functools.partial(per_device, mesh.shape["doc"], mesh.shape["term"]),
        mesh=mesh,
        in_specs=placed,
        out_specs=(P("doc", "term", None), P("term", "doc", None)),
        check_vma=False,
    )
```

```python
import functools

import jax
import jax.numpy as jnp
from jax import lax
from jax.experimental import pallas as pl
from jax.experimental.pallas import tpu as pltpu
from jax.sharding import PartitionSpec as P

CLUSTERS = 64
ITERS = 2
CHUNK = 128
GROUP = 16
DEG_ROWS = 8

HIGH = lax.Precision.HIGHEST
NT_DIMS = (((1,), (1,)), ((), ()))


def tile_kernel(transpose_tile, with_degree, group, rows_ref, cols_ref, cnt_ref, tiles_ref, side_ref, out_ref):
    step = pl.program_id(0)
    chunk = tiles_ref.shape[0]
    width = side_ref.shape[1]

    @pl.when(step == 0)
    def _():
        out_ref[...] = jnp.zeros_like(out_ref)

    count = cnt_ref[0]
    base = step * chunk
    live = jnp.clip(count - base, 0, chunk)

    def product(lhs, tile):
        if transpose_tile:
            return lax.dot_general(lhs, tile, NT_DIMS, preferred_element_type=jnp.float32)
        return jnp.dot(lhs, tile, preferred_element_type=jnp.float32)

    def run(g, masked):
        results = []
        for u in range(group):
            j = g * group + u
            slot = base + j
            if transpose_tile:
                src, dst = cols_ref[slot], rows_ref[slot]
            else:
                src, dst = rows_ref[slot], cols_ref[slot]
            tile = tiles_ref[j]
            prod = product(side_ref[src], tile)
            if masked:
                prod = jnp.where(slot < count, prod, 0.0)
            results.append((dst, prod))
        for dst, prod in results:
            out_ref[dst] += prod

    def body(g, carry):
        run(g, False)
        return carry

    full = live // group
    lax.fori_loop(0, full, body, 0)

    @pl.when(full * group < live)
    def _():
        run(full, True)


def tile_pass(tiles, rows, cols, count, side, transpose_tile, with_degree):
    slots, edge, _ = tiles.shape
    n_tiles, width, _ = side.shape
    chunk = min(CHUNK, slots)
    steps = slots // chunk
    if with_degree:
        side = jnp.concatenate([side, jnp.ones((n_tiles, DEG_ROWS, edge), side.dtype)], axis=1)
    out_rows = side.shape[1]
    kernel = functools.partial(tile_kernel, transpose_tile, with_degree, GROUP)

    def tile_map(i, rows_ref, cols_ref, cnt_ref):
        return (jnp.minimum(i, jnp.maximum(cnt_ref[0] - 1, 0) // chunk), 0, 0)

    def whole_map(i, rows_ref, cols_ref, cnt_ref):
        return (0, 0, 0)

    flops = 2 * slots * edge * edge * out_rows
    cost = pl.CostEstimate(
        flops=flops,
        transcendentals=0,
        bytes_accessed=tiles.size * 2 + side.size * 2 + n_tiles * out_rows * edge * 4,
    )
    return pl.pallas_call(
        kernel,
        out_shape=jax.ShapeDtypeStruct((n_tiles, out_rows, edge), jnp.float32),
        grid_spec=pltpu.PrefetchScalarGridSpec(
            num_scalar_prefetch=3,
            grid=(steps,),
            in_specs=[
                pl.BlockSpec((chunk, edge, edge), tile_map),
                pl.BlockSpec((n_tiles, out_rows, edge), whole_map),
            ],
            out_specs=pl.BlockSpec((n_tiles, out_rows, edge), whole_map),
        ),
        compiler_params=pltpu.CompilerParams(dimension_semantics=("arbitrary",)),
        cost_estimate=cost,
    )(rows, cols, count, tiles, side)


def scatter_sum(x, axis_name, parts):
    pieces = x.reshape((parts, x.shape[0] // parts) + x.shape[1:])
    return jnp.sum(lax.all_to_all(pieces, axis_name, 0, 0, tiled=False), axis=0)


def exchange_sum(flat, axis_name, parts):
    copies = jnp.broadcast_to(flat, (parts,) + flat.shape)
    return jnp.sum(lax.all_to_all(copies, axis_name, 0, 0, tiled=False), axis=0)


def exchange_gather(x, axis_name, parts):
    copies = jnp.broadcast_to(x, (parts,) + x.shape)
    got = lax.all_to_all(copies, axis_name, 0, 0, tiled=False)
    return got.reshape((parts * x.shape[0],) + x.shape[1:])


def packed_psum(n_doc, n_term, values):
    flat = jnp.concatenate([jnp.reshape(v, (-1,)) for v in values])
    flat = exchange_sum(exchange_sum(flat, "term", n_term), "doc", n_doc)
    out, start = [], 0
    for v in values:
        size = int(jnp.size(v))
        out.append(flat[start : start + size].reshape(jnp.shape(v)))
        start += size
    return out


def per_device(n_doc, n_term, tiles, tile_rows, tile_cols, tile_count, start_block, doc_cluster, term_cluster):
    local_tiles = tiles[0, 0]
    rows = tile_rows[0, 0]
    cols = tile_cols[0, 0]
    count = tile_count[0, 0].reshape(1)
    edge = local_tiles.shape[1]
    start_rows = start_block[0]
    width_k = start_rows.shape[1]
    term_tiles_own = start_rows.shape[0] // edge
    start_t = start_rows.reshape(term_tiles_own, edge, width_k).transpose(0, 2, 1)
    doc_labels = doc_cluster[0].reshape(-1, edge)
    term_labels = term_cluster[0].reshape(-1, edge)
    clusters = jnp.arange(CLUSTERS, dtype=jnp.int32)
    doc_onehot = (doc_labels[:, :, None] == clusters).astype(jnp.float32)
    term_onehot = (term_labels[:, :, None] == clusters).astype(jnp.float32)

    weights = start_t
    basis = None
    doc_degree = None
    term_degree = None
    root = None
    summed_own = None
    energy = None
    volume = None
    for step in range(ITERS):
        first = step == 0
        w_all = exchange_gather(weights, "doc", n_doc)
        left = tile_pass(local_tiles, rows, cols, count, w_all, True, first)
        left_own = lax.psum_scatter(left, "term", scatter_dimension=0, tiled=True)
        summed_own = left_own[:, :width_k, :]
        if first:
            doc_degree = left_own[:, width_k, :]
        quotient = (summed_own / doc_degree[:, None, :]).astype(jnp.bfloat16)
        q_all = lax.all_gather(quotient, "term", axis=0, tiled=True)
        right = tile_pass(local_tiles, rows, cols, count, q_all, False, first)
        right_own = scatter_sum(right, "doc", n_doc)
        if first:
            term_degree = right_own[:, width_k, :]
            root = jnp.sqrt(term_degree)
        raw = right_own[:, :width_k, :] / root[:, None, :]
        previous = root[:, None, :] * start_t.astype(jnp.float32) if first else basis
        gram_part = jnp.einsum("tki,tli->kl", raw, raw, precision=HIGH)
        along_part = jnp.einsum("tki,ti->k", raw, root, precision=HIGH)
        energy_part = jnp.sum(previous * raw, axis=(0, 2))
        volume_part = jnp.sum(term_degree)
        sums = [gram_part, along_part, energy_part, volume_part]
        if step == ITERS - 1:
            doc_ratio = summed_own / doc_degree[:, None, :]
            doc_part = jnp.einsum("tki,tij->kj", doc_ratio, doc_onehot, precision=HIGH)
            term_part = jnp.einsum("tki,tij->kj", raw / root[:, None, :], term_onehot, precision=HIGH)
            sums += [doc_part, term_part, jnp.sum(doc_onehot, axis=(0, 1)), jnp.sum(term_onehot, axis=(0, 1))]
        sums = packed_psum(n_doc, n_term, sums)
        gram_matrix, along, energy, volume = sums[:4]
        lower = jnp.linalg.cholesky(gram_matrix - jnp.outer(along, along) / volume)
        projected = raw - root[:, None, :] * (along / volume)[None, :, None]
        flat = projected.transpose(1, 0, 2).reshape(width_k, -1)
        solved = jax.scipy.linalg.solve_triangular(lower, flat, lower=True)
        basis = solved.reshape(width_k, term_tiles_own, edge).transpose(1, 0, 2)
        weights = (basis / root[:, None, :]).astype(jnp.bfloat16)

    doc_part, term_part, doc_count, term_count = sums[4:]
    scale = jnp.sqrt(volume)
    column_scale = scale * lax.rsqrt(energy)
    doc_embed = summed_own / doc_degree[:, None, :] * column_scale[None, :, None]
    term_embed = scale * basis / root[:, None, :]
    term_centered = term_part - jnp.outer(along / volume, term_count)
    term_sums = scale * jax.scipy.linalg.solve_triangular(lower, term_centered, lower=True)
    centers = (column_scale[:, None] * doc_part + term_sums) / (doc_count + term_count)[None, :]
    center_norm = jnp.sum(centers * centers, axis=0)

    def distances(embed):
        near = jnp.einsum("tki,kj->tij", embed, centers, precision=HIGH)
        norm = jnp.sum(embed * embed, axis=1)
        dist = (norm[:, :, None] - 2.0 * near + center_norm[None, None, :]) / width_k
        return dist.reshape(-1, CLUSTERS)

    return (distances(doc_embed)[None], distances(term_embed)[None])


def solution(mesh):
    placed = (
        P("doc", "term", None, None, None),
        P("doc", "term", None),
        P("doc", "term", None),
        P("doc", "term"),
        P("term", "doc", None),
        P("doc", "term"),
        P("term", "doc"),
    )
    return jax.shard_map(
        functools.partial(per_device, mesh.shape["doc"], mesh.shape["term"]),
        mesh=mesh,
        in_specs=placed,
        out_specs=(P("doc", "term", None), P("term", "doc", None)),
        check_vma=False,
    )
```

```python
import functools

import jax
import jax.numpy as jnp
from jax import lax
from jax.experimental import pallas as pl
from jax.experimental.pallas import tpu as pltpu
from jax.sharding import PartitionSpec as P

CLUSTERS = 64
ITERS = 2
CHUNK = 128
GROUP = 16
DEG_ROWS = 8

HIGH = lax.Precision.HIGHEST
NT_DIMS = (((1,), (1,)), ((), ()))


def tile_kernel(transpose_tile, with_degree, group, split, rows_ref, cols_ref, cnt_ref, tiles_ref, side_ref, out_ref, rest_ref):
    step = pl.program_id(0)
    chunk = tiles_ref.shape[0]
    width = side_ref.shape[1]

    @pl.when(step == 0)
    def _():
        out_ref[...] = jnp.zeros_like(out_ref)
        rest_ref[...] = jnp.zeros_like(rest_ref)

    count = cnt_ref[0]
    base = step * chunk
    live = jnp.clip(count - base, 0, chunk)

    def product(lhs, tile):
        if transpose_tile:
            return lax.dot_general(lhs, tile, NT_DIMS, preferred_element_type=jnp.float32)
        return jnp.dot(lhs, tile, preferred_element_type=jnp.float32)

    def run(g, masked):
        results = []
        for u in range(group):
            j = g * group + u
            slot = base + j
            if transpose_tile:
                src, dst = cols_ref[slot], rows_ref[slot]
            else:
                src, dst = rows_ref[slot], cols_ref[slot]
            tile = tiles_ref[j]
            prod = product(side_ref[src], tile)
            if masked:
                prod = jnp.where(slot < count, prod, 0.0)
            results.append((dst, prod))
        for dst, prod in results:
            out_ref[dst] += prod[:split]
            rest_ref[dst] += prod[split:]

    def body(g, carry):
        run(g, False)
        return carry

    full = live // group
    lax.fori_loop(0, full, body, 0)

    @pl.when(full * group < live)
    def _():
        run(full, True)


def tile_pass(tiles, rows, cols, count, side, transpose_tile, with_degree, split):
    slots, edge, _ = tiles.shape
    n_tiles, width, _ = side.shape
    chunk = min(CHUNK, slots)
    steps = slots // chunk
    if with_degree:
        side = jnp.concatenate([side, jnp.ones((n_tiles, DEG_ROWS, edge), side.dtype)], axis=1)
    out_rows = side.shape[1]
    kernel = functools.partial(tile_kernel, transpose_tile, with_degree, GROUP, split)

    def tile_map(i, rows_ref, cols_ref, cnt_ref):
        return (jnp.minimum(i, jnp.maximum(cnt_ref[0] - 1, 0) // chunk), 0, 0)

    def whole_map(i, rows_ref, cols_ref, cnt_ref):
        return (0, 0, 0)

    flops = 2 * slots * edge * edge * out_rows
    cost = pl.CostEstimate(
        flops=flops,
        transcendentals=0,
        bytes_accessed=tiles.size * 2 + side.size * 2 + n_tiles * out_rows * edge * 4,
    )
    return pl.pallas_call(
        kernel,
        out_shape=(
            jax.ShapeDtypeStruct((n_tiles, split, edge), jnp.float32),
            jax.ShapeDtypeStruct((n_tiles, out_rows - split, edge), jnp.float32),
        ),
        grid_spec=pltpu.PrefetchScalarGridSpec(
            num_scalar_prefetch=3,
            grid=(steps,),
            in_specs=[
                pl.BlockSpec((chunk, edge, edge), tile_map),
                pl.BlockSpec((n_tiles, out_rows, edge), whole_map),
            ],
            out_specs=(
                pl.BlockSpec((n_tiles, split, edge), whole_map),
                pl.BlockSpec((n_tiles, out_rows - split, edge), whole_map),
            ),
        ),
        compiler_params=pltpu.CompilerParams(dimension_semantics=("arbitrary",)),
        cost_estimate=cost,
    )(rows, cols, count, tiles, side)


def scatter_sum(x, axis_name, parts):
    pieces = x.reshape((parts, x.shape[0] // parts) + x.shape[1:])
    return jnp.sum(lax.all_to_all(pieces, axis_name, 0, 0, tiled=False), axis=0)


def exchange_sum(flat, axis_name, parts):
    copies = jnp.broadcast_to(flat, (parts,) + flat.shape)
    return jnp.sum(lax.all_to_all(copies, axis_name, 0, 0, tiled=False), axis=0)


def exchange_gather(x, axis_name, parts):
    copies = jnp.broadcast_to(x, (parts,) + x.shape)
    got = lax.all_to_all(copies, axis_name, 0, 0, tiled=False)
    return got.reshape((parts * x.shape[0],) + x.shape[1:])


def split_scatter_sum(offloaded, exchanged, axis_name, parts):
    first = lax.psum_scatter(offloaded, axis_name, scatter_dimension=0, tiled=True)
    second = scatter_sum(exchanged, axis_name, parts)
    return jnp.concatenate([first, second], axis=1)


def split_gather(x, axis_name, parts, offloaded_rows):
    first = lax.all_gather(x[:, :offloaded_rows], axis_name, axis=0, tiled=True)
    second = exchange_gather(x[:, offloaded_rows:], axis_name, parts)
    return jnp.concatenate([first, second], axis=1)


def packed_psum(n_doc, n_term, values):
    flat = jnp.concatenate([jnp.reshape(v, (-1,)) for v in values])
    flat = exchange_sum(exchange_sum(flat, "term", n_term), "doc", n_doc)
    out, start = [], 0
    for v in values:
        size = int(jnp.size(v))
        out.append(flat[start : start + size].reshape(jnp.shape(v)))
        start += size
    return out


def per_device(n_doc, n_term, tiles, tile_rows, tile_cols, tile_count, start_block, doc_cluster, term_cluster):
    local_tiles = tiles[0, 0]
    rows = tile_rows[0, 0]
    cols = tile_cols[0, 0]
    count = tile_count[0, 0].reshape(1)
    edge = local_tiles.shape[1]
    start_rows = start_block[0]
    width_k = start_rows.shape[1]
    term_tiles_own = start_rows.shape[0] // edge
    start_t = start_rows.reshape(term_tiles_own, edge, width_k).transpose(0, 2, 1)
    doc_labels = doc_cluster[0].reshape(-1, edge)
    term_labels = term_cluster[0].reshape(-1, edge)
    clusters = jnp.arange(CLUSTERS, dtype=jnp.int32)
    doc_onehot = (doc_labels[:, :, None] == clusters).astype(jnp.float32)
    term_onehot = (term_labels[:, :, None] == clusters).astype(jnp.float32)

    weights = start_t
    basis = None
    doc_degree = None
    term_degree = None
    root = None
    summed_own = None
    energy = None
    volume = None
    for step in range(ITERS):
        first = step == 0
        w_all = split_gather(weights, "doc", n_doc, 24)
        left = tile_pass(local_tiles, rows, cols, count, w_all, True, first, 40)
        left_own = split_scatter_sum(*left, "term", n_term)
        summed_own = left_own[:, :width_k, :]
        if first:
            doc_degree = left_own[:, width_k, :]
        quotient = (summed_own / doc_degree[:, None, :]).astype(jnp.bfloat16)
        q_all = split_gather(quotient, "term", n_term, 32)
        right = tile_pass(local_tiles, rows, cols, count, q_all, False, first, 24)
        right_own = split_scatter_sum(*right, "doc", n_doc)
        if first:
            term_degree = right_own[:, width_k, :]
            root = jnp.sqrt(term_degree)
        raw = right_own[:, :width_k, :] / root[:, None, :]
        previous = root[:, None, :] * start_t.astype(jnp.float32) if first else basis
        gram_part = jnp.einsum("tki,tli->kl", raw, raw, precision=HIGH)
        along_part = jnp.einsum("tki,ti->k", raw, root, precision=HIGH)
        energy_part = jnp.sum(previous * raw, axis=(0, 2))
        volume_part = jnp.sum(term_degree)
        sums = [gram_part, along_part, energy_part, volume_part]
        if step == ITERS - 1:
            doc_ratio = summed_own / doc_degree[:, None, :]
            doc_part = jnp.einsum("tki,tij->kj", doc_ratio, doc_onehot, precision=HIGH)
            term_part = jnp.einsum("tki,tij->kj", raw / root[:, None, :], term_onehot, precision=HIGH)
            sums += [doc_part, term_part, jnp.sum(doc_onehot, axis=(0, 1)), jnp.sum(term_onehot, axis=(0, 1))]
        sums = packed_psum(n_doc, n_term, sums)
        gram_matrix, along, energy, volume = sums[:4]
        lower = jnp.linalg.cholesky(gram_matrix - jnp.outer(along, along) / volume)
        projected = raw - root[:, None, :] * (along / volume)[None, :, None]
        flat = projected.transpose(1, 0, 2).reshape(width_k, -1)
        solved = jax.scipy.linalg.solve_triangular(lower, flat, lower=True)
        basis = solved.reshape(width_k, term_tiles_own, edge).transpose(1, 0, 2)
        weights = (basis / root[:, None, :]).astype(jnp.bfloat16)

    doc_part, term_part, doc_count, term_count = sums[4:]
    scale = jnp.sqrt(volume)
    column_scale = scale * lax.rsqrt(energy)
    doc_embed = summed_own / doc_degree[:, None, :] * column_scale[None, :, None]
    term_embed = scale * basis / root[:, None, :]
    term_centered = term_part - jnp.outer(along / volume, term_count)
    term_sums = scale * jax.scipy.linalg.solve_triangular(lower, term_centered, lower=True)
    centers = (column_scale[:, None] * doc_part + term_sums) / (doc_count + term_count)[None, :]
    center_norm = jnp.sum(centers * centers, axis=0)

    def distances(embed):
        near = jnp.einsum("tki,kj->tij", embed, centers, precision=HIGH)
        norm = jnp.sum(embed * embed, axis=1)
        dist = (norm[:, :, None] - 2.0 * near + center_norm[None, None, :]) / width_k
        return dist.reshape(-1, CLUSTERS)

    return (distances(doc_embed)[None], distances(term_embed)[None])


def solution(mesh):
    placed = (
        P("doc", "term", None, None, None),
        P("doc", "term", None),
        P("doc", "term", None),
        P("doc", "term"),
        P("term", "doc", None),
        P("doc", "term"),
        P("term", "doc"),
    )
    return jax.shard_map(
        functools.partial(per_device, mesh.shape["doc"], mesh.shape["term"]),
        mesh=mesh,
        in_specs=placed,
        out_specs=(P("doc", "term", None), P("term", "doc", None)),
        check_vma=False,
    )
```

```python
import functools

import jax
import jax.numpy as jnp
from jax import lax
from jax.experimental import pallas as pl
from jax.experimental.pallas import tpu as pltpu
from jax.sharding import PartitionSpec as P

CLUSTERS = 64
ITERS = 2
CHUNK = 128
GROUP = 16
DEG_ROWS = 8

HIGH = lax.Precision.HIGHEST
NT_DIMS = (((1,), (1,)), ((), ()))


def tile_kernel(transpose_tile, with_degree, group, rows_ref, cols_ref, cnt_ref, tiles_ref, side_ref, out_ref):
    step = pl.program_id(0)
    chunk = tiles_ref.shape[0]
    width = side_ref.shape[1]

    @pl.when(step == 0)
    def _():
        out_ref[...] = jnp.zeros_like(out_ref)

    count = cnt_ref[0]
    base = step * chunk
    live = jnp.clip(count - base, 0, chunk)

    def product(lhs, tile):
        if transpose_tile:
            return lax.dot_general(lhs, tile, NT_DIMS, preferred_element_type=jnp.float32)
        return jnp.dot(lhs, tile, preferred_element_type=jnp.float32)

    def run(g, masked):
        results = []
        for u in range(group):
            j = g * group + u
            slot = base + j
            if transpose_tile:
                src, dst = cols_ref[slot], rows_ref[slot]
            else:
                src, dst = rows_ref[slot], cols_ref[slot]
            tile = tiles_ref[j]
            lhs = side_ref[src]
            if with_degree:
                lhs = jnp.concatenate([lhs, jnp.ones((DEG_ROWS, lhs.shape[1]), lhs.dtype)], axis=0)
            prod = product(lhs, tile)
            if masked:
                prod = jnp.where(slot < count, prod, 0.0)
            results.append((dst, prod))
        for dst, prod in results:
            out_ref[dst] += prod

    def body(g, carry):
        run(g, False)
        return carry

    full = live // group
    lax.fori_loop(0, full, body, 0)

    @pl.when(full * group < live)
    def _():
        run(full, True)


def tile_pass(tiles, rows, cols, count, side, transpose_tile, with_degree):
    slots, edge, _ = tiles.shape
    n_tiles, width, _ = side.shape
    chunk = min(CHUNK, slots)
    steps = slots // chunk
    out_rows = width + (DEG_ROWS if with_degree else 0)
    kernel = functools.partial(tile_kernel, transpose_tile, with_degree, GROUP)

    def tile_map(i, rows_ref, cols_ref, cnt_ref):
        return (jnp.minimum(i, jnp.maximum(cnt_ref[0] - 1, 0) // chunk), 0, 0)

    def whole_map(i, rows_ref, cols_ref, cnt_ref):
        return (0, 0, 0)

    flops = 2 * slots * edge * edge * out_rows
    cost = pl.CostEstimate(
        flops=flops,
        transcendentals=0,
        bytes_accessed=tiles.size * 2 + side.size * 2 + n_tiles * out_rows * edge * 4,
    )
    return pl.pallas_call(
        kernel,
        out_shape=jax.ShapeDtypeStruct((n_tiles, out_rows, edge), jnp.float32),
        grid_spec=pltpu.PrefetchScalarGridSpec(
            num_scalar_prefetch=3,
            grid=(steps,),
            in_specs=[
                pl.BlockSpec((chunk, edge, edge), tile_map),
                pl.BlockSpec((n_tiles, width, edge), whole_map),
            ],
            out_specs=pl.BlockSpec((n_tiles, out_rows, edge), whole_map),
        ),
        compiler_params=pltpu.CompilerParams(dimension_semantics=("arbitrary",)),
        cost_estimate=cost,
    )(rows, cols, count, tiles, side)


def scatter_sum(x, axis_name, parts):
    pieces = x.reshape((parts, x.shape[0] // parts) + x.shape[1:])
    return jnp.sum(lax.all_to_all(pieces, axis_name, 0, 0, tiled=False), axis=0)


def exchange_sum(flat, axis_name, parts):
    copies = jnp.broadcast_to(flat, (parts,) + flat.shape)
    return jnp.sum(lax.all_to_all(copies, axis_name, 0, 0, tiled=False), axis=0)


def exchange_gather(x, axis_name, parts):
    copies = jnp.broadcast_to(x, (parts,) + x.shape)
    got = lax.all_to_all(copies, axis_name, 0, 0, tiled=False)
    return got.reshape((parts * x.shape[0],) + x.shape[1:])


def packed_psum(n_doc, n_term, values):
    flat = jnp.concatenate([jnp.reshape(v, (-1,)) for v in values])
    flat = exchange_sum(exchange_sum(flat, "term", n_term), "doc", n_doc)
    out, start = [], 0
    for v in values:
        size = int(jnp.size(v))
        out.append(flat[start : start + size].reshape(jnp.shape(v)))
        start += size
    return out


def per_device(n_doc, n_term, tiles, tile_rows, tile_cols, tile_count, start_block, doc_cluster, term_cluster):
    local_tiles = tiles[0, 0]
    rows = tile_rows[0, 0]
    cols = tile_cols[0, 0]
    count = tile_count[0, 0].reshape(1)
    edge = local_tiles.shape[1]
    start_rows = start_block[0]
    width_k = start_rows.shape[1]
    term_tiles_own = start_rows.shape[0] // edge
    start_t = start_rows.reshape(term_tiles_own, edge, width_k).transpose(0, 2, 1)
    doc_labels = doc_cluster[0].reshape(-1, edge)
    term_labels = term_cluster[0].reshape(-1, edge)
    clusters = jnp.arange(CLUSTERS, dtype=jnp.int32)
    doc_onehot = (doc_labels[:, :, None] == clusters).astype(jnp.float32)
    term_onehot = (term_labels[:, :, None] == clusters).astype(jnp.float32)

    weights = start_t
    basis = None
    doc_degree = None
    term_degree = None
    root = None
    summed_own = None
    energy = None
    volume = None
    for step in range(ITERS):
        first = step == 0
        w_all = exchange_gather(weights, "doc", n_doc)
        left = tile_pass(local_tiles, rows, cols, count, w_all, True, first)
        left_own = lax.psum_scatter(left, "term", scatter_dimension=0, tiled=True)
        summed_own = left_own[:, :width_k, :]
        if first:
            doc_degree = left_own[:, width_k, :]
        quotient = (summed_own / doc_degree[:, None, :]).astype(jnp.bfloat16)
        q_all = lax.all_gather(quotient, "term", axis=0, tiled=True)
        right = tile_pass(local_tiles, rows, cols, count, q_all, False, first)
        right_own = scatter_sum(right, "doc", n_doc)
        if first:
            term_degree = right_own[:, width_k, :]
            root = jnp.sqrt(term_degree)
        raw = right_own[:, :width_k, :] / root[:, None, :]
        previous = root[:, None, :] * start_t.astype(jnp.float32) if first else basis
        gram_part = jnp.einsum("tki,tli->kl", raw, raw, precision=HIGH)
        along_part = jnp.einsum("tki,ti->k", raw, root, precision=HIGH)
        energy_part = jnp.sum(previous * raw, axis=(0, 2))
        volume_part = jnp.sum(term_degree)
        sums = [gram_part, along_part, energy_part, volume_part]
        if step == ITERS - 1:
            doc_ratio = summed_own / doc_degree[:, None, :]
            doc_part = jnp.einsum("tki,tij->kj", doc_ratio, doc_onehot, precision=HIGH)
            term_part = jnp.einsum("tki,tij->kj", raw / root[:, None, :], term_onehot, precision=HIGH)
            sums += [doc_part, term_part, jnp.sum(doc_onehot, axis=(0, 1)), jnp.sum(term_onehot, axis=(0, 1))]
        sums = packed_psum(n_doc, n_term, sums)
        gram_matrix, along, energy, volume = sums[:4]
        lower = jnp.linalg.cholesky(gram_matrix - jnp.outer(along, along) / volume)
        projected = raw - root[:, None, :] * (along / volume)[None, :, None]
        flat = projected.transpose(1, 0, 2).reshape(width_k, -1)
        solved = jax.scipy.linalg.solve_triangular(lower, flat, lower=True)
        basis = solved.reshape(width_k, term_tiles_own, edge).transpose(1, 0, 2)
        weights = (basis / root[:, None, :]).astype(jnp.bfloat16)

    doc_part, term_part, doc_count, term_count = sums[4:]
    scale = jnp.sqrt(volume)
    column_scale = scale * lax.rsqrt(energy)
    doc_embed = summed_own / doc_degree[:, None, :] * column_scale[None, :, None]
    term_embed = scale * basis / root[:, None, :]
    term_centered = term_part - jnp.outer(along / volume, term_count)
    term_sums = scale * jax.scipy.linalg.solve_triangular(lower, term_centered, lower=True)
    centers = (column_scale[:, None] * doc_part + term_sums) / (doc_count + term_count)[None, :]
    center_norm = jnp.sum(centers * centers, axis=0)

    def distances(embed):
        near = jnp.einsum("tki,kj->tij", embed, centers, precision=HIGH)
        norm = jnp.sum(embed * embed, axis=1)
        dist = (norm[:, :, None] - 2.0 * near + center_norm[None, None, :]) / width_k
        return dist.reshape(-1, CLUSTERS)

    return (distances(doc_embed)[None], distances(term_embed)[None])


def solution(mesh):
    placed = (
        P("doc", "term", None, None, None),
        P("doc", "term", None),
        P("doc", "term", None),
        P("doc", "term"),
        P("term", "doc", None),
        P("doc", "term"),
        P("term", "doc"),
    )
    return jax.shard_map(
        functools.partial(per_device, mesh.shape["doc"], mesh.shape["term"]),
        mesh=mesh,
        in_specs=placed,
        out_specs=(P("doc", "term", None), P("term", "doc", None)),
        check_vma=False,
    )
```

```python
import functools

import jax
import jax.numpy as jnp
from jax import lax
from jax.experimental import pallas as pl
from jax.experimental.pallas import tpu as pltpu
from jax.sharding import PartitionSpec as P

CLUSTERS = 64
ITERS = 2
CHUNK = 128
GROUP = 16
DEG_ROWS = 8

HIGH = lax.Precision.HIGHEST
NT_DIMS = (((1,), (1,)), ((), ()))


def tile_kernel(transpose_tile, with_degree, group, split, rows_ref, cols_ref, cnt_ref, tiles_ref, side_ref, out_ref, *rest):
    step = pl.program_id(0)
    chunk = tiles_ref.shape[0]
    width = side_ref.shape[1]

    @pl.when(step == 0)
    def _():
        out_ref[...] = jnp.zeros_like(out_ref)
        for extra in rest:
            extra[...] = jnp.zeros_like(extra)

    count = cnt_ref[0]
    base = step * chunk
    live = jnp.clip(count - base, 0, chunk)

    def product(lhs, tile):
        if transpose_tile:
            return lax.dot_general(lhs, tile, NT_DIMS, preferred_element_type=jnp.float32)
        return jnp.dot(lhs, tile, preferred_element_type=jnp.float32)

    def run(g, masked):
        results = []
        for u in range(group):
            j = g * group + u
            slot = base + j
            if transpose_tile:
                src, dst = cols_ref[slot], rows_ref[slot]
            else:
                src, dst = rows_ref[slot], cols_ref[slot]
            tile = tiles_ref[j]
            lhs = side_ref[src]
            if with_degree:
                lhs = jnp.concatenate([lhs, jnp.ones((DEG_ROWS, lhs.shape[1]), lhs.dtype)], axis=0)
            prod = product(lhs, tile)
            if masked:
                prod = jnp.where(slot < count, prod, 0.0)
            results.append((dst, prod))
        for dst, prod in results:
            if split is None:
                out_ref[dst] += prod
            else:
                head = prod[:split]
                if with_degree:
                    head = jnp.concatenate([head, prod[width:]], axis=0)
                out_ref[dst] += head
                rest[0][dst] += prod[split:width]

    def body(g, carry):
        run(g, False)
        return carry

    full = live // group
    lax.fori_loop(0, full, body, 0)

    @pl.when(full * group < live)
    def _():
        run(full, True)


def tile_pass(tiles, rows, cols, count, side, transpose_tile, with_degree, split=None):
    slots, edge, _ = tiles.shape
    n_tiles, width, _ = side.shape
    chunk = min(CHUNK, slots)
    steps = slots // chunk
    out_rows = width + (DEG_ROWS if with_degree else 0)
    kernel = functools.partial(tile_kernel, transpose_tile, with_degree, GROUP, split)
    if split is None:
        shapes = [(n_tiles, out_rows, edge)]
    else:
        shapes = [(n_tiles, out_rows - width + split, edge), (n_tiles, width - split, edge)]

    def tile_map(i, rows_ref, cols_ref, cnt_ref):
        return (jnp.minimum(i, jnp.maximum(cnt_ref[0] - 1, 0) // chunk), 0, 0)

    def whole_map(i, rows_ref, cols_ref, cnt_ref):
        return (0, 0, 0)

    flops = 2 * slots * edge * edge * out_rows
    cost = pl.CostEstimate(
        flops=flops,
        transcendentals=0,
        bytes_accessed=tiles.size * 2 + side.size * 2 + n_tiles * out_rows * edge * 4,
    )
    outs = pl.pallas_call(
        kernel,
        out_shape=[jax.ShapeDtypeStruct(shape, jnp.float32) for shape in shapes],
        grid_spec=pltpu.PrefetchScalarGridSpec(
            num_scalar_prefetch=3,
            grid=(steps,),
            in_specs=[
                pl.BlockSpec((chunk, edge, edge), tile_map),
                pl.BlockSpec((n_tiles, width, edge), whole_map),
            ],
            out_specs=[pl.BlockSpec(shape, whole_map) for shape in shapes],
        ),
        compiler_params=pltpu.CompilerParams(dimension_semantics=("arbitrary",)),
        cost_estimate=cost,
    )(rows, cols, count, tiles, side)
    return outs[0] if split is None else outs


def scatter_sum(x, axis_name, parts):
    pieces = x.reshape((parts, x.shape[0] // parts) + x.shape[1:])
    return jnp.sum(lax.all_to_all(pieces, axis_name, 0, 0, tiled=False), axis=0)


def exchange_sum(flat, axis_name, parts):
    copies = jnp.broadcast_to(flat, (parts,) + flat.shape)
    return jnp.sum(lax.all_to_all(copies, axis_name, 0, 0, tiled=False), axis=0)


def exchange_gather(x, axis_name, parts):
    copies = jnp.broadcast_to(x, (parts,) + x.shape)
    got = lax.all_to_all(copies, axis_name, 0, 0, tiled=False)
    return got.reshape((parts * x.shape[0],) + x.shape[1:])


def packed_psum(n_doc, n_term, values):
    flat = jnp.concatenate([jnp.reshape(v, (-1,)) for v in values])
    flat = exchange_sum(exchange_sum(flat, "term", n_term), "doc", n_doc)
    out, start = [], 0
    for v in values:
        size = int(jnp.size(v))
        out.append(flat[start : start + size].reshape(jnp.shape(v)))
        start += size
    return out


def per_device(n_doc, n_term, tiles, tile_rows, tile_cols, tile_count, start_block, doc_cluster, term_cluster):
    local_tiles = tiles[0, 0]
    rows = tile_rows[0, 0]
    cols = tile_cols[0, 0]
    count = tile_count[0, 0].reshape(1)
    edge = local_tiles.shape[1]
    start_rows = start_block[0]
    width_k = start_rows.shape[1]
    term_tiles_own = start_rows.shape[0] // edge
    start_t = start_rows.reshape(term_tiles_own, edge, width_k).transpose(0, 2, 1)
    doc_labels = doc_cluster[0].reshape(-1, edge)
    term_labels = term_cluster[0].reshape(-1, edge)
    clusters = jnp.arange(CLUSTERS, dtype=jnp.int32)
    doc_onehot = (doc_labels[:, :, None] == clusters).astype(jnp.float32)
    term_onehot = (term_labels[:, :, None] == clusters).astype(jnp.float32)

    weights = start_t
    basis = None
    doc_degree = None
    term_degree = None
    root = None
    summed_own = None
    energy = None
    volume = None
    for step in range(ITERS):
        first = step == 0
        w_all = exchange_gather(weights, "doc", n_doc)
        half = width_k // 2
        left_a, left_b = tile_pass(local_tiles, rows, cols, count, w_all, True, first, half)
        own_a = lax.psum_scatter(left_a, "term", scatter_dimension=0, tiled=True)
        if first:
            doc_degree = own_a[:, half, :]
        summed_a = own_a[:, :half, :]
        qa_all = lax.all_gather((summed_a / doc_degree[:, None, :]).astype(jnp.bfloat16), "term", axis=0, tiled=True)
        left_b, _ = lax.optimization_barrier((left_b, qa_all))
        summed_b = lax.psum_scatter(left_b, "term", scatter_dimension=0, tiled=True)
        qb_all = lax.all_gather((summed_b / doc_degree[:, None, :]).astype(jnp.bfloat16), "term", axis=0, tiled=True)
        summed_own = jnp.concatenate([summed_a, summed_b], axis=1)
        right_a = scatter_sum(tile_pass(local_tiles, rows, cols, count, qa_all, False, first), "doc", n_doc)
        right_b = scatter_sum(tile_pass(local_tiles, rows, cols, count, qb_all, False, False), "doc", n_doc)
        if first:
            term_degree = right_a[:, half, :]
            root = jnp.sqrt(term_degree)
        right_own = jnp.concatenate([right_a[:, :half, :], right_b], axis=1)
        raw = right_own[:, :width_k, :] / root[:, None, :]
        previous = root[:, None, :] * start_t.astype(jnp.float32) if first else basis
        gram_part = jnp.einsum("tki,tli->kl", raw, raw, precision=HIGH)
        along_part = jnp.einsum("tki,ti->k", raw, root, precision=HIGH)
        energy_part = jnp.sum(previous * raw, axis=(0, 2))
        volume_part = jnp.sum(term_degree)
        sums = [gram_part, along_part, energy_part, volume_part]
        if step == ITERS - 1:
            doc_ratio = summed_own / doc_degree[:, None, :]
            doc_part = jnp.einsum("tki,tij->kj", doc_ratio, doc_onehot, precision=HIGH)
            term_part = jnp.einsum("tki,tij->kj", raw / root[:, None, :], term_onehot, precision=HIGH)
            sums += [doc_part, term_part, jnp.sum(doc_onehot, axis=(0, 1)), jnp.sum(term_onehot, axis=(0, 1))]
        sums = packed_psum(n_doc, n_term, sums)
        gram_matrix, along, energy, volume = sums[:4]
        lower = jnp.linalg.cholesky(gram_matrix - jnp.outer(along, along) / volume)
        projected = raw - root[:, None, :] * (along / volume)[None, :, None]
        flat = projected.transpose(1, 0, 2).reshape(width_k, -1)
        solved = jax.scipy.linalg.solve_triangular(lower, flat, lower=True)
        basis = solved.reshape(width_k, term_tiles_own, edge).transpose(1, 0, 2)
        weights = (basis / root[:, None, :]).astype(jnp.bfloat16)

    doc_part, term_part, doc_count, term_count = sums[4:]
    scale = jnp.sqrt(volume)
    column_scale = scale * lax.rsqrt(energy)
    doc_embed = summed_own / doc_degree[:, None, :] * column_scale[None, :, None]
    term_embed = scale * basis / root[:, None, :]
    term_centered = term_part - jnp.outer(along / volume, term_count)
    term_sums = scale * jax.scipy.linalg.solve_triangular(lower, term_centered, lower=True)
    centers = (column_scale[:, None] * doc_part + term_sums) / (doc_count + term_count)[None, :]
    center_norm = jnp.sum(centers * centers, axis=0)

    def distances(embed):
        near = jnp.einsum("tki,kj->tij", embed, centers, precision=HIGH)
        norm = jnp.sum(embed * embed, axis=1)
        dist = (norm[:, :, None] - 2.0 * near + center_norm[None, None, :]) / width_k
        return dist.reshape(-1, CLUSTERS)

    return (distances(doc_embed)[None], distances(term_embed)[None])


def solution(mesh):
    placed = (
        P("doc", "term", None, None, None),
        P("doc", "term", None),
        P("doc", "term", None),
        P("doc", "term"),
        P("term", "doc", None),
        P("doc", "term"),
        P("term", "doc"),
    )
    return jax.shard_map(
        functools.partial(per_device, mesh.shape["doc"], mesh.shape["term"]),
        mesh=mesh,
        in_specs=placed,
        out_specs=(P("doc", "term", None), P("term", "doc", None)),
        check_vma=False,
    )
```

```python
import functools

import jax
import jax.numpy as jnp
from jax import lax
from jax.experimental import pallas as pl
from jax.experimental.pallas import tpu as pltpu
from jax.sharding import PartitionSpec as P

CLUSTERS = 64
ITERS = 2
CHUNK = 128
GROUP = 16
DEG_ROWS = 8

HIGH = lax.Precision.HIGHEST
NT_DIMS = (((1,), (1,)), ((), ()))


def tile_kernel(transpose_tile, with_degree, group, split, rows_ref, cols_ref, cnt_ref, tiles_ref, side_ref, out_ref, *rest):
    step = pl.program_id(0)
    chunk = tiles_ref.shape[0]
    width = side_ref.shape[1]

    @pl.when(step == 0)
    def _():
        out_ref[...] = jnp.zeros_like(out_ref)
        for extra in rest:
            extra[...] = jnp.zeros_like(extra)

    count = cnt_ref[0]
    base = step * chunk
    live = jnp.clip(count - base, 0, chunk)

    def product(lhs, tile):
        if transpose_tile:
            return lax.dot_general(lhs, tile, NT_DIMS, preferred_element_type=jnp.float32)
        return jnp.dot(lhs, tile, preferred_element_type=jnp.float32)

    def run(g, masked):
        results = []
        for u in range(group):
            j = g * group + u
            slot = base + j
            if transpose_tile:
                src, dst = cols_ref[slot], rows_ref[slot]
            else:
                src, dst = rows_ref[slot], cols_ref[slot]
            tile = tiles_ref[j]
            lhs = side_ref[src]
            if with_degree:
                lhs = jnp.concatenate([lhs, jnp.ones((DEG_ROWS, lhs.shape[1]), lhs.dtype)], axis=0)
            prod = product(lhs, tile)
            if masked:
                prod = jnp.where(slot < count, prod, 0.0)
            results.append((dst, prod))
        for dst, prod in results:
            if split is None:
                out_ref[dst] += prod
            else:
                head = prod[:split]
                if with_degree:
                    head = jnp.concatenate([head, prod[width:]], axis=0)
                out_ref[dst] += head
                rest[0][dst] += prod[split:width]

    def body(g, carry):
        run(g, False)
        return carry

    full = live // group
    lax.fori_loop(0, full, body, 0)

    @pl.when(full * group < live)
    def _():
        run(full, True)


def tile_pass(tiles, rows, cols, count, side, transpose_tile, with_degree, split=None):
    slots, edge, _ = tiles.shape
    n_tiles, width, _ = side.shape
    chunk = min(CHUNK, slots)
    steps = slots // chunk
    out_rows = width + (DEG_ROWS if with_degree else 0)
    kernel = functools.partial(tile_kernel, transpose_tile, with_degree, GROUP, split)
    if split is None:
        shapes = [(n_tiles, out_rows, edge)]
    else:
        shapes = [(n_tiles, out_rows - width + split, edge), (n_tiles, width - split, edge)]

    def tile_map(i, rows_ref, cols_ref, cnt_ref):
        return (jnp.minimum(i, jnp.maximum(cnt_ref[0] - 1, 0) // chunk), 0, 0)

    def whole_map(i, rows_ref, cols_ref, cnt_ref):
        return (0, 0, 0)

    flops = 2 * slots * edge * edge * out_rows
    cost = pl.CostEstimate(
        flops=flops,
        transcendentals=0,
        bytes_accessed=tiles.size * 2 + side.size * 2 + n_tiles * out_rows * edge * 4,
    )
    outs = pl.pallas_call(
        kernel,
        out_shape=[jax.ShapeDtypeStruct(shape, jnp.float32) for shape in shapes],
        grid_spec=pltpu.PrefetchScalarGridSpec(
            num_scalar_prefetch=3,
            grid=(steps,),
            in_specs=[
                pl.BlockSpec((chunk, edge, edge), tile_map),
                pl.BlockSpec((n_tiles, width, edge), whole_map),
            ],
            out_specs=[pl.BlockSpec(shape, whole_map) for shape in shapes],
        ),
        compiler_params=pltpu.CompilerParams(dimension_semantics=("arbitrary",)),
        cost_estimate=cost,
    )(rows, cols, count, tiles, side)
    return outs[0] if split is None else outs


def scatter_sum(x, axis_name, parts):
    pieces = x.reshape((parts, x.shape[0] // parts) + x.shape[1:])
    return jnp.sum(lax.all_to_all(pieces, axis_name, 0, 0, tiled=False), axis=0)


def exchange_sum(flat, axis_name, parts):
    copies = jnp.broadcast_to(flat, (parts,) + flat.shape)
    return jnp.sum(lax.all_to_all(copies, axis_name, 0, 0, tiled=False), axis=0)


def exchange_gather(x, axis_name, parts):
    copies = jnp.broadcast_to(x, (parts,) + x.shape)
    got = lax.all_to_all(copies, axis_name, 0, 0, tiled=False)
    return got.reshape((parts * x.shape[0],) + x.shape[1:])


def packed_psum(n_doc, n_term, values):
    flat = jnp.concatenate([jnp.reshape(v, (-1,)) for v in values])
    flat = exchange_sum(exchange_sum(flat, "term", n_term), "doc", n_doc)
    out, start = [], 0
    for v in values:
        size = int(jnp.size(v))
        out.append(flat[start : start + size].reshape(jnp.shape(v)))
        start += size
    return out


def per_device(n_doc, n_term, tiles, tile_rows, tile_cols, tile_count, start_block, doc_cluster, term_cluster):
    local_tiles = tiles[0, 0]
    rows = tile_rows[0, 0]
    cols = tile_cols[0, 0]
    count = tile_count[0, 0].reshape(1)
    edge = local_tiles.shape[1]
    start_rows = start_block[0]
    width_k = start_rows.shape[1]
    term_tiles_own = start_rows.shape[0] // edge
    start_t = start_rows.reshape(term_tiles_own, edge, width_k).transpose(0, 2, 1)
    doc_labels = doc_cluster[0].reshape(-1, edge)
    term_labels = term_cluster[0].reshape(-1, edge)
    clusters = jnp.arange(CLUSTERS, dtype=jnp.int32)
    doc_onehot = (doc_labels[:, :, None] == clusters).astype(jnp.float32)
    term_onehot = (term_labels[:, :, None] == clusters).astype(jnp.float32)

    weights = start_t
    basis = None
    doc_degree = None
    term_degree = None
    root = None
    summed_own = None
    energy = None
    volume = None
    for step in range(ITERS):
        first = step == 0
        w_all = exchange_gather(weights, "doc", n_doc)
        half = width_k // 2
        left_a, left_b = tile_pass(local_tiles, rows, cols, count, w_all, True, first, half)
        own_a = lax.psum_scatter(left_a, "term", scatter_dimension=0, tiled=True)
        if first:
            doc_degree = own_a[:, half, :]
        summed_a = own_a[:, :half, :]
        qa_all = lax.all_gather((summed_a / doc_degree[:, None, :]).astype(jnp.bfloat16), "term", axis=0, tiled=True)
        summed_b = lax.psum_scatter(left_b, "term", scatter_dimension=0, tiled=True)
        qb_all = lax.all_gather((summed_b / doc_degree[:, None, :]).astype(jnp.bfloat16), "term", axis=0, tiled=True)
        summed_own = jnp.concatenate([summed_a, summed_b], axis=1)
        right_a = scatter_sum(tile_pass(local_tiles, rows, cols, count, qa_all, False, first), "doc", n_doc)
        right_b = scatter_sum(tile_pass(local_tiles, rows, cols, count, qb_all, False, False), "doc", n_doc)
        if first:
            term_degree = right_a[:, half, :]
            root = jnp.sqrt(term_degree)
        right_own = jnp.concatenate([right_a[:, :half, :], right_b], axis=1)
        raw = right_own[:, :width_k, :] / root[:, None, :]
        previous = root[:, None, :] * start_t.astype(jnp.float32) if first else basis
        gram_part = jnp.einsum("tki,tli->kl", raw, raw, precision=HIGH)
        along_part = jnp.einsum("tki,ti->k", raw, root, precision=HIGH)
        energy_part = jnp.sum(previous * raw, axis=(0, 2))
        volume_part = jnp.sum(term_degree)
        sums = [gram_part, along_part, energy_part, volume_part]
        if step == ITERS - 1:
            doc_ratio = summed_own / doc_degree[:, None, :]
            doc_part = jnp.einsum("tki,tij->kj", doc_ratio, doc_onehot, precision=HIGH)
            term_part = jnp.einsum("tki,tij->kj", raw / root[:, None, :], term_onehot, precision=HIGH)
            sums += [doc_part, term_part, jnp.sum(doc_onehot, axis=(0, 1)), jnp.sum(term_onehot, axis=(0, 1))]
        sums = packed_psum(n_doc, n_term, sums)
        gram_matrix, along, energy, volume = sums[:4]
        lower = jnp.linalg.cholesky(gram_matrix - jnp.outer(along, along) / volume)
        projected = raw - root[:, None, :] * (along / volume)[None, :, None]
        flat = projected.transpose(1, 0, 2).reshape(width_k, -1)
        solved = jax.scipy.linalg.solve_triangular(lower, flat, lower=True)
        basis = solved.reshape(width_k, term_tiles_own, edge).transpose(1, 0, 2)
        weights = (basis / root[:, None, :]).astype(jnp.bfloat16)

    doc_part, term_part, doc_count, term_count = sums[4:]
    scale = jnp.sqrt(volume)
    column_scale = scale * lax.rsqrt(energy)
    doc_embed = summed_own / doc_degree[:, None, :] * column_scale[None, :, None]
    term_embed = scale * basis / root[:, None, :]
    term_centered = term_part - jnp.outer(along / volume, term_count)
    term_sums = scale * jax.scipy.linalg.solve_triangular(lower, term_centered, lower=True)
    centers = (column_scale[:, None] * doc_part + term_sums) / (doc_count + term_count)[None, :]
    center_norm = jnp.sum(centers * centers, axis=0)

    def distances(embed):
        near = jnp.einsum("tki,kj->tij", embed, centers, precision=HIGH)
        norm = jnp.sum(embed * embed, axis=1)
        dist = (norm[:, :, None] - 2.0 * near + center_norm[None, None, :]) / width_k
        return dist.reshape(-1, CLUSTERS)

    return (distances(doc_embed)[None], distances(term_embed)[None])


def solution(mesh):
    placed = (
        P("doc", "term", None, None, None),
        P("doc", "term", None),
        P("doc", "term", None),
        P("doc", "term"),
        P("term", "doc", None),
        P("doc", "term"),
        P("term", "doc"),
    )
    return jax.shard_map(
        functools.partial(per_device, mesh.shape["doc"], mesh.shape["term"]),
        mesh=mesh,
        in_specs=placed,
        out_specs=(P("doc", "term", None), P("term", "doc", None)),
        check_vma=False,
    )
```

```python
import functools

import jax
import jax.numpy as jnp
from jax import lax
from jax.experimental import pallas as pl
from jax.experimental.pallas import tpu as pltpu
from jax.sharding import PartitionSpec as P

CLUSTERS = 64
ITERS = 2
CHUNK = 128
GROUP = 16
DEG_ROWS = 8

HIGH = lax.Precision.HIGHEST
NT_DIMS = (((1,), (1,)), ((), ()))


def tile_kernel(transpose_tile, with_degree, group, split, rows_ref, cols_ref, cnt_ref, tiles_ref, side_ref, out_ref, *rest):
    step = pl.program_id(0)
    chunk = tiles_ref.shape[0]
    width = side_ref.shape[1]

    @pl.when(step == 0)
    def _():
        out_ref[...] = jnp.zeros_like(out_ref)
        for extra in rest:
            extra[...] = jnp.zeros_like(extra)

    count = cnt_ref[0]
    base = step * chunk
    live = jnp.clip(count - base, 0, chunk)

    def product(lhs, tile):
        if transpose_tile:
            return lax.dot_general(lhs, tile, NT_DIMS, preferred_element_type=jnp.float32)
        return jnp.dot(lhs, tile, preferred_element_type=jnp.float32)

    def run(g, masked):
        results = []
        for u in range(group):
            j = g * group + u
            slot = base + j
            if transpose_tile:
                src, dst = cols_ref[slot], rows_ref[slot]
            else:
                src, dst = rows_ref[slot], cols_ref[slot]
            tile = tiles_ref[j]
            lhs = side_ref[src]
            if with_degree:
                lhs = jnp.concatenate([lhs, jnp.ones((DEG_ROWS, lhs.shape[1]), lhs.dtype)], axis=0)
            prod = product(lhs, tile)
            if masked:
                prod = jnp.where(slot < count, prod, 0.0)
            results.append((dst, prod))
        for dst, prod in results:
            if split is None:
                out_ref[dst] += prod
            else:
                head = prod[:split]
                if with_degree:
                    head = jnp.concatenate([head, prod[width:]], axis=0)
                out_ref[dst] += head
                rest[0][dst] += prod[split:width]

    def body(g, carry):
        run(g, False)
        return carry

    full = live // group
    lax.fori_loop(0, full, body, 0)

    @pl.when(full * group < live)
    def _():
        run(full, True)


def tile_pass(tiles, rows, cols, count, side, transpose_tile, with_degree, split=None):
    slots, edge, _ = tiles.shape
    n_tiles, width, _ = side.shape
    chunk = min(CHUNK, slots)
    steps = slots // chunk
    out_rows = width + (DEG_ROWS if with_degree else 0)
    kernel = functools.partial(tile_kernel, transpose_tile, with_degree, GROUP, split)
    if split is None:
        shapes = [(n_tiles, out_rows, edge)]
    else:
        shapes = [(n_tiles, out_rows - width + split, edge), (n_tiles, width - split, edge)]

    def tile_map(i, rows_ref, cols_ref, cnt_ref):
        return (jnp.minimum(i, jnp.maximum(cnt_ref[0] - 1, 0) // chunk), 0, 0)

    def whole_map(i, rows_ref, cols_ref, cnt_ref):
        return (0, 0, 0)

    flops = 2 * slots * edge * edge * out_rows
    cost = pl.CostEstimate(
        flops=flops,
        transcendentals=0,
        bytes_accessed=tiles.size * 2 + side.size * 2 + n_tiles * out_rows * edge * 4,
    )
    outs = pl.pallas_call(
        kernel,
        out_shape=[jax.ShapeDtypeStruct(shape, jnp.float32) for shape in shapes],
        grid_spec=pltpu.PrefetchScalarGridSpec(
            num_scalar_prefetch=3,
            grid=(steps,),
            in_specs=[
                pl.BlockSpec((chunk, edge, edge), tile_map),
                pl.BlockSpec((n_tiles, width, edge), whole_map),
            ],
            out_specs=[pl.BlockSpec(shape, whole_map) for shape in shapes],
        ),
        compiler_params=pltpu.CompilerParams(dimension_semantics=("arbitrary",)),
        cost_estimate=cost,
    )(rows, cols, count, tiles, side)
    return outs[0] if split is None else outs


def scatter_sum(x, axis_name, parts):
    pieces = x.reshape((parts, x.shape[0] // parts) + x.shape[1:])
    return jnp.sum(lax.all_to_all(pieces, axis_name, 0, 0, tiled=False), axis=0)


def exchange_sum(flat, axis_name, parts):
    copies = jnp.broadcast_to(flat, (parts,) + flat.shape)
    return jnp.sum(lax.all_to_all(copies, axis_name, 0, 0, tiled=False), axis=0)


def exchange_gather(x, axis_name, parts):
    copies = jnp.broadcast_to(x, (parts,) + x.shape)
    got = lax.all_to_all(copies, axis_name, 0, 0, tiled=False)
    return got.reshape((parts * x.shape[0],) + x.shape[1:])


def packed_psum(n_doc, n_term, values):
    flat = jnp.concatenate([jnp.reshape(v, (-1,)) for v in values])
    flat = exchange_sum(exchange_sum(flat, "term", n_term), "doc", n_doc)
    out, start = [], 0
    for v in values:
        size = int(jnp.size(v))
        out.append(flat[start : start + size].reshape(jnp.shape(v)))
        start += size
    return out


def per_device(n_doc, n_term, tiles, tile_rows, tile_cols, tile_count, start_block, doc_cluster, term_cluster):
    local_tiles = tiles[0, 0]
    rows = tile_rows[0, 0]
    cols = tile_cols[0, 0]
    count = tile_count[0, 0].reshape(1)
    edge = local_tiles.shape[1]
    start_rows = start_block[0]
    width_k = start_rows.shape[1]
    term_tiles_own = start_rows.shape[0] // edge
    start_t = start_rows.reshape(term_tiles_own, edge, width_k).transpose(0, 2, 1)
    doc_labels = doc_cluster[0].reshape(-1, edge)
    term_labels = term_cluster[0].reshape(-1, edge)
    clusters = jnp.arange(CLUSTERS, dtype=jnp.int32)
    doc_onehot = (doc_labels[:, :, None] == clusters).astype(jnp.float32)
    term_onehot = (term_labels[:, :, None] == clusters).astype(jnp.float32)

    weights = start_t
    basis = None
    doc_degree = None
    term_degree = None
    root = None
    summed_own = None
    energy = None
    volume = None
    for step in range(ITERS):
        first = step == 0
        w_all = exchange_gather(weights, "doc", n_doc)
        half = width_k * 3 // 4
        left_a, left_b = tile_pass(local_tiles, rows, cols, count, w_all, True, first, half)
        own_a = lax.psum_scatter(left_a, "term", scatter_dimension=0, tiled=True)
        if first:
            doc_degree = own_a[:, half, :]
        summed_a = own_a[:, :half, :]
        qa_all = lax.all_gather((summed_a / doc_degree[:, None, :]).astype(jnp.bfloat16), "term", axis=0, tiled=True)
        left_b, _ = lax.optimization_barrier((left_b, qa_all))
        summed_b = lax.psum_scatter(left_b, "term", scatter_dimension=0, tiled=True)
        qb_all = lax.all_gather((summed_b / doc_degree[:, None, :]).astype(jnp.bfloat16), "term", axis=0, tiled=True)
        summed_own = jnp.concatenate([summed_a, summed_b], axis=1)
        right_a = scatter_sum(tile_pass(local_tiles, rows, cols, count, qa_all, False, first), "doc", n_doc)
        right_b = scatter_sum(tile_pass(local_tiles, rows, cols, count, qb_all, False, False), "doc", n_doc)
        if first:
            term_degree = right_a[:, half, :]
            root = jnp.sqrt(term_degree)
        right_own = jnp.concatenate([right_a[:, :half, :], right_b], axis=1)
        raw = right_own[:, :width_k, :] / root[:, None, :]
        previous = root[:, None, :] * start_t.astype(jnp.float32) if first else basis
        gram_part = jnp.einsum("tki,tli->kl", raw, raw, precision=HIGH)
        along_part = jnp.einsum("tki,ti->k", raw, root, precision=HIGH)
        energy_part = jnp.sum(previous * raw, axis=(0, 2))
        volume_part = jnp.sum(term_degree)
        sums = [gram_part, along_part, energy_part, volume_part]
        if step == ITERS - 1:
            doc_ratio = summed_own / doc_degree[:, None, :]
            doc_part = jnp.einsum("tki,tij->kj", doc_ratio, doc_onehot, precision=HIGH)
            term_part = jnp.einsum("tki,tij->kj", raw / root[:, None, :], term_onehot, precision=HIGH)
            sums += [doc_part, term_part, jnp.sum(doc_onehot, axis=(0, 1)), jnp.sum(term_onehot, axis=(0, 1))]
        sums = packed_psum(n_doc, n_term, sums)
        gram_matrix, along, energy, volume = sums[:4]
        lower = jnp.linalg.cholesky(gram_matrix - jnp.outer(along, along) / volume)
        projected = raw - root[:, None, :] * (along / volume)[None, :, None]
        flat = projected.transpose(1, 0, 2).reshape(width_k, -1)
        solved = jax.scipy.linalg.solve_triangular(lower, flat, lower=True)
        basis = solved.reshape(width_k, term_tiles_own, edge).transpose(1, 0, 2)
        weights = (basis / root[:, None, :]).astype(jnp.bfloat16)

    doc_part, term_part, doc_count, term_count = sums[4:]
    scale = jnp.sqrt(volume)
    column_scale = scale * lax.rsqrt(energy)
    doc_embed = summed_own / doc_degree[:, None, :] * column_scale[None, :, None]
    term_embed = scale * basis / root[:, None, :]
    term_centered = term_part - jnp.outer(along / volume, term_count)
    term_sums = scale * jax.scipy.linalg.solve_triangular(lower, term_centered, lower=True)
    centers = (column_scale[:, None] * doc_part + term_sums) / (doc_count + term_count)[None, :]
    center_norm = jnp.sum(centers * centers, axis=0)

    def distances(embed):
        near = jnp.einsum("tki,kj->tij", embed, centers, precision=HIGH)
        norm = jnp.sum(embed * embed, axis=1)
        dist = (norm[:, :, None] - 2.0 * near + center_norm[None, None, :]) / width_k
        return dist.reshape(-1, CLUSTERS)

    return (distances(doc_embed)[None], distances(term_embed)[None])


def solution(mesh):
    placed = (
        P("doc", "term", None, None, None),
        P("doc", "term", None),
        P("doc", "term", None),
        P("doc", "term"),
        P("term", "doc", None),
        P("doc", "term"),
        P("term", "doc"),
    )
    return jax.shard_map(
        functools.partial(per_device, mesh.shape["doc"], mesh.shape["term"]),
        mesh=mesh,
        in_specs=placed,
        out_specs=(P("doc", "term", None), P("term", "doc", None)),
        check_vma=False,
    )
```

```python
import functools

import jax
import jax.numpy as jnp
from jax import lax
from jax.experimental import pallas as pl
from jax.experimental.pallas import tpu as pltpu
from jax.sharding import PartitionSpec as P

CLUSTERS = 64
ITERS = 2
CHUNK = 128
GROUP = 16
DEG_ROWS = 8

HIGH = lax.Precision.HIGHEST
NT_DIMS = (((1,), (1,)), ((), ()))


def tile_kernel(transpose_tile, with_degree, group, split, rows_ref, cols_ref, cnt_ref, tiles_ref, side_ref, out_ref, *rest):
    step = pl.program_id(0)
    chunk = tiles_ref.shape[0]
    width = side_ref.shape[1]

    @pl.when(step == 0)
    def _():
        out_ref[...] = jnp.zeros_like(out_ref)
        for extra in rest:
            extra[...] = jnp.zeros_like(extra)

    count = cnt_ref[0]
    base = step * chunk
    live = jnp.clip(count - base, 0, chunk)

    def product(lhs, tile):
        if transpose_tile:
            return lax.dot_general(lhs, tile, NT_DIMS, preferred_element_type=jnp.float32)
        return jnp.dot(lhs, tile, preferred_element_type=jnp.float32)

    def run(g, masked):
        results = []
        for u in range(group):
            j = g * group + u
            slot = base + j
            if transpose_tile:
                src, dst = cols_ref[slot], rows_ref[slot]
            else:
                src, dst = rows_ref[slot], cols_ref[slot]
            tile = tiles_ref[j]
            lhs = side_ref[src]
            if with_degree:
                lhs = jnp.concatenate([lhs, jnp.ones((DEG_ROWS, lhs.shape[1]), lhs.dtype)], axis=0)
            prod = product(lhs, tile)
            if masked:
                prod = jnp.where(slot < count, prod, 0.0)
            results.append((dst, prod))
        for dst, prod in results:
            if split is None:
                out_ref[dst] += prod
            else:
                head = prod[:split]
                if with_degree:
                    head = jnp.concatenate([head, prod[width:]], axis=0)
                out_ref[dst] += head
                rest[0][dst] += prod[split:width]

    def body(g, carry):
        run(g, False)
        return carry

    full = live // group
    lax.fori_loop(0, full, body, 0)

    @pl.when(full * group < live)
    def _():
        run(full, True)


def tile_pass(tiles, rows, cols, count, side, transpose_tile, with_degree, split=None):
    slots, edge, _ = tiles.shape
    n_tiles, width, _ = side.shape
    chunk = min(CHUNK, slots)
    steps = slots // chunk
    out_rows = width + (DEG_ROWS if with_degree else 0)
    kernel = functools.partial(tile_kernel, transpose_tile, with_degree, GROUP, split)
    if split is None:
        shapes = [(n_tiles, out_rows, edge)]
    else:
        shapes = [(n_tiles, out_rows - width + split, edge), (n_tiles, width - split, edge)]

    def tile_map(i, rows_ref, cols_ref, cnt_ref):
        return (jnp.minimum(i, jnp.maximum(cnt_ref[0] - 1, 0) // chunk), 0, 0)

    def whole_map(i, rows_ref, cols_ref, cnt_ref):
        return (0, 0, 0)

    flops = 2 * slots * edge * edge * out_rows
    cost = pl.CostEstimate(
        flops=flops,
        transcendentals=0,
        bytes_accessed=tiles.size * 2 + side.size * 2 + n_tiles * out_rows * edge * 4,
    )
    outs = pl.pallas_call(
        kernel,
        out_shape=[jax.ShapeDtypeStruct(shape, jnp.float32) for shape in shapes],
        grid_spec=pltpu.PrefetchScalarGridSpec(
            num_scalar_prefetch=3,
            grid=(steps,),
            in_specs=[
                pl.BlockSpec((chunk, edge, edge), tile_map),
                pl.BlockSpec((n_tiles, width, edge), whole_map),
            ],
            out_specs=[pl.BlockSpec(shape, whole_map) for shape in shapes],
        ),
        compiler_params=pltpu.CompilerParams(dimension_semantics=("arbitrary",)),
        cost_estimate=cost,
    )(rows, cols, count, tiles, side)
    return outs[0] if split is None else outs


def scatter_sum(x, axis_name, parts):
    pieces = x.reshape((parts, x.shape[0] // parts) + x.shape[1:])
    return jnp.sum(lax.all_to_all(pieces, axis_name, 0, 0, tiled=False), axis=0)


def exchange_sum(flat, axis_name, parts):
    copies = jnp.broadcast_to(flat, (parts,) + flat.shape)
    return jnp.sum(lax.all_to_all(copies, axis_name, 0, 0, tiled=False), axis=0)


def exchange_gather(x, axis_name, parts):
    copies = jnp.broadcast_to(x, (parts,) + x.shape)
    got = lax.all_to_all(copies, axis_name, 0, 0, tiled=False)
    return got.reshape((parts * x.shape[0],) + x.shape[1:])


def packed_psum(n_doc, n_term, values):
    flat = jnp.concatenate([jnp.reshape(v, (-1,)) for v in values])
    if flat.size * n_doc * n_term <= 1 << 18:
        flat = exchange_sum(flat, ("doc", "term"), n_doc * n_term)
    else:
        flat = exchange_sum(exchange_sum(flat, "term", n_term), "doc", n_doc)
    out, start = [], 0
    for v in values:
        size = int(jnp.size(v))
        out.append(flat[start : start + size].reshape(jnp.shape(v)))
        start += size
    return out


def per_device(n_doc, n_term, tiles, tile_rows, tile_cols, tile_count, start_block, doc_cluster, term_cluster):
    local_tiles = tiles[0, 0]
    rows = tile_rows[0, 0]
    cols = tile_cols[0, 0]
    count = tile_count[0, 0].reshape(1)
    edge = local_tiles.shape[1]
    start_rows = start_block[0]
    width_k = start_rows.shape[1]
    term_tiles_own = start_rows.shape[0] // edge
    start_t = start_rows.reshape(term_tiles_own, edge, width_k).transpose(0, 2, 1)
    doc_labels = doc_cluster[0].reshape(-1, edge)
    term_labels = term_cluster[0].reshape(-1, edge)
    clusters = jnp.arange(CLUSTERS, dtype=jnp.int32)
    doc_onehot = (doc_labels[:, :, None] == clusters).astype(jnp.float32)
    term_onehot = (term_labels[:, :, None] == clusters).astype(jnp.float32)

    weights = start_t
    basis = None
    doc_degree = None
    term_degree = None
    root = None
    summed_own = None
    energy = None
    volume = None
    for step in range(ITERS):
        first = step == 0
        w_all = exchange_gather(weights, "doc", n_doc)
        half = width_k // 2
        left_a, left_b = tile_pass(local_tiles, rows, cols, count, w_all, True, first, half)
        own_a = lax.psum_scatter(left_a, "term", scatter_dimension=0, tiled=True)
        if first:
            doc_degree = own_a[:, half, :]
        summed_a = own_a[:, :half, :]
        qa_all = lax.all_gather((summed_a / doc_degree[:, None, :]).astype(jnp.bfloat16), "term", axis=0, tiled=True)
        left_b, _ = lax.optimization_barrier((left_b, qa_all))
        summed_b = lax.psum_scatter(left_b, "term", scatter_dimension=0, tiled=True)
        qb_all = lax.all_gather((summed_b / doc_degree[:, None, :]).astype(jnp.bfloat16), "term", axis=0, tiled=True)
        summed_own = jnp.concatenate([summed_a, summed_b], axis=1)
        right_a = scatter_sum(tile_pass(local_tiles, rows, cols, count, qa_all, False, first), "doc", n_doc)
        right_b = scatter_sum(tile_pass(local_tiles, rows, cols, count, qb_all, False, False), "doc", n_doc)
        if first:
            term_degree = right_a[:, half, :]
            root = jnp.sqrt(term_degree)
        right_own = jnp.concatenate([right_a[:, :half, :], right_b], axis=1)
        raw = right_own[:, :width_k, :] / root[:, None, :]
        previous = root[:, None, :] * start_t.astype(jnp.float32) if first else basis
        gram_part = jnp.einsum("tki,tli->kl", raw, raw, precision=HIGH)
        along_part = jnp.einsum("tki,ti->k", raw, root, precision=HIGH)
        energy_part = jnp.sum(previous * raw, axis=(0, 2))
        volume_part = jnp.sum(term_degree)
        sums = [gram_part, along_part, energy_part, volume_part]
        if step == ITERS - 1:
            doc_ratio = summed_own / doc_degree[:, None, :]
            doc_part = jnp.einsum("tki,tij->kj", doc_ratio, doc_onehot, precision=HIGH)
            term_part = jnp.einsum("tki,tij->kj", raw / root[:, None, :], term_onehot, precision=HIGH)
            sums += [doc_part, term_part, jnp.sum(doc_onehot, axis=(0, 1)), jnp.sum(term_onehot, axis=(0, 1))]
        sums = packed_psum(n_doc, n_term, sums)
        gram_matrix, along, energy, volume = sums[:4]
        lower = jnp.linalg.cholesky(gram_matrix - jnp.outer(along, along) / volume)
        projected = raw - root[:, None, :] * (along / volume)[None, :, None]
        flat = projected.transpose(1, 0, 2).reshape(width_k, -1)
        solved = jax.scipy.linalg.solve_triangular(lower, flat, lower=True)
        basis = solved.reshape(width_k, term_tiles_own, edge).transpose(1, 0, 2)
        weights = (basis / root[:, None, :]).astype(jnp.bfloat16)

    doc_part, term_part, doc_count, term_count = sums[4:]
    scale = jnp.sqrt(volume)
    column_scale = scale * lax.rsqrt(energy)
    doc_embed = summed_own / doc_degree[:, None, :] * column_scale[None, :, None]
    term_embed = scale * basis / root[:, None, :]
    term_centered = term_part - jnp.outer(along / volume, term_count)
    term_sums = scale * jax.scipy.linalg.solve_triangular(lower, term_centered, lower=True)
    centers = (column_scale[:, None] * doc_part + term_sums) / (doc_count + term_count)[None, :]
    center_norm = jnp.sum(centers * centers, axis=0)

    def distances(embed):
        near = jnp.einsum("tki,kj->tij", embed, centers, precision=HIGH)
        norm = jnp.sum(embed * embed, axis=1)
        dist = (norm[:, :, None] - 2.0 * near + center_norm[None, None, :]) / width_k
        return dist.reshape(-1, CLUSTERS)

    return (distances(doc_embed)[None], distances(term_embed)[None])


def solution(mesh):
    placed = (
        P("doc", "term", None, None, None),
        P("doc", "term", None),
        P("doc", "term", None),
        P("doc", "term"),
        P("term", "doc", None),
        P("doc", "term"),
        P("term", "doc"),
    )
    return jax.shard_map(
        functools.partial(per_device, mesh.shape["doc"], mesh.shape["term"]),
        mesh=mesh,
        in_specs=placed,
        out_specs=(P("doc", "term", None), P("term", "doc", None)),
        check_vma=False,
    )
```

```python
import functools

import jax
import jax.numpy as jnp
from jax import lax
from jax.experimental import pallas as pl
from jax.experimental.pallas import tpu as pltpu
from jax.sharding import PartitionSpec as P

CLUSTERS = 64
ITERS = 2
CHUNK = 128
GROUP = 16
DEG_ROWS = 8

HIGH = lax.Precision.HIGHEST
NT_DIMS = (((1,), (1,)), ((), ()))


def tile_kernel(transpose_tile, with_degree, group, split, rows_ref, cols_ref, cnt_ref, tiles_ref, side_ref, out_ref, *rest):
    step = pl.program_id(0)
    chunk = tiles_ref.shape[0]
    width = side_ref.shape[1]

    @pl.when(step == 0)
    def _():
        out_ref[...] = jnp.zeros_like(out_ref)
        for extra in rest:
            extra[...] = jnp.zeros_like(extra)

    count = cnt_ref[0]
    base = step * chunk
    live = jnp.clip(count - base, 0, chunk)

    def product(lhs, tile):
        if transpose_tile:
            return lax.dot_general(lhs, tile, NT_DIMS, preferred_element_type=jnp.float32)
        return jnp.dot(lhs, tile, preferred_element_type=jnp.float32)

    def run(g, masked):
        results = []
        for u in range(group):
            j = g * group + u
            slot = base + j
            if transpose_tile:
                src, dst = cols_ref[slot], rows_ref[slot]
            else:
                src, dst = rows_ref[slot], cols_ref[slot]
            tile = tiles_ref[j]
            lhs = side_ref[src]
            if with_degree:
                lhs = jnp.concatenate([lhs, jnp.ones((DEG_ROWS, lhs.shape[1]), lhs.dtype)], axis=0)
            prod = product(lhs, tile)
            if masked:
                prod = jnp.where(slot < count, prod, 0.0)
            results.append((dst, prod))
        for dst, prod in results:
            if split is None:
                out_ref[dst] += prod
            else:
                head = prod[:split]
                if with_degree:
                    head = jnp.concatenate([head, prod[width:]], axis=0)
                out_ref[dst] += head
                rest[0][dst] += prod[split:width]

    def body(g, carry):
        run(g, False)
        return carry

    full = live // group
    lax.fori_loop(0, full, body, 0)

    @pl.when(full * group < live)
    def _():
        run(full, True)


def tile_pass(tiles, rows, cols, count, side, transpose_tile, with_degree, split=None):
    slots, edge, _ = tiles.shape
    n_tiles, width, _ = side.shape
    chunk = min(CHUNK, slots)
    steps = slots // chunk
    out_rows = width + (DEG_ROWS if with_degree else 0)
    kernel = functools.partial(tile_kernel, transpose_tile, with_degree, GROUP, split)
    if split is None:
        shapes = [(n_tiles, out_rows, edge)]
    else:
        shapes = [(n_tiles, out_rows - width + split, edge), (n_tiles, width - split, edge)]

    def tile_map(i, rows_ref, cols_ref, cnt_ref):
        return (jnp.minimum(i, jnp.maximum(cnt_ref[0] - 1, 0) // chunk), 0, 0)

    def whole_map(i, rows_ref, cols_ref, cnt_ref):
        return (0, 0, 0)

    flops = 2 * slots * edge * edge * out_rows
    cost = pl.CostEstimate(
        flops=flops,
        transcendentals=0,
        bytes_accessed=tiles.size * 2 + side.size * 2 + n_tiles * out_rows * edge * 4,
    )
    outs = pl.pallas_call(
        kernel,
        out_shape=[jax.ShapeDtypeStruct(shape, jnp.float32) for shape in shapes],
        grid_spec=pltpu.PrefetchScalarGridSpec(
            num_scalar_prefetch=3,
            grid=(steps,),
            in_specs=[
                pl.BlockSpec((chunk, edge, edge), tile_map),
                pl.BlockSpec((n_tiles, width, edge), whole_map),
            ],
            out_specs=[pl.BlockSpec(shape, whole_map) for shape in shapes],
        ),
        compiler_params=pltpu.CompilerParams(dimension_semantics=("arbitrary",)),
        cost_estimate=cost,
    )(rows, cols, count, tiles, side)
    return outs[0] if split is None else outs


def scatter_sum(x, axis_name, parts):
    pieces = x.reshape((parts, x.shape[0] // parts) + x.shape[1:])
    return jnp.sum(lax.all_to_all(pieces, axis_name, 0, 0, tiled=False), axis=0)


def exchange_sum(flat, axis_name, parts):
    copies = jnp.broadcast_to(flat, (parts,) + flat.shape)
    return jnp.sum(lax.all_to_all(copies, axis_name, 0, 0, tiled=False), axis=0)


def exchange_gather(x, axis_name, parts):
    copies = jnp.broadcast_to(x, (parts,) + x.shape)
    got = lax.all_to_all(copies, axis_name, 0, 0, tiled=False)
    return got.reshape((parts * x.shape[0],) + x.shape[1:])


def packed_psum(n_doc, n_term, values):
    flat = jnp.concatenate([jnp.reshape(v, (-1,)) for v in values])
    flat = exchange_sum(exchange_sum(flat, "term", n_term), "doc", n_doc)
    out, start = [], 0
    for v in values:
        size = int(jnp.size(v))
        out.append(flat[start : start + size].reshape(jnp.shape(v)))
        start += size
    return out


def per_device(n_doc, n_term, tiles, tile_rows, tile_cols, tile_count, start_block, doc_cluster, term_cluster):
    local_tiles = tiles[0, 0]
    rows = tile_rows[0, 0]
    cols = tile_cols[0, 0]
    count = tile_count[0, 0].reshape(1)
    edge = local_tiles.shape[1]
    start_rows = start_block[0]
    width_k = start_rows.shape[1]
    term_tiles_own = start_rows.shape[0] // edge
    start_t = start_rows.reshape(term_tiles_own, edge, width_k).transpose(0, 2, 1)
    doc_labels = doc_cluster[0].reshape(-1, edge)
    term_labels = term_cluster[0].reshape(-1, edge)
    clusters = jnp.arange(CLUSTERS, dtype=jnp.int32)
    doc_onehot = (doc_labels[:, :, None] == clusters).astype(jnp.float32)
    term_onehot = (term_labels[:, :, None] == clusters).astype(jnp.float32)

    weights = start_t
    basis = None
    doc_degree = None
    term_degree = None
    root = None
    summed_own = None
    energy = None
    volume = None
    for step in range(ITERS):
        first = step == 0
        w_all = exchange_gather(weights, "doc", n_doc)
        half = width_k // 2
        left_a, left_b = tile_pass(local_tiles, rows, cols, count, w_all, True, first, half)
        own_a = lax.psum_scatter(left_a, "term", scatter_dimension=0, tiled=True)
        if first:
            doc_degree = own_a[:, half, :]
        summed_a = own_a[:, :half, :]
        qa_all = lax.all_gather((summed_a / doc_degree[:, None, :]).astype(jnp.bfloat16), "term", axis=0, tiled=True)
        left_b, _ = lax.optimization_barrier((left_b, qa_all))
        summed_b = lax.psum_scatter(left_b, "term", scatter_dimension=0, tiled=True)
        qb_all = lax.all_gather((summed_b / doc_degree[:, None, :]).astype(jnp.bfloat16), "term", axis=0, tiled=True)
        summed_own = jnp.concatenate([summed_a, summed_b], axis=1)
        right_a = scatter_sum(tile_pass(local_tiles, rows, cols, count, qa_all, False, first), "doc", n_doc)
        right_b = scatter_sum(tile_pass(local_tiles, rows, cols, count, qb_all, False, False), "doc", n_doc)
        if first:
            term_degree = right_a[:, half, :]
            root = jnp.sqrt(term_degree)
        right_own = jnp.concatenate([right_a[:, :half, :], right_b], axis=1)
        raw = right_own[:, :width_k, :] / root[:, None, :]
        previous = root[:, None, :] * start_t.astype(jnp.float32) if first else basis
        gram_part = jnp.einsum("tki,tli->kl", raw, raw, precision=HIGH)
        along_part = jnp.einsum("tki,ti->k", raw, root, precision=HIGH)
        energy_part = jnp.sum(previous * raw, axis=(0, 2))
        volume_part = jnp.sum(term_degree)
        sums = [gram_part, along_part, energy_part, volume_part]
        if step == ITERS - 1:
            doc_ratio = summed_own / doc_degree[:, None, :]
            doc_part = jnp.einsum("tki,tij->kj", doc_ratio, doc_onehot, precision=HIGH)
            term_part = jnp.einsum("tki,tij->kj", raw / root[:, None, :], term_onehot, precision=HIGH)
            sums += [doc_part, term_part, jnp.sum(doc_onehot, axis=(0, 1)), jnp.sum(term_onehot, axis=(0, 1))]
        sums = packed_psum(n_doc, n_term, sums)
        gram_matrix, along, energy, volume = sums[:4]
        lower = jnp.linalg.cholesky(gram_matrix - jnp.outer(along, along) / volume, symmetrize_input=False)
        projected = raw - root[:, None, :] * (along / volume)[None, :, None]
        flat = projected.transpose(1, 0, 2).reshape(width_k, -1)
        solved = jax.scipy.linalg.solve_triangular(lower, flat, lower=True)
        basis = solved.reshape(width_k, term_tiles_own, edge).transpose(1, 0, 2)
        weights = (basis / root[:, None, :]).astype(jnp.bfloat16)

    doc_part, term_part, doc_count, term_count = sums[4:]
    scale = jnp.sqrt(volume)
    column_scale = scale * lax.rsqrt(energy)
    doc_embed = summed_own / doc_degree[:, None, :] * column_scale[None, :, None]
    term_embed = scale * basis / root[:, None, :]
    term_centered = term_part - jnp.outer(along / volume, term_count)
    term_sums = scale * jax.scipy.linalg.solve_triangular(lower, term_centered, lower=True)
    centers = (column_scale[:, None] * doc_part + term_sums) / (doc_count + term_count)[None, :]
    center_norm = jnp.sum(centers * centers, axis=0)

    def distances(embed):
        near = jnp.einsum("tki,kj->tij", embed, centers, precision=HIGH)
        norm = jnp.sum(embed * embed, axis=1)
        dist = (norm[:, :, None] - 2.0 * near + center_norm[None, None, :]) / width_k
        return dist.reshape(-1, CLUSTERS)

    return (distances(doc_embed)[None], distances(term_embed)[None])


def solution(mesh):
    placed = (
        P("doc", "term", None, None, None),
        P("doc", "term", None),
        P("doc", "term", None),
        P("doc", "term"),
        P("term", "doc", None),
        P("doc", "term"),
        P("term", "doc"),
    )
    return jax.shard_map(
        functools.partial(per_device, mesh.shape["doc"], mesh.shape["term"]),
        mesh=mesh,
        in_specs=placed,
        out_specs=(P("doc", "term", None), P("term", "doc", None)),
        check_vma=False,
    )
```

```python
import functools

import jax
import jax.numpy as jnp
from jax import lax
from jax.experimental import pallas as pl
from jax.experimental.pallas import tpu as pltpu
from jax.sharding import PartitionSpec as P

CLUSTERS = 64
ITERS = 2
CHUNK = 128
GROUP = 32
DEG_ROWS = 8

HIGH = lax.Precision.HIGHEST
NT_DIMS = (((1,), (1,)), ((), ()))


def tile_kernel(transpose_tile, with_degree, group, split, rows_ref, cols_ref, cnt_ref, tiles_ref, side_ref, out_ref, *rest):
    step = pl.program_id(0)
    chunk = tiles_ref.shape[0]
    width = side_ref.shape[1]

    @pl.when(step == 0)
    def _():
        out_ref[...] = jnp.zeros_like(out_ref)
        for extra in rest:
            extra[...] = jnp.zeros_like(extra)

    count = cnt_ref[0]
    base = step * chunk
    live = jnp.clip(count - base, 0, chunk)

    def product(lhs, tile):
        if transpose_tile:
            return lax.dot_general(lhs, tile, NT_DIMS, preferred_element_type=jnp.float32)
        return jnp.dot(lhs, tile, preferred_element_type=jnp.float32)

    def run(g, masked):
        results = []
        for u in range(group):
            j = g * group + u
            slot = base + j
            if transpose_tile:
                src, dst = cols_ref[slot], rows_ref[slot]
            else:
                src, dst = rows_ref[slot], cols_ref[slot]
            tile = tiles_ref[j]
            lhs = side_ref[src]
            if with_degree:
                lhs = jnp.concatenate([lhs, jnp.ones((DEG_ROWS, lhs.shape[1]), lhs.dtype)], axis=0)
            prod = product(lhs, tile)
            if masked:
                prod = jnp.where(slot < count, prod, 0.0)
            results.append((dst, prod))
        for dst, prod in results:
            if split is None:
                out_ref[dst] += prod
            else:
                head = prod[:split]
                if with_degree:
                    head = jnp.concatenate([head, prod[width:]], axis=0)
                out_ref[dst] += head
                rest[0][dst] += prod[split:width]

    def body(g, carry):
        run(g, False)
        return carry

    full = live // group
    lax.fori_loop(0, full, body, 0)

    @pl.when(full * group < live)
    def _():
        run(full, True)


def tile_pass(tiles, rows, cols, count, side, transpose_tile, with_degree, split=None):
    slots, edge, _ = tiles.shape
    n_tiles, width, _ = side.shape
    chunk = min(CHUNK, slots)
    steps = slots // chunk
    out_rows = width + (DEG_ROWS if with_degree else 0)
    kernel = functools.partial(tile_kernel, transpose_tile, with_degree, GROUP, split)
    if split is None:
        shapes = [(n_tiles, out_rows, edge)]
    else:
        shapes = [(n_tiles, out_rows - width + split, edge), (n_tiles, width - split, edge)]

    def tile_map(i, rows_ref, cols_ref, cnt_ref):
        return (jnp.minimum(i, jnp.maximum(cnt_ref[0] - 1, 0) // chunk), 0, 0)

    def whole_map(i, rows_ref, cols_ref, cnt_ref):
        return (0, 0, 0)

    flops = 2 * slots * edge * edge * out_rows
    cost = pl.CostEstimate(
        flops=flops,
        transcendentals=0,
        bytes_accessed=tiles.size * 2 + side.size * 2 + n_tiles * out_rows * edge * 4,
    )
    outs = pl.pallas_call(
        kernel,
        out_shape=[jax.ShapeDtypeStruct(shape, jnp.float32) for shape in shapes],
        grid_spec=pltpu.PrefetchScalarGridSpec(
            num_scalar_prefetch=3,
            grid=(steps,),
            in_specs=[
                pl.BlockSpec((chunk, edge, edge), tile_map),
                pl.BlockSpec((n_tiles, width, edge), whole_map),
            ],
            out_specs=[pl.BlockSpec(shape, whole_map) for shape in shapes],
        ),
        compiler_params=pltpu.CompilerParams(dimension_semantics=("arbitrary",)),
        cost_estimate=cost,
    )(rows, cols, count, tiles, side)
    return outs[0] if split is None else outs


def scatter_sum(x, axis_name, parts):
    pieces = x.reshape((parts, x.shape[0] // parts) + x.shape[1:])
    return jnp.sum(lax.all_to_all(pieces, axis_name, 0, 0, tiled=False), axis=0)


def exchange_sum(flat, axis_name, parts):
    copies = jnp.broadcast_to(flat, (parts,) + flat.shape)
    return jnp.sum(lax.all_to_all(copies, axis_name, 0, 0, tiled=False), axis=0)


def exchange_gather(x, axis_name, parts):
    copies = jnp.broadcast_to(x, (parts,) + x.shape)
    got = lax.all_to_all(copies, axis_name, 0, 0, tiled=False)
    return got.reshape((parts * x.shape[0],) + x.shape[1:])


def packed_psum(n_doc, n_term, values):
    flat = jnp.concatenate([jnp.reshape(v, (-1,)) for v in values])
    flat = exchange_sum(exchange_sum(flat, "term", n_term), "doc", n_doc)
    out, start = [], 0
    for v in values:
        size = int(jnp.size(v))
        out.append(flat[start : start + size].reshape(jnp.shape(v)))
        start += size
    return out


def per_device(n_doc, n_term, tiles, tile_rows, tile_cols, tile_count, start_block, doc_cluster, term_cluster):
    local_tiles = tiles[0, 0]
    rows = tile_rows[0, 0]
    cols = tile_cols[0, 0]
    count = tile_count[0, 0].reshape(1)
    edge = local_tiles.shape[1]
    start_rows = start_block[0]
    width_k = start_rows.shape[1]
    term_tiles_own = start_rows.shape[0] // edge
    start_t = start_rows.reshape(term_tiles_own, edge, width_k).transpose(0, 2, 1)
    doc_labels = doc_cluster[0].reshape(-1, edge)
    term_labels = term_cluster[0].reshape(-1, edge)
    clusters = jnp.arange(CLUSTERS, dtype=jnp.int32)
    doc_onehot = (doc_labels[:, :, None] == clusters).astype(jnp.float32)
    term_onehot = (term_labels[:, :, None] == clusters).astype(jnp.float32)

    weights = start_t
    basis = None
    doc_degree = None
    term_degree = None
    root = None
    summed_own = None
    energy = None
    volume = None
    for step in range(ITERS):
        first = step == 0
        w_all = exchange_gather(weights, "doc", n_doc)
        half = width_k // 2
        left_a, left_b = tile_pass(local_tiles, rows, cols, count, w_all, True, first, half)
        own_a = lax.psum_scatter(left_a, "term", scatter_dimension=0, tiled=True)
        if first:
            doc_degree = own_a[:, half, :]
        summed_a = own_a[:, :half, :]
        qa_all = lax.all_gather((summed_a / doc_degree[:, None, :]).astype(jnp.bfloat16), "term", axis=0, tiled=True)
        left_b, _ = lax.optimization_barrier((left_b, qa_all))
        summed_b = lax.psum_scatter(left_b, "term", scatter_dimension=0, tiled=True)
        qb_all = lax.all_gather((summed_b / doc_degree[:, None, :]).astype(jnp.bfloat16), "term", axis=0, tiled=True)
        summed_own = jnp.concatenate([summed_a, summed_b], axis=1)
        right_a = scatter_sum(tile_pass(local_tiles, rows, cols, count, qa_all, False, first), "doc", n_doc)
        right_b = scatter_sum(tile_pass(local_tiles, rows, cols, count, qb_all, False, False), "doc", n_doc)
        if first:
            term_degree = right_a[:, half, :]
            root = jnp.sqrt(term_degree)
        right_own = jnp.concatenate([right_a[:, :half, :], right_b], axis=1)
        raw = right_own[:, :width_k, :] / root[:, None, :]
        previous = root[:, None, :] * start_t.astype(jnp.float32) if first else basis
        gram_part = jnp.einsum("tki,tli->kl", raw, raw, precision=HIGH)
        along_part = jnp.einsum("tki,ti->k", raw, root, precision=HIGH)
        energy_part = jnp.sum(previous * raw, axis=(0, 2))
        volume_part = jnp.sum(term_degree)
        sums = [gram_part, along_part, energy_part, volume_part]
        if step == ITERS - 1:
            doc_ratio = summed_own / doc_degree[:, None, :]
            doc_part = jnp.einsum("tki,tij->kj", doc_ratio, doc_onehot, precision=HIGH)
            term_part = jnp.einsum("tki,tij->kj", raw / root[:, None, :], term_onehot, precision=HIGH)
            sums += [doc_part, term_part, jnp.sum(doc_onehot, axis=(0, 1)), jnp.sum(term_onehot, axis=(0, 1))]
        sums = packed_psum(n_doc, n_term, sums)
        gram_matrix, along, energy, volume = sums[:4]
        lower = jnp.linalg.cholesky(gram_matrix - jnp.outer(along, along) / volume, symmetrize_input=False)
        projected = raw - root[:, None, :] * (along / volume)[None, :, None]
        flat = projected.transpose(1, 0, 2).reshape(width_k, -1)
        solved = jax.scipy.linalg.solve_triangular(lower, flat, lower=True)
        basis = solved.reshape(width_k, term_tiles_own, edge).transpose(1, 0, 2)
        weights = (basis / root[:, None, :]).astype(jnp.bfloat16)

    doc_part, term_part, doc_count, term_count = sums[4:]
    scale = jnp.sqrt(volume)
    column_scale = scale * lax.rsqrt(energy)
    doc_embed = summed_own / doc_degree[:, None, :] * column_scale[None, :, None]
    term_embed = scale * basis / root[:, None, :]
    term_centered = term_part - jnp.outer(along / volume, term_count)
    term_sums = scale * jax.scipy.linalg.solve_triangular(lower, term_centered, lower=True)
    centers = (column_scale[:, None] * doc_part + term_sums) / (doc_count + term_count)[None, :]
    center_norm = jnp.sum(centers * centers, axis=0)

    def distances(embed):
        near = jnp.einsum("tki,kj->tij", embed, centers, precision=HIGH)
        norm = jnp.sum(embed * embed, axis=1)
        dist = (norm[:, :, None] - 2.0 * near + center_norm[None, None, :]) / width_k
        return dist.reshape(-1, CLUSTERS)

    return (distances(doc_embed)[None], distances(term_embed)[None])


def solution(mesh):
    placed = (
        P("doc", "term", None, None, None),
        P("doc", "term", None),
        P("doc", "term", None),
        P("doc", "term"),
        P("term", "doc", None),
        P("doc", "term"),
        P("term", "doc"),
    )
    return jax.shard_map(
        functools.partial(per_device, mesh.shape["doc"], mesh.shape["term"]),
        mesh=mesh,
        in_specs=placed,
        out_specs=(P("doc", "term", None), P("term", "doc", None)),
        check_vma=False,
    )
```

```python
import functools

import jax
import jax.numpy as jnp
from jax import lax
from jax.experimental import pallas as pl
from jax.experimental.pallas import tpu as pltpu
from jax.sharding import PartitionSpec as P

CLUSTERS = 64
ITERS = 2
CHUNK = 128
GROUP = 64
DEG_ROWS = 8

HIGH = lax.Precision.HIGHEST
NT_DIMS = (((1,), (1,)), ((), ()))


def tile_kernel(transpose_tile, with_degree, group, split, rows_ref, cols_ref, cnt_ref, tiles_ref, side_ref, out_ref, *rest):
    step = pl.program_id(0)
    chunk = tiles_ref.shape[0]
    width = side_ref.shape[1]

    @pl.when(step == 0)
    def _():
        out_ref[...] = jnp.zeros_like(out_ref)
        for extra in rest:
            extra[...] = jnp.zeros_like(extra)

    count = cnt_ref[0]
    base = step * chunk
    live = jnp.clip(count - base, 0, chunk)

    def product(lhs, tile):
        if transpose_tile:
            return lax.dot_general(lhs, tile, NT_DIMS, preferred_element_type=jnp.float32)
        return jnp.dot(lhs, tile, preferred_element_type=jnp.float32)

    def run(g, masked):
        results = []
        for u in range(group):
            j = g * group + u
            slot = base + j
            if transpose_tile:
                src, dst = cols_ref[slot], rows_ref[slot]
            else:
                src, dst = rows_ref[slot], cols_ref[slot]
            tile = tiles_ref[j]
            lhs = side_ref[src]
            if with_degree:
                lhs = jnp.concatenate([lhs, jnp.ones((DEG_ROWS, lhs.shape[1]), lhs.dtype)], axis=0)
            prod = product(lhs, tile)
            if masked:
                prod = jnp.where(slot < count, prod, 0.0)
            results.append((dst, prod))
        for dst, prod in results:
            if split is None:
                out_ref[dst] += prod
            else:
                head = prod[:split]
                if with_degree:
                    head = jnp.concatenate([head, prod[width:]], axis=0)
                out_ref[dst] += head
                rest[0][dst] += prod[split:width]

    def body(g, carry):
        run(g, False)
        return carry

    full = live // group
    lax.fori_loop(0, full, body, 0)

    @pl.when(full * group < live)
    def _():
        run(full, True)


def tile_pass(tiles, rows, cols, count, side, transpose_tile, with_degree, split=None):
    slots, edge, _ = tiles.shape
    n_tiles, width, _ = side.shape
    chunk = min(CHUNK, slots)
    steps = slots // chunk
    out_rows = width + (DEG_ROWS if with_degree else 0)
    kernel = functools.partial(tile_kernel, transpose_tile, with_degree, GROUP, split)
    if split is None:
        shapes = [(n_tiles, out_rows, edge)]
    else:
        shapes = [(n_tiles, out_rows - width + split, edge), (n_tiles, width - split, edge)]

    def tile_map(i, rows_ref, cols_ref, cnt_ref):
        return (jnp.minimum(i, jnp.maximum(cnt_ref[0] - 1, 0) // chunk), 0, 0)

    def whole_map(i, rows_ref, cols_ref, cnt_ref):
        return (0, 0, 0)

    flops = 2 * slots * edge * edge * out_rows
    cost = pl.CostEstimate(
        flops=flops,
        transcendentals=0,
        bytes_accessed=tiles.size * 2 + side.size * 2 + n_tiles * out_rows * edge * 4,
    )
    outs = pl.pallas_call(
        kernel,
        out_shape=[jax.ShapeDtypeStruct(shape, jnp.float32) for shape in shapes],
        grid_spec=pltpu.PrefetchScalarGridSpec(
            num_scalar_prefetch=3,
            grid=(steps,),
            in_specs=[
                pl.BlockSpec((chunk, edge, edge), tile_map),
                pl.BlockSpec((n_tiles, width, edge), whole_map),
            ],
            out_specs=[pl.BlockSpec(shape, whole_map) for shape in shapes],
        ),
        compiler_params=pltpu.CompilerParams(dimension_semantics=("arbitrary",)),
        cost_estimate=cost,
    )(rows, cols, count, tiles, side)
    return outs[0] if split is None else outs


def scatter_sum(x, axis_name, parts):
    pieces = x.reshape((parts, x.shape[0] // parts) + x.shape[1:])
    return jnp.sum(lax.all_to_all(pieces, axis_name, 0, 0, tiled=False), axis=0)


def exchange_sum(flat, axis_name, parts):
    copies = jnp.broadcast_to(flat, (parts,) + flat.shape)
    return jnp.sum(lax.all_to_all(copies, axis_name, 0, 0, tiled=False), axis=0)


def exchange_gather(x, axis_name, parts):
    copies = jnp.broadcast_to(x, (parts,) + x.shape)
    got = lax.all_to_all(copies, axis_name, 0, 0, tiled=False)
    return got.reshape((parts * x.shape[0],) + x.shape[1:])


def packed_psum(n_doc, n_term, values):
    flat = jnp.concatenate([jnp.reshape(v, (-1,)) for v in values])
    flat = exchange_sum(exchange_sum(flat, "term", n_term), "doc", n_doc)
    out, start = [], 0
    for v in values:
        size = int(jnp.size(v))
        out.append(flat[start : start + size].reshape(jnp.shape(v)))
        start += size
    return out


def per_device(n_doc, n_term, tiles, tile_rows, tile_cols, tile_count, start_block, doc_cluster, term_cluster):
    local_tiles = tiles[0, 0]
    rows = tile_rows[0, 0]
    cols = tile_cols[0, 0]
    count = tile_count[0, 0].reshape(1)
    edge = local_tiles.shape[1]
    start_rows = start_block[0]
    width_k = start_rows.shape[1]
    term_tiles_own = start_rows.shape[0] // edge
    start_t = start_rows.reshape(term_tiles_own, edge, width_k).transpose(0, 2, 1)
    doc_labels = doc_cluster[0].reshape(-1, edge)
    term_labels = term_cluster[0].reshape(-1, edge)
    clusters = jnp.arange(CLUSTERS, dtype=jnp.int32)
    doc_onehot = (doc_labels[:, :, None] == clusters).astype(jnp.float32)
    term_onehot = (term_labels[:, :, None] == clusters).astype(jnp.float32)

    weights = start_t
    basis = None
    doc_degree = None
    term_degree = None
    root = None
    summed_own = None
    energy = None
    volume = None
    for step in range(ITERS):
        first = step == 0
        w_all = exchange_gather(weights, "doc", n_doc)
        half = width_k // 2
        left_a, left_b = tile_pass(local_tiles, rows, cols, count, w_all, True, first, half)
        own_a = lax.psum_scatter(left_a, "term", scatter_dimension=0, tiled=True)
        if first:
            doc_degree = own_a[:, half, :]
        summed_a = own_a[:, :half, :]
        qa_all = lax.all_gather((summed_a / doc_degree[:, None, :]).astype(jnp.bfloat16), "term", axis=0, tiled=True)
        left_b, _ = lax.optimization_barrier((left_b, qa_all))
        summed_b = lax.psum_scatter(left_b, "term", scatter_dimension=0, tiled=True)
        qb_all = lax.all_gather((summed_b / doc_degree[:, None, :]).astype(jnp.bfloat16), "term", axis=0, tiled=True)
        summed_own = jnp.concatenate([summed_a, summed_b], axis=1)
        right_a = scatter_sum(tile_pass(local_tiles, rows, cols, count, qa_all, False, first), "doc", n_doc)
        right_b = scatter_sum(tile_pass(local_tiles, rows, cols, count, qb_all, False, False), "doc", n_doc)
        if first:
            term_degree = right_a[:, half, :]
            root = jnp.sqrt(term_degree)
        right_own = jnp.concatenate([right_a[:, :half, :], right_b], axis=1)
        raw = right_own[:, :width_k, :] / root[:, None, :]
        previous = root[:, None, :] * start_t.astype(jnp.float32) if first else basis
        gram_part = jnp.einsum("tki,tli->kl", raw, raw, precision=HIGH)
        along_part = jnp.einsum("tki,ti->k", raw, root, precision=HIGH)
        energy_part = jnp.sum(previous * raw, axis=(0, 2))
        volume_part = jnp.sum(term_degree)
        sums = [gram_part, along_part, energy_part, volume_part]
        if step == ITERS - 1:
            doc_ratio = summed_own / doc_degree[:, None, :]
            doc_part = jnp.einsum("tki,tij->kj", doc_ratio, doc_onehot, precision=HIGH)
            term_part = jnp.einsum("tki,tij->kj", raw / root[:, None, :], term_onehot, precision=HIGH)
            sums += [doc_part, term_part, jnp.sum(doc_onehot, axis=(0, 1)), jnp.sum(term_onehot, axis=(0, 1))]
        sums = packed_psum(n_doc, n_term, sums)
        gram_matrix, along, energy, volume = sums[:4]
        lower = jnp.linalg.cholesky(gram_matrix - jnp.outer(along, along) / volume, symmetrize_input=False)
        projected = raw - root[:, None, :] * (along / volume)[None, :, None]
        flat = projected.transpose(1, 0, 2).reshape(width_k, -1)
        solved = jax.scipy.linalg.solve_triangular(lower, flat, lower=True)
        basis = solved.reshape(width_k, term_tiles_own, edge).transpose(1, 0, 2)
        weights = (basis / root[:, None, :]).astype(jnp.bfloat16)

    doc_part, term_part, doc_count, term_count = sums[4:]
    scale = jnp.sqrt(volume)
    column_scale = scale * lax.rsqrt(energy)
    doc_embed = summed_own / doc_degree[:, None, :] * column_scale[None, :, None]
    term_embed = scale * basis / root[:, None, :]
    term_centered = term_part - jnp.outer(along / volume, term_count)
    term_sums = scale * jax.scipy.linalg.solve_triangular(lower, term_centered, lower=True)
    centers = (column_scale[:, None] * doc_part + term_sums) / (doc_count + term_count)[None, :]
    center_norm = jnp.sum(centers * centers, axis=0)

    def distances(embed):
        near = jnp.einsum("tki,kj->tij", embed, centers, precision=HIGH)
        norm = jnp.sum(embed * embed, axis=1)
        dist = (norm[:, :, None] - 2.0 * near + center_norm[None, None, :]) / width_k
        return dist.reshape(-1, CLUSTERS)

    return (distances(doc_embed)[None], distances(term_embed)[None])


def solution(mesh):
    placed = (
        P("doc", "term", None, None, None),
        P("doc", "term", None),
        P("doc", "term", None),
        P("doc", "term"),
        P("term", "doc", None),
        P("doc", "term"),
        P("term", "doc"),
    )
    return jax.shard_map(
        functools.partial(per_device, mesh.shape["doc"], mesh.shape["term"]),
        mesh=mesh,
        in_specs=placed,
        out_specs=(P("doc", "term", None), P("term", "doc", None)),
        check_vma=False,
    )
```

```python
import functools

import jax
import jax.numpy as jnp
from jax import lax
from jax.experimental import pallas as pl
from jax.experimental.pallas import tpu as pltpu
from jax.sharding import PartitionSpec as P

CLUSTERS = 64
ITERS = 2
CHUNK = 256
GROUP = 64
DEG_ROWS = 8

HIGH = lax.Precision.HIGHEST
NT_DIMS = (((1,), (1,)), ((), ()))


def tile_kernel(transpose_tile, with_degree, group, split, rows_ref, cols_ref, cnt_ref, tiles_ref, side_ref, out_ref, *rest):
    step = pl.program_id(0)
    chunk = tiles_ref.shape[0]
    width = side_ref.shape[1]

    @pl.when(step == 0)
    def _():
        out_ref[...] = jnp.zeros_like(out_ref)
        for extra in rest:
            extra[...] = jnp.zeros_like(extra)

    count = cnt_ref[0]
    base = step * chunk
    live = jnp.clip(count - base, 0, chunk)

    def product(lhs, tile):
        if transpose_tile:
            return lax.dot_general(lhs, tile, NT_DIMS, preferred_element_type=jnp.float32)
        return jnp.dot(lhs, tile, preferred_element_type=jnp.float32)

    def run(g, masked):
        results = []
        for u in range(group):
            j = g * group + u
            slot = base + j
            if transpose_tile:
                src, dst = cols_ref[slot], rows_ref[slot]
            else:
                src, dst = rows_ref[slot], cols_ref[slot]
            tile = tiles_ref[j]
            lhs = side_ref[src]
            if with_degree:
                lhs = jnp.concatenate([lhs, jnp.ones((DEG_ROWS, lhs.shape[1]), lhs.dtype)], axis=0)
            prod = product(lhs, tile)
            if masked:
                prod = jnp.where(slot < count, prod, 0.0)
            results.append((dst, prod))
        for dst, prod in results:
            if split is None:
                out_ref[dst] += prod
            else:
                head = prod[:split]
                if with_degree:
                    head = jnp.concatenate([head, prod[width:]], axis=0)
                out_ref[dst] += head
                rest[0][dst] += prod[split:width]

    def body(g, carry):
        run(g, False)
        return carry

    full = live // group
    lax.fori_loop(0, full, body, 0)

    @pl.when(full * group < live)
    def _():
        run(full, True)


def tile_pass(tiles, rows, cols, count, side, transpose_tile, with_degree, split=None):
    slots, edge, _ = tiles.shape
    n_tiles, width, _ = side.shape
    chunk = min(CHUNK, slots)
    steps = slots // chunk
    out_rows = width + (DEG_ROWS if with_degree else 0)
    kernel = functools.partial(tile_kernel, transpose_tile, with_degree, GROUP, split)
    if split is None:
        shapes = [(n_tiles, out_rows, edge)]
    else:
        shapes = [(n_tiles, out_rows - width + split, edge), (n_tiles, width - split, edge)]

    def tile_map(i, rows_ref, cols_ref, cnt_ref):
        return (jnp.minimum(i, jnp.maximum(cnt_ref[0] - 1, 0) // chunk), 0, 0)

    def whole_map(i, rows_ref, cols_ref, cnt_ref):
        return (0, 0, 0)

    flops = 2 * slots * edge * edge * out_rows
    cost = pl.CostEstimate(
        flops=flops,
        transcendentals=0,
        bytes_accessed=tiles.size * 2 + side.size * 2 + n_tiles * out_rows * edge * 4,
    )
    outs = pl.pallas_call(
        kernel,
        out_shape=[jax.ShapeDtypeStruct(shape, jnp.float32) for shape in shapes],
        grid_spec=pltpu.PrefetchScalarGridSpec(
            num_scalar_prefetch=3,
            grid=(steps,),
            in_specs=[
                pl.BlockSpec((chunk, edge, edge), tile_map),
                pl.BlockSpec((n_tiles, width, edge), whole_map),
            ],
            out_specs=[pl.BlockSpec(shape, whole_map) for shape in shapes],
        ),
        compiler_params=pltpu.CompilerParams(dimension_semantics=("arbitrary",)),
        cost_estimate=cost,
    )(rows, cols, count, tiles, side)
    return outs[0] if split is None else outs


def scatter_sum(x, axis_name, parts):
    pieces = x.reshape((parts, x.shape[0] // parts) + x.shape[1:])
    return jnp.sum(lax.all_to_all(pieces, axis_name, 0, 0, tiled=False), axis=0)


def exchange_sum(flat, axis_name, parts):
    copies = jnp.broadcast_to(flat, (parts,) + flat.shape)
    return jnp.sum(lax.all_to_all(copies, axis_name, 0, 0, tiled=False), axis=0)


def exchange_gather(x, axis_name, parts):
    copies = jnp.broadcast_to(x, (parts,) + x.shape)
    got = lax.all_to_all(copies, axis_name, 0, 0, tiled=False)
    return got.reshape((parts * x.shape[0],) + x.shape[1:])


def packed_psum(n_doc, n_term, values):
    flat = jnp.concatenate([jnp.reshape(v, (-1,)) for v in values])
    flat = exchange_sum(exchange_sum(flat, "term", n_term), "doc", n_doc)
    out, start = [], 0
    for v in values:
        size = int(jnp.size(v))
        out.append(flat[start : start + size].reshape(jnp.shape(v)))
        start += size
    return out


def per_device(n_doc, n_term, tiles, tile_rows, tile_cols, tile_count, start_block, doc_cluster, term_cluster):
    local_tiles = tiles[0, 0]
    rows = tile_rows[0, 0]
    cols = tile_cols[0, 0]
    count = tile_count[0, 0].reshape(1)
    edge = local_tiles.shape[1]
    start_rows = start_block[0]
    width_k = start_rows.shape[1]
    term_tiles_own = start_rows.shape[0] // edge
    start_t = start_rows.reshape(term_tiles_own, edge, width_k).transpose(0, 2, 1)
    doc_labels = doc_cluster[0].reshape(-1, edge)
    term_labels = term_cluster[0].reshape(-1, edge)
    clusters = jnp.arange(CLUSTERS, dtype=jnp.int32)
    doc_onehot = (doc_labels[:, :, None] == clusters).astype(jnp.float32)
    term_onehot = (term_labels[:, :, None] == clusters).astype(jnp.float32)

    weights = start_t
    basis = None
    doc_degree = None
    term_degree = None
    root = None
    summed_own = None
    energy = None
    volume = None
    for step in range(ITERS):
        first = step == 0
        w_all = exchange_gather(weights, "doc", n_doc)
        half = width_k // 2
        left_a, left_b = tile_pass(local_tiles, rows, cols, count, w_all, True, first, half)
        own_a = lax.psum_scatter(left_a, "term", scatter_dimension=0, tiled=True)
        if first:
            doc_degree = own_a[:, half, :]
        summed_a = own_a[:, :half, :]
        qa_all = lax.all_gather((summed_a / doc_degree[:, None, :]).astype(jnp.bfloat16), "term", axis=0, tiled=True)
        left_b, _ = lax.optimization_barrier((left_b, qa_all))
        summed_b = lax.psum_scatter(left_b, "term", scatter_dimension=0, tiled=True)
        qb_all = lax.all_gather((summed_b / doc_degree[:, None, :]).astype(jnp.bfloat16), "term", axis=0, tiled=True)
        summed_own = jnp.concatenate([summed_a, summed_b], axis=1)
        right_a = scatter_sum(tile_pass(local_tiles, rows, cols, count, qa_all, False, first), "doc", n_doc)
        right_b = scatter_sum(tile_pass(local_tiles, rows, cols, count, qb_all, False, False), "doc", n_doc)
        if first:
            term_degree = right_a[:, half, :]
            root = jnp.sqrt(term_degree)
        right_own = jnp.concatenate([right_a[:, :half, :], right_b], axis=1)
        raw = right_own[:, :width_k, :] / root[:, None, :]
        previous = root[:, None, :] * start_t.astype(jnp.float32) if first else basis
        gram_part = jnp.einsum("tki,tli->kl", raw, raw, precision=HIGH)
        along_part = jnp.einsum("tki,ti->k", raw, root, precision=HIGH)
        energy_part = jnp.sum(previous * raw, axis=(0, 2))
        volume_part = jnp.sum(term_degree)
        sums = [gram_part, along_part, energy_part, volume_part]
        if step == ITERS - 1:
            doc_ratio = summed_own / doc_degree[:, None, :]
            doc_part = jnp.einsum("tki,tij->kj", doc_ratio, doc_onehot, precision=HIGH)
            term_part = jnp.einsum("tki,tij->kj", raw / root[:, None, :], term_onehot, precision=HIGH)
            sums += [doc_part, term_part, jnp.sum(doc_onehot, axis=(0, 1)), jnp.sum(term_onehot, axis=(0, 1))]
        sums = packed_psum(n_doc, n_term, sums)
        gram_matrix, along, energy, volume = sums[:4]
        lower = jnp.linalg.cholesky(gram_matrix - jnp.outer(along, along) / volume, symmetrize_input=False)
        projected = raw - root[:, None, :] * (along / volume)[None, :, None]
        flat = projected.transpose(1, 0, 2).reshape(width_k, -1)
        solved = jax.scipy.linalg.solve_triangular(lower, flat, lower=True)
        basis = solved.reshape(width_k, term_tiles_own, edge).transpose(1, 0, 2)
        weights = (basis / root[:, None, :]).astype(jnp.bfloat16)

    doc_part, term_part, doc_count, term_count = sums[4:]
    scale = jnp.sqrt(volume)
    column_scale = scale * lax.rsqrt(energy)
    doc_embed = summed_own / doc_degree[:, None, :] * column_scale[None, :, None]
    term_embed = scale * basis / root[:, None, :]
    term_centered = term_part - jnp.outer(along / volume, term_count)
    term_sums = scale * jax.scipy.linalg.solve_triangular(lower, term_centered, lower=True)
    centers = (column_scale[:, None] * doc_part + term_sums) / (doc_count + term_count)[None, :]
    center_norm = jnp.sum(centers * centers, axis=0)

    def distances(embed):
        near = jnp.einsum("tki,kj->tij", embed, centers, precision=HIGH)
        norm = jnp.sum(embed * embed, axis=1)
        dist = (norm[:, :, None] - 2.0 * near + center_norm[None, None, :]) / width_k
        return dist.reshape(-1, CLUSTERS)

    return (distances(doc_embed)[None], distances(term_embed)[None])


def solution(mesh):
    placed = (
        P("doc", "term", None, None, None),
        P("doc", "term", None),
        P("doc", "term", None),
        P("doc", "term"),
        P("term", "doc", None),
        P("doc", "term"),
        P("term", "doc"),
    )
    return jax.shard_map(
        functools.partial(per_device, mesh.shape["doc"], mesh.shape["term"]),
        mesh=mesh,
        in_specs=placed,
        out_specs=(P("doc", "term", None), P("term", "doc", None)),
        check_vma=False,
    )
```

```python
import functools

import jax
import jax.numpy as jnp
from jax import lax
from jax.experimental import pallas as pl
from jax.experimental.pallas import tpu as pltpu
from jax.sharding import PartitionSpec as P

CLUSTERS = 64
ITERS = 2
CHUNK = 512
GROUP = 64
DEG_ROWS = 8

HIGH = lax.Precision.HIGHEST
NT_DIMS = (((1,), (1,)), ((), ()))


def tile_kernel(transpose_tile, with_degree, group, split, rows_ref, cols_ref, cnt_ref, tiles_ref, side_ref, out_ref, *rest):
    step = pl.program_id(0)
    chunk = tiles_ref.shape[0]
    width = side_ref.shape[1]

    @pl.when(step == 0)
    def _():
        out_ref[...] = jnp.zeros_like(out_ref)
        for extra in rest:
            extra[...] = jnp.zeros_like(extra)

    count = cnt_ref[0]
    base = step * chunk
    live = jnp.clip(count - base, 0, chunk)

    def product(lhs, tile):
        if transpose_tile:
            return lax.dot_general(lhs, tile, NT_DIMS, preferred_element_type=jnp.float32)
        return jnp.dot(lhs, tile, preferred_element_type=jnp.float32)

    def run(g, masked):
        results = []
        for u in range(group):
            j = g * group + u
            slot = base + j
            if transpose_tile:
                src, dst = cols_ref[slot], rows_ref[slot]
            else:
                src, dst = rows_ref[slot], cols_ref[slot]
            tile = tiles_ref[j]
            lhs = side_ref[src]
            if with_degree:
                lhs = jnp.concatenate([lhs, jnp.ones((DEG_ROWS, lhs.shape[1]), lhs.dtype)], axis=0)
            prod = product(lhs, tile)
            if masked:
                prod = jnp.where(slot < count, prod, 0.0)
            results.append((dst, prod))
        for dst, prod in results:
            if split is None:
                out_ref[dst] += prod
            else:
                head = prod[:split]
                if with_degree:
                    head = jnp.concatenate([head, prod[width:]], axis=0)
                out_ref[dst] += head
                rest[0][dst] += prod[split:width]

    def body(g, carry):
        run(g, False)
        return carry

    full = live // group
    lax.fori_loop(0, full, body, 0)

    @pl.when(full * group < live)
    def _():
        run(full, True)


def tile_pass(tiles, rows, cols, count, side, transpose_tile, with_degree, split=None):
    slots, edge, _ = tiles.shape
    n_tiles, width, _ = side.shape
    chunk = min(CHUNK, slots)
    steps = slots // chunk
    out_rows = width + (DEG_ROWS if with_degree else 0)
    kernel = functools.partial(tile_kernel, transpose_tile, with_degree, GROUP, split)
    if split is None:
        shapes = [(n_tiles, out_rows, edge)]
    else:
        shapes = [(n_tiles, out_rows - width + split, edge), (n_tiles, width - split, edge)]

    def tile_map(i, rows_ref, cols_ref, cnt_ref):
        return (jnp.minimum(i, jnp.maximum(cnt_ref[0] - 1, 0) // chunk), 0, 0)

    def whole_map(i, rows_ref, cols_ref, cnt_ref):
        return (0, 0, 0)

    flops = 2 * slots * edge * edge * out_rows
    cost = pl.CostEstimate(
        flops=flops,
        transcendentals=0,
        bytes_accessed=tiles.size * 2 + side.size * 2 + n_tiles * out_rows * edge * 4,
    )
    outs = pl.pallas_call(
        kernel,
        out_shape=[jax.ShapeDtypeStruct(shape, jnp.float32) for shape in shapes],
        grid_spec=pltpu.PrefetchScalarGridSpec(
            num_scalar_prefetch=3,
            grid=(steps,),
            in_specs=[
                pl.BlockSpec((chunk, edge, edge), tile_map),
                pl.BlockSpec((n_tiles, width, edge), whole_map),
            ],
            out_specs=[pl.BlockSpec(shape, whole_map) for shape in shapes],
        ),
        compiler_params=pltpu.CompilerParams(dimension_semantics=("arbitrary",)),
        cost_estimate=cost,
    )(rows, cols, count, tiles, side)
    return outs[0] if split is None else outs


def scatter_sum(x, axis_name, parts):
    pieces = x.reshape((parts, x.shape[0] // parts) + x.shape[1:])
    return jnp.sum(lax.all_to_all(pieces, axis_name, 0, 0, tiled=False), axis=0)


def exchange_sum(flat, axis_name, parts):
    copies = jnp.broadcast_to(flat, (parts,) + flat.shape)
    return jnp.sum(lax.all_to_all(copies, axis_name, 0, 0, tiled=False), axis=0)


def exchange_gather(x, axis_name, parts):
    copies = jnp.broadcast_to(x, (parts,) + x.shape)
    got = lax.all_to_all(copies, axis_name, 0, 0, tiled=False)
    return got.reshape((parts * x.shape[0],) + x.shape[1:])


def packed_psum(n_doc, n_term, values):
    flat = jnp.concatenate([jnp.reshape(v, (-1,)) for v in values])
    flat = exchange_sum(exchange_sum(flat, "term", n_term), "doc", n_doc)
    out, start = [], 0
    for v in values:
        size = int(jnp.size(v))
        out.append(flat[start : start + size].reshape(jnp.shape(v)))
        start += size
    return out


def per_device(n_doc, n_term, tiles, tile_rows, tile_cols, tile_count, start_block, doc_cluster, term_cluster):
    local_tiles = tiles[0, 0]
    rows = tile_rows[0, 0]
    cols = tile_cols[0, 0]
    count = tile_count[0, 0].reshape(1)
    edge = local_tiles.shape[1]
    start_rows = start_block[0]
    width_k = start_rows.shape[1]
    term_tiles_own = start_rows.shape[0] // edge
    start_t = start_rows.reshape(term_tiles_own, edge, width_k).transpose(0, 2, 1)
    doc_labels = doc_cluster[0].reshape(-1, edge)
    term_labels = term_cluster[0].reshape(-1, edge)
    clusters = jnp.arange(CLUSTERS, dtype=jnp.int32)
    doc_onehot = (doc_labels[:, :, None] == clusters).astype(jnp.float32)
    term_onehot = (term_labels[:, :, None] == clusters).astype(jnp.float32)

    weights = start_t
    basis = None
    doc_degree = None
    term_degree = None
    root = None
    summed_own = None
    energy = None
    volume = None
    for step in range(ITERS):
        first = step == 0
        w_all = exchange_gather(weights, "doc", n_doc)
        half = width_k // 2
        left_a, left_b = tile_pass(local_tiles, rows, cols, count, w_all, True, first, half)
        own_a = lax.psum_scatter(left_a, "term", scatter_dimension=0, tiled=True)
        if first:
            doc_degree = own_a[:, half, :]
        summed_a = own_a[:, :half, :]
        qa_all = lax.all_gather((summed_a / doc_degree[:, None, :]).astype(jnp.bfloat16), "term", axis=0, tiled=True)
        left_b, _ = lax.optimization_barrier((left_b, qa_all))
        summed_b = lax.psum_scatter(left_b, "term", scatter_dimension=0, tiled=True)
        qb_all = lax.all_gather((summed_b / doc_degree[:, None, :]).astype(jnp.bfloat16), "term", axis=0, tiled=True)
        summed_own = jnp.concatenate([summed_a, summed_b], axis=1)
        right_a = scatter_sum(tile_pass(local_tiles, rows, cols, count, qa_all, False, first), "doc", n_doc)
        right_b = scatter_sum(tile_pass(local_tiles, rows, cols, count, qb_all, False, False), "doc", n_doc)
        if first:
            term_degree = right_a[:, half, :]
            root = jnp.sqrt(term_degree)
        right_own = jnp.concatenate([right_a[:, :half, :], right_b], axis=1)
        raw = right_own[:, :width_k, :] / root[:, None, :]
        previous = root[:, None, :] * start_t.astype(jnp.float32) if first else basis
        gram_part = jnp.einsum("tki,tli->kl", raw, raw, precision=HIGH)
        along_part = jnp.einsum("tki,ti->k", raw, root, precision=HIGH)
        energy_part = jnp.sum(previous * raw, axis=(0, 2))
        volume_part = jnp.sum(term_degree)
        sums = [gram_part, along_part, energy_part, volume_part]
        if step == ITERS - 1:
            doc_ratio = summed_own / doc_degree[:, None, :]
            doc_part = jnp.einsum("tki,tij->kj", doc_ratio, doc_onehot, precision=HIGH)
            term_part = jnp.einsum("tki,tij->kj", raw / root[:, None, :], term_onehot, precision=HIGH)
            sums += [doc_part, term_part, jnp.sum(doc_onehot, axis=(0, 1)), jnp.sum(term_onehot, axis=(0, 1))]
        sums = packed_psum(n_doc, n_term, sums)
        gram_matrix, along, energy, volume = sums[:4]
        lower = jnp.linalg.cholesky(gram_matrix - jnp.outer(along, along) / volume, symmetrize_input=False)
        projected = raw - root[:, None, :] * (along / volume)[None, :, None]
        flat = projected.transpose(1, 0, 2).reshape(width_k, -1)
        solved = jax.scipy.linalg.solve_triangular(lower, flat, lower=True)
        basis = solved.reshape(width_k, term_tiles_own, edge).transpose(1, 0, 2)
        weights = (basis / root[:, None, :]).astype(jnp.bfloat16)

    doc_part, term_part, doc_count, term_count = sums[4:]
    scale = jnp.sqrt(volume)
    column_scale = scale * lax.rsqrt(energy)
    doc_embed = summed_own / doc_degree[:, None, :] * column_scale[None, :, None]
    term_embed = scale * basis / root[:, None, :]
    term_centered = term_part - jnp.outer(along / volume, term_count)
    term_sums = scale * jax.scipy.linalg.solve_triangular(lower, term_centered, lower=True)
    centers = (column_scale[:, None] * doc_part + term_sums) / (doc_count + term_count)[None, :]
    center_norm = jnp.sum(centers * centers, axis=0)

    def distances(embed):
        near = jnp.einsum("tki,kj->tij", embed, centers, precision=HIGH)
        norm = jnp.sum(embed * embed, axis=1)
        dist = (norm[:, :, None] - 2.0 * near + center_norm[None, None, :]) / width_k
        return dist.reshape(-1, CLUSTERS)

    return (distances(doc_embed)[None], distances(term_embed)[None])


def solution(mesh):
    placed = (
        P("doc", "term", None, None, None),
        P("doc", "term", None),
        P("doc", "term", None),
        P("doc", "term"),
        P("term", "doc", None),
        P("doc", "term"),
        P("term", "doc"),
    )
    return jax.shard_map(
        functools.partial(per_device, mesh.shape["doc"], mesh.shape["term"]),
        mesh=mesh,
        in_specs=placed,
        out_specs=(P("doc", "term", None), P("term", "doc", None)),
        check_vma=False,
    )
```
